32 devices in a mesh: phase: 4 (over y, x), rows: 8 (over z, core).
Axes of the slice: x: 2, y: 2, z: 4, core: 2. Of those that a mesh axis runs over, the one named last changes fastest.
Arguments:
- frames: bfloat16 [2, 192, 16, 128], P(None, None, 'rows'), may hold values from -12 to 12, as said below
- causal_cache: bfloat16 [4, 2, 2, 192, 16, 128], P('phase', None, None, None, 'rows'), may hold values from -4 to 4
- conv_weight: bfloat16 [4, 2, 3, 3, 3, 192, 192], P('phase'), may hold values from -0.15625 to 0.15625
- conv_bias: float32 [4, 2, 192], P('phase'), may hold values from -3 to 3
- norm_gain: float32 [4, 2, 192], P('phase'), may hold values from 0.1 to 1.9
- norm_shift: float32 [4, 2, 192], P('phase'), may hold values from -3 to 3
Outputs:
- phase_out: bfloat16 [4, 2, 192, 16, 128], P('phase', None, None, 'rows')
- new_cache: bfloat16 [4, 2, 2, 192, 16, 128], P('phase', None, None, None, 'rows')
The draws below stay inside these ranges and needn't reach their ends.
Inputs may be any that keep to these rules, and one draw needn't show every extreme that they name: `frames`: Real-valued frame features.
All inputs are finite; a program needn't handle non-finite values.
Results may differ from the reference program's by a relative error of at most 0.0066.
Values may be sent and summed in bfloat16 or wider, within the bound.
No kernel may reach another device: no remote copies, remote signals or barrier semaphores. Data moves between devices by JAX's collectives and lax.ppermute only.
A program may use at most 64 MiB of HBM per device.

```python
import math
import jax
import jax.numpy as jnp
from jax import lax

C = 192
GROUPS = 32
W = 128
FRAMES = 2
PHASES = 4
H = 16


def draw_frames(key, part):
    noise_key = jax.random.fold_in(key, 11)
    scale_key = jax.random.fold_in(key, 12)
    offset_key = jax.random.fold_in(key, 13)
    position = jnp.arange(H, dtype=jnp.float32) / (H - 1)
    group_scale = jnp.exp(jax.random.uniform(scale_key, (FRAMES, GROUPS, 1, 1, 1), jnp.float32, math.log(0.4), math.log(2.5)))
    base = jnp.clip(jax.random.normal(noise_key, (FRAMES, C, H, W), jnp.float32), -4.0, 4.0)
    ramp = 1.0 + 2.0 * position
    group_offset = jax.random.uniform(offset_key, (FRAMES, GROUPS, 1, 1, 1), jnp.float32, -1.5, 1.5)
    grouped = base.reshape(FRAMES, GROUPS, C // GROUPS, H, W)
    shaped = ((grouped + group_offset) * group_scale).reshape(FRAMES, C, H, W)
    values = shaped * ramp[None, None, :, None]
    return jnp.clip(values, -12.0, 12.0).astype(jnp.bfloat16)


def level_of(own_key, extent, cuts, least, largest):
    loudness, own = 1.0, jax.random.fold_in(own_key, 6)
    for dim, blocks in cuts:
        steps = jnp.exp(jax.random.uniform(jax.random.fold_in(own, dim), (blocks,), jnp.float32, least / len(cuts), largest / len(cuts)))
        loudness = loudness * jnp.repeat(steps, extent[dim] // blocks).reshape([-1 if axis == dim else 1 for axis in range(len(extent))])
    return loudness


def scatter_about(own_key, dims, deviation, reach, shards=(), kind=jnp.bfloat16):
    gain = level_of(own_key, dims, shards, -0.22, 0.18) if shards else 1.0
    drawn = jax.random.normal(own_key, dims, jnp.float32) * deviation * gain
    return jnp.minimum(jnp.maximum(drawn, -reach), reach).astype(kind)


def setup_inputs(seed: int = 0) -> dict:
    key_list = jax.random.split(jax.random.key(seed), 7)
    frames = draw_frames(jax.random.fold_in(key_list[6], 71), 0)
    causal_cache = scatter_about(key_list[1], (PHASES, 2, 2, C, H, W), 0.7, 4.0, ((0, 4), (4, 8)))
    conv_weight = scatter_about(key_list[2], (PHASES, 2, 3, 3, 3, C, C), (9 * C) ** -0.5, 0.15625, ((0, 4),))
    conv_bias = scatter_about(key_list[3], (PHASES, 2, C), 0.5, 3.0, ((0, 4),), jnp.float32)
    norm_gain = jnp.clip(1.0 + 0.18 * jax.random.normal(key_list[4], (PHASES, 2, C), jnp.float32), 0.1, 1.9)
    norm_shift = scatter_about(key_list[5], (PHASES, 2, C), 0.5, 3.0, ((0, 4),), jnp.float32)
    return dict(frames=frames, causal_cache=causal_cache, conv_weight=conv_weight, conv_bias=conv_bias, norm_gain=norm_gain, norm_shift=norm_shift)


EPS = 1e-06

def activate(source, gain_vec, shift_vec):
    channels, height, columns = source.shape
    grouped = source.astype(jnp.float32).reshape(GROUPS, channels // GROUPS, height, columns)
    average = lax.optimization_barrier(jnp.mean(grouped, axis=(1, 2, 3), keepdims=True))
    spread = lax.optimization_barrier(jnp.mean(jnp.square(grouped - average), axis=(1, 2, 3), keepdims=True))
    normed = ((grouped - average) * lax.rsqrt(spread + EPS)).reshape(channels, height, columns)
    normed = normed * gain_vec[:, None, None] + shift_vec[:, None, None]
    return jax.nn.silu(normed).astype(jnp.bfloat16)

def causal_conv(window, weight, bias_vec):
    channels = window.shape[1]
    height = window.shape[2]
    columns = window.shape[3]
    padded = jnp.pad(window, ((0, 0), (0, 0), (1, 1), (1, 1)))
    running = jnp.zeros((weight.shape[3], height * columns), jnp.float32)
    for step_t in range(3):
        for step_y in range(3):
            for step_x in range(3):
                segment = padded[step_t, :, step_y:step_y + height, step_x:step_x + columns].reshape(channels, height * columns)
                running = running + jnp.dot(weight[step_t, step_y, step_x], segment, preferred_element_type=jnp.float32)
    return running.reshape(-1, height, columns) + bias_vec[:, None, None]

def reference(frames, causal_cache, conv_weight, conv_bias, norm_gain, norm_shift):
    current = frames
    phase_outs = []
    cache_outs = []
    for phase_no in range(PHASES):
        first_hist = causal_cache[phase_no, 0]
        second_hist = causal_cache[phase_no, 1]
        produced = []
        for frame_no in range(FRAMES):
            source = current[frame_no]
            first_in = activate(source, norm_gain[phase_no, 0], norm_shift[phase_no, 0])
            first_win = jnp.concatenate([first_hist, first_in[None]], axis=0)
            hidden = causal_conv(first_win, conv_weight[phase_no, 0], conv_bias[phase_no, 0]).astype(jnp.bfloat16)
            second_in = activate(hidden, norm_gain[phase_no, 1], norm_shift[phase_no, 1])
            second_win = jnp.concatenate([second_hist, second_in[None]], axis=0)
            result = causal_conv(second_win, conv_weight[phase_no, 1], conv_bias[phase_no, 1]) + source.astype(jnp.float32)
            produced.append(result.astype(jnp.bfloat16))
            first_hist = first_win[1:]
            second_hist = second_win[1:]
        current = jnp.stack(produced)
        phase_outs.append(current)
        cache_outs.append(jnp.stack([first_hist, second_hist]))
    return (jnp.stack(phase_outs), jnp.stack(cache_outs))
```

```python
import jax
import jax.numpy as jnp
from jax import lax
from jax.sharding import PartitionSpec as P

GROUPS = 32
EPS = 1e-06
MAX_SPAN = 16


def span_devices(peers, rows_here):
    count = 1
    while count * 2 <= peers and peers % (count * 2) == 0 and count * 2 * rows_here <= MAX_SPAN:
        count *= 2
    return count


def gather_span(array, dim, span_count):
    if span_count == 1:
        return array
    peers = lax.axis_size("rows")
    if span_count == peers:
        return lax.all_gather(array, "rows", axis=dim, tiled=True)
    place = lax.axis_index("rows") % span_count
    pieces = [array]
    for shift in range(1, span_count):
        pairs = [
            (b * span_count + p, b * span_count + (p + shift) % span_count)
            for b in range(peers // span_count)
            for p in range(span_count)
        ]
        pieces.append(lax.ppermute(array, "rows", pairs))
    stacked = jnp.stack(pieces)
    order = (place - jnp.arange(span_count)) % span_count
    picked = jnp.take(stacked, order, axis=0)
    picked = jnp.moveaxis(picked, 0, dim)
    shape = list(array.shape)
    shape[dim] = shape[dim] * span_count
    return picked.reshape(shape)


def with_rim(array, dim, span_count):
    peers = lax.axis_size("rows")
    length = array.shape[dim]
    if span_count == peers:
        pad = [(0, 0)] * array.ndim
        pad[dim] = (1, 1)
        return jnp.pad(array, pad)
    up = [(i, i + span_count) for i in range(peers - span_count)]
    down = [(j, i) for i, j in up]
    last = lax.slice_in_dim(array, length - 1, length, axis=dim)
    leading = lax.slice_in_dim(array, 0, 1, axis=dim)
    before = lax.ppermute(last, "rows", up)
    after = lax.ppermute(leading, "rows", down)
    return jnp.concatenate([before, array, after], axis=dim)


def arrange_taps(weight):
    outputs = weight.shape[3]
    channels = weight.shape[4]
    return jnp.transpose(weight, (2, 3, 0, 1, 4)).reshape(3 * outputs, 9 * channels)


def causal_conv(window, taps, rows_out):
    channels = window.shape[1]
    columns = window.shape[3]
    outputs = taps.shape[0] // 3
    pieces = [
        window[step_t, :, step_y : step_y + rows_out, :]
        for step_t in range(3)
        for step_y in range(3)
    ]
    stacked = jnp.stack(pieces).reshape(9 * channels, rows_out * columns)
    running = jnp.dot(taps, stacked, preferred_element_type=jnp.float32)
    running = running.reshape(3, outputs, rows_out, columns)
    leftward = jnp.pad(running[0, :, :, :-1], ((0, 0), (0, 0), (1, 0)))
    rightward = jnp.pad(running[2, :, :, 1:], ((0, 0), (0, 0), (0, 1)))
    return running[1] + leftward + rightward


def block_sum(values, span_count):
    peers = lax.axis_size("rows")
    if span_count == peers:
        return values
    lead = (lax.axis_index("rows") % span_count == 0).astype(values.dtype)
    return lax.psum(values * lead, "rows")


def activate(source, gain_vec, shift_vec, cell_count, span_count):
    channels, height, columns = source.shape
    grouped = source.astype(jnp.float32).reshape(GROUPS, channels // GROUPS, height, columns)
    average = block_sum(jnp.sum(grouped, axis=(1, 2, 3)), span_count) / cell_count
    centred = grouped - average[:, None, None, None]
    spread = block_sum(jnp.sum(centred * centred, axis=(1, 2, 3)), span_count) / cell_count
    inverse = lax.rsqrt(spread + EPS)
    normed = (centred * inverse[:, None, None, None]).reshape(channels, height, columns)
    normed = normed * gain_vec[:, None, None] + shift_vec[:, None, None]
    return jax.nn.silu(normed).astype(jnp.bfloat16)


def run_frame(source, first_hist, second_hist, kernels, biases, gains, shifts, cell_count, span_count):
    span = source.shape[1]
    first_in = with_rim(activate(source, gains[0], shifts[0], cell_count, span_count), 1, span_count)
    first_win = jnp.concatenate([first_hist, first_in[None]], axis=0)
    hidden = (causal_conv(first_win, kernels[0], span) + biases[0][:, None, None]).astype(jnp.bfloat16)
    second_in = with_rim(activate(hidden, gains[1], shifts[1], cell_count, span_count), 1, span_count)
    second_win = jnp.concatenate([second_hist, second_in[None]], axis=0)
    result = causal_conv(second_win, kernels[1], span) + biases[1][:, None, None] + source.astype(jnp.float32)
    return (result.astype(jnp.bfloat16), first_win[1:], second_win[1:])


def shards(frames, causal_cache, conv_weight, conv_bias, norm_gain, norm_shift):
    phase_no = lax.axis_index("phase")
    phase_count = lax.axis_size("phase")
    peers = lax.axis_size("rows")
    frame_count = frames.shape[0]
    channels = frames.shape[1]
    rows_here = frames.shape[2]
    columns = frames.shape[3]
    span_count = span_devices(peers, rows_here)
    span = rows_here * span_count
    cell_count = float(channels // GROUPS * rows_here * peers * columns)
    frames_span = gather_span(frames, 2, span_count)
    cache_span = gather_span(causal_cache[0], 3, span_count)
    rimmed = with_rim(cache_span, 3, span_count)
    first_hist = rimmed[0]
    second_hist = rimmed[1]
    local_taps = (arrange_taps(conv_weight[0, 0]), arrange_taps(conv_weight[0, 1]))
    incoming = jnp.zeros_like(frames_span[0])
    produced = jnp.zeros_like(frames_span)
    tick_count = frame_count + phase_count - 1
    for tick_no in range(tick_count):
        frame_no = tick_no - phase_no
        active_now = jnp.logical_and(frame_no >= 0, frame_no < frame_count)
        source = jnp.where(phase_no == 0, frames_span[min(tick_no, frame_count - 1)], incoming)
        result, first_next, second_next = run_frame(
            source, first_hist, second_hist, local_taps, conv_bias[0], norm_gain[0], norm_shift[0],
            cell_count, span_count,
        )
        first_hist = jnp.where(active_now, first_next, first_hist)
        second_hist = jnp.where(active_now, second_next, second_hist)
        frame_slot = jnp.clip(frame_no, 0, frame_count - 1)
        produced = jnp.where(
            active_now, lax.dynamic_update_index_in_dim(produced, result, frame_slot, 0), produced
        )
        if tick_no + 1 < tick_count:
            incoming = lax.ppermute(result, "phase", [(s, s + 1) for s in range(phase_count - 1)])
    start = (lax.axis_index("rows") % span_count) * rows_here
    new_cache = jnp.stack([first_hist[:, :, 1 : 1 + span, :], second_hist[:, :, 1 : 1 + span, :]])
    produced = lax.dynamic_slice_in_dim(produced, start, rows_here, axis=2)
    new_cache = lax.dynamic_slice_in_dim(new_cache, start, rows_here, axis=3)
    return (produced[None], new_cache[None])


def solution(mesh):
    in_specs = (
        P(None, None, "rows", None),
        P("phase", None, None, None, "rows", None),
        P("phase", None, None, None, None, None, None),
        P("phase", None, None),
        P("phase", None, None),
        P("phase", None, None),
    )
    out_specs = (P("phase", None, None, "rows", None), P("phase", None, None, None, "rows", None))
    return jax.shard_map(shards, mesh=mesh, in_specs=in_specs, out_specs=out_specs, check_vma=False)
```

```python
import jax
import jax.numpy as jnp
from jax import lax
from jax.sharding import PartitionSpec as P
from jax.experimental import pallas as pl
from jax.experimental.pallas import tpu as pltpu
import functools

GROUPS = 32
EPS = 1e-06
MAX_SPAN = 16


def span_devices(peers, rows_here):
    count = 1
    while count * 2 <= peers and peers % (count * 2) == 0 and count * 2 * rows_here <= MAX_SPAN:
        count *= 2
    return count


def gather_span(array, dim, span_count):
    if span_count == 1:
        return array
    peers = lax.axis_size("rows")
    if span_count == peers:
        return lax.all_gather(array, "rows", axis=dim, tiled=True)
    place = lax.axis_index("rows") % span_count
    pieces = [array]
    for shift in range(1, span_count):
        pairs = [
            (b * span_count + p, b * span_count + (p + shift) % span_count)
            for b in range(peers // span_count)
            for p in range(span_count)
        ]
        pieces.append(lax.ppermute(array, "rows", pairs))
    stacked = jnp.stack(pieces)
    order = (place - jnp.arange(span_count)) % span_count
    picked = jnp.take(stacked, order, axis=0)
    picked = jnp.moveaxis(picked, 0, dim)
    shape = list(array.shape)
    shape[dim] = shape[dim] * span_count
    return picked.reshape(shape)


def with_rim(array, dim, span_count):
    peers = lax.axis_size("rows")
    length = array.shape[dim]
    if span_count == peers:
        pad = [(0, 0)] * array.ndim
        pad[dim] = (1, 1)
        return jnp.pad(array, pad)
    up = [(i, i + span_count) for i in range(peers - span_count)]
    down = [(j, i) for i, j in up]
    last = lax.slice_in_dim(array, length - 1, length, axis=dim)
    leading = lax.slice_in_dim(array, 0, 1, axis=dim)
    before = lax.ppermute(last, "rows", up)
    after = lax.ppermute(leading, "rows", down)
    return jnp.concatenate([before, array, after], axis=dim)


def arrange_taps(weight):
    outputs = weight.shape[3]
    channels = weight.shape[4]
    return jnp.transpose(weight, (2, 3, 0, 1, 4)).reshape(3 * outputs, 9 * channels)


def conv_body(x0, x1, x2, taps, bias, *rest, rows_out, pair, with_res):
    if with_res:
        res, out = rest
    else:
        (out,) = rest
    outputs = out.shape[1]
    columns = out.shape[2]
    lanes = pair * columns
    lane = lax.broadcasted_iota(jnp.int32, (outputs, lanes), 1) % columns

    def step(i, carry):
        r = i * pair
        cols = []
        for k in range(pair):
            parts = [x0[pl.ds(r + k, 3)], x1[pl.ds(r + k, 3)], x2[pl.ds(r + k, 3)]]
            cols.append(jnp.concatenate(parts, axis=0).reshape(9 * x0.shape[1], columns))
        rhs = cols[0] if pair == 1 else jnp.concatenate(cols, axis=1)
        acc = jnp.dot(taps[...], rhs, preferred_element_type=jnp.float32)
        left = pltpu.roll(acc[:outputs], 1, 1)
        right = pltpu.roll(acc[2 * outputs :], lanes - 1, 1)
        total = acc[outputs : 2 * outputs] + jnp.where(lane == 0, 0.0, left)
        total = total + jnp.where(lane == columns - 1, 0.0, right) + bias[...]
        for k in range(pair):
            piece = total[:, k * columns : (k + 1) * columns]
            if with_res:
                piece = piece + res[r + k].astype(jnp.float32)
            out[r + k] = piece.astype(out.dtype)
        return carry

    lax.fori_loop(0, rows_out // pair, step, 0)


def causal_conv(x0, x1, x2, taps, bias_vec, res=None):
    rows_out = x0.shape[0] - 2
    outputs = taps.shape[0] // 3
    pair = 4 if rows_out % 4 == 0 else (2 if rows_out % 2 == 0 else 1)
    args = [x0, x1, x2, taps, bias_vec.reshape(outputs, 1)]
    if res is not None:
        args.append(res)
    body = functools.partial(conv_body, rows_out=rows_out, pair=pair, with_res=res is not None)
    shape = jax.ShapeDtypeStruct((rows_out, outputs, x0.shape[2]), jnp.bfloat16)
    return pl.pallas_call(body, out_shape=shape)(*args)


def block_sum(values, span_count):
    peers = lax.axis_size("rows")
    if span_count == peers:
        return values
    lead = (lax.axis_index("rows") % span_count == 0).astype(values.dtype)
    return lax.psum(values * lead, "rows")


def activate(source, gain_vec, shift_vec, cell_count, span_count):
    height, channels, columns = source.shape
    grouped = source.astype(jnp.float32).reshape(height, GROUPS, channels // GROUPS, columns)
    average = block_sum(jnp.sum(grouped, axis=(0, 2, 3)), span_count) / cell_count
    centred = grouped - average[None, :, None, None]
    spread = block_sum(jnp.sum(centred * centred, axis=(0, 2, 3)), span_count) / cell_count
    inverse = lax.rsqrt(spread + EPS)
    normed = (centred * inverse[None, :, None, None]).reshape(height, channels, columns)
    normed = normed * gain_vec[None, :, None] + shift_vec[None, :, None]
    return jax.nn.silu(normed).astype(jnp.bfloat16)


def run_frame(source, first_hist, second_hist, kernels, biases, gains, shifts, cell_count, span_count):
    first_in = with_rim(activate(source, gains[0], shifts[0], cell_count, span_count), 0, span_count)
    hidden = causal_conv(first_hist[0], first_hist[1], first_in, kernels[0], biases[0])
    second_in = with_rim(activate(hidden, gains[1], shifts[1], cell_count, span_count), 0, span_count)
    result = causal_conv(second_hist[0], second_hist[1], second_in, kernels[1], biases[1], source)
    first_next = jnp.stack([first_hist[1], first_in])
    second_next = jnp.stack([second_hist[1], second_in])
    return (result, first_next, second_next)


def shards(frames, causal_cache, conv_weight, conv_bias, norm_gain, norm_shift):
    phase_no = lax.axis_index("phase")
    phase_count = lax.axis_size("phase")
    peers = lax.axis_size("rows")
    frame_count = frames.shape[0]
    channels = frames.shape[1]
    rows_here = frames.shape[2]
    columns = frames.shape[3]
    span_count = span_devices(peers, rows_here)
    span = rows_here * span_count
    cell_count = float(channels // GROUPS * rows_here * peers * columns)
    frames_span = gather_span(jnp.transpose(frames, (0, 2, 1, 3)), 1, span_count)
    cache_span = gather_span(jnp.transpose(causal_cache[0], (0, 1, 3, 2, 4)), 2, span_count)
    rimmed = with_rim(cache_span, 2, span_count)
    first_hist = rimmed[0]
    second_hist = rimmed[1]
    local_taps = (arrange_taps(conv_weight[0, 0]), arrange_taps(conv_weight[0, 1]))
    incoming = jnp.zeros_like(frames_span[0])
    produced = jnp.zeros_like(frames_span)
    tick_count = frame_count + phase_count - 1
    for tick_no in range(tick_count):
        frame_no = tick_no - phase_no
        active_now = jnp.logical_and(frame_no >= 0, frame_no < frame_count)
        source = jnp.where(phase_no == 0, frames_span[min(tick_no, frame_count - 1)], incoming)
        result, first_next, second_next = run_frame(
            source, first_hist, second_hist, local_taps, conv_bias[0], norm_gain[0], norm_shift[0],
            cell_count, span_count,
        )
        first_hist = jnp.where(active_now, first_next, first_hist)
        second_hist = jnp.where(active_now, second_next, second_hist)
        frame_slot = jnp.clip(frame_no, 0, frame_count - 1)
        produced = jnp.where(
            active_now, lax.dynamic_update_index_in_dim(produced, result, frame_slot, 0), produced
        )
        if tick_no + 1 < tick_count:
            incoming = lax.ppermute(result, "phase", [(s, s + 1) for s in range(phase_count - 1)])
    start = (lax.axis_index("rows") % span_count) * rows_here
    new_cache = jnp.stack([first_hist, second_hist])
    produced = lax.dynamic_slice_in_dim(produced, start, rows_here, axis=1)
    new_cache = lax.dynamic_slice_in_dim(new_cache, start + 1, rows_here, axis=2)
    produced = jnp.transpose(produced, (0, 2, 1, 3))
    new_cache = jnp.transpose(new_cache, (0, 1, 3, 2, 4))
    return (produced[None], new_cache[None])


def solution(mesh):
    in_specs = (
        P(None, None, "rows", None),
        P("phase", None, None, None, "rows", None),
        P("phase", None, None, None, None, None, None),
        P("phase", None, None),
        P("phase", None, None),
        P("phase", None, None),
    )
    out_specs = (P("phase", None, None, "rows", None), P("phase", None, None, None, "rows", None))
    return jax.shard_map(shards, mesh=mesh, in_specs=in_specs, out_specs=out_specs, check_vma=False)
```

```python
import jax
import jax.numpy as jnp
from jax import lax
from jax.sharding import PartitionSpec as P
from jax.experimental import pallas as pl
from jax.experimental.pallas import tpu as pltpu
import functools

GROUPS = 32
EPS = 1e-06
MAX_SPAN = 16


def span_devices(peers, rows_here):
    count = 1
    while count * 2 <= peers and peers % (count * 2) == 0 and count * 2 * rows_here <= MAX_SPAN:
        count *= 2
    return count


def gather_span(array, dim, span_count):
    if span_count == 1:
        return array
    peers = lax.axis_size("rows")
    if span_count == peers:
        return lax.all_gather(array, "rows", axis=dim, tiled=True)
    place = lax.axis_index("rows") % span_count
    pieces = [array]
    for shift in range(1, span_count):
        pairs = [
            (b * span_count + p, b * span_count + (p + shift) % span_count)
            for b in range(peers // span_count)
            for p in range(span_count)
        ]
        pieces.append(lax.ppermute(array, "rows", pairs))
    stacked = jnp.stack(pieces)
    order = (place - jnp.arange(span_count)) % span_count
    picked = jnp.take(stacked, order, axis=0)
    picked = jnp.moveaxis(picked, 0, dim)
    shape = list(array.shape)
    shape[dim] = shape[dim] * span_count
    return picked.reshape(shape)


def with_rim(array, dim, span_count):
    peers = lax.axis_size("rows")
    length = array.shape[dim]
    if span_count == peers:
        return array
    up = [(i, i + span_count) for i in range(peers - span_count)]
    down = [(j, i) for i, j in up]
    last = lax.slice_in_dim(array, length - 1, length, axis=dim)
    leading = lax.slice_in_dim(array, 0, 1, axis=dim)
    before = lax.ppermute(last, "rows", up)
    after = lax.ppermute(leading, "rows", down)
    return jnp.concatenate([before, array, after], axis=dim)


def pass_on(result, span_count):
    phase_count = lax.axis_size("phase")
    forward = [(s, s + 1) for s in range(phase_count - 1)]
    length = result.shape[0]
    if span_count % 2 or length % 2:
        return lax.ppermute(result, "phase", forward)
    peers = lax.axis_size("rows")
    half = length // 2
    core = lax.axis_index("rows") % 2
    mine = lax.dynamic_slice_in_dim(result, core * half, half, axis=0)
    got = lax.ppermute(mine, "phase", forward)
    other = lax.ppermute(got, "rows", [(i, i ^ 1) for i in range(peers)])
    return jnp.where(core == 0, jnp.concatenate([got, other]), jnp.concatenate([other, got]))


def arrange_taps(weight):
    outputs = weight.shape[3]
    channels = weight.shape[4]
    return jnp.transpose(weight, (2, 3, 0, 1, 4)).reshape(3 * outputs, 9 * channels)


def conv_body(x0, x1, x2, taps, bias, *rest, rows_out, pair, with_res, padded):
    if with_res:
        res, out = rest
    else:
        (out,) = rest
    outputs = out.shape[1]
    channels = x0.shape[1]
    columns = out.shape[2]
    lanes = pair * columns
    lane = lax.broadcasted_iota(jnp.int32, (outputs, lanes), 1) % columns
    frames = (x0, x1, x2)

    def column(r):
        if padded or 0 < r < rows_out - 1:
            base = r if padded else r - 1
            parts = [x[pl.ds(base, 3)] for x in frames]
            return jnp.concatenate(parts, axis=0).reshape(9 * channels, columns)
        zero = jnp.zeros((1, channels, columns), x0.dtype)
        parts = []
        for x in frames:
            for dy in range(3):
                q = r + dy - 1
                parts.append(zero if q < 0 or q >= rows_out else x[pl.ds(q, 1)])
        return jnp.concatenate(parts, axis=0).reshape(9 * channels, columns)

    for r in range(0, rows_out, pair):
        cols = [column(r + k) for k in range(pair)]
        rhs = cols[0] if pair == 1 else jnp.concatenate(cols, axis=1)
        acc = jnp.dot(taps[...], rhs, preferred_element_type=jnp.float32)
        left = pltpu.roll(acc[:outputs], 1, 1)
        right = pltpu.roll(acc[2 * outputs :], lanes - 1, 1)
        total = acc[outputs : 2 * outputs] + jnp.where(lane == 0, 0.0, left)
        total = total + jnp.where(lane == columns - 1, 0.0, right) + bias[...]
        for k in range(pair):
            piece = total[:, k * columns : (k + 1) * columns]
            if with_res:
                piece = piece + res[r + k].astype(jnp.float32)
            out[r + k] = piece.astype(out.dtype)


def causal_conv(x0, x1, x2, taps, bias_vec, res, padded):
    rows_out = x0.shape[0] - 2 if padded else x0.shape[0]
    outputs = taps.shape[0] // 3
    pair = 4 if rows_out % 4 == 0 else (2 if rows_out % 2 == 0 else 1)
    args = [x0, x1, x2, taps, bias_vec.reshape(outputs, 1)]
    if res is not None:
        args.append(res)
    body = functools.partial(
        conv_body, rows_out=rows_out, pair=pair, with_res=res is not None, padded=padded
    )
    shape = jax.ShapeDtypeStruct((rows_out, outputs, x0.shape[2]), jnp.bfloat16)
    return pl.pallas_call(body, out_shape=shape)(*args)


def block_sum(values, span_count):
    peers = lax.axis_size("rows")
    if span_count == peers:
        return values
    lead = (lax.axis_index("rows") % span_count == 0).astype(values.dtype)
    return lax.psum(values * lead, "rows")


def activate(source, gain_vec, shift_vec, cell_count, span_count):
    height, channels, columns = source.shape
    grouped = source.astype(jnp.float32).reshape(height, GROUPS, channels // GROUPS, columns)
    average = block_sum(jnp.sum(grouped, axis=(0, 2, 3)), span_count) / cell_count
    centred = grouped - average[None, :, None, None]
    spread = block_sum(jnp.sum(centred * centred, axis=(0, 2, 3)), span_count) / cell_count
    inverse = lax.rsqrt(spread + EPS)
    normed = (centred * inverse[None, :, None, None]).reshape(height, channels, columns)
    normed = normed * gain_vec[None, :, None] + shift_vec[None, :, None]
    return jax.nn.silu(normed).astype(jnp.bfloat16)


def run_frame(source, first_hist, second_hist, kernels, biases, gains, shifts, cell_count, span_count):
    padded = span_count != lax.axis_size("rows")
    first_in = with_rim(activate(source, gains[0], shifts[0], cell_count, span_count), 0, span_count)
    hidden = causal_conv(first_hist[0], first_hist[1], first_in, kernels[0], biases[0], None, padded)
    second_in = with_rim(activate(hidden, gains[1], shifts[1], cell_count, span_count), 0, span_count)
    result = causal_conv(second_hist[0], second_hist[1], second_in, kernels[1], biases[1], source, padded)
    return (result, (first_hist[1], first_in), (second_hist[1], second_in))


def shards(frames, causal_cache, conv_weight, conv_bias, norm_gain, norm_shift):
    phase_no = lax.axis_index("phase")
    phase_count = lax.axis_size("phase")
    peers = lax.axis_size("rows")
    frame_count = frames.shape[0]
    channels = frames.shape[1]
    rows_here = frames.shape[2]
    columns = frames.shape[3]
    span_count = span_devices(peers, rows_here)
    span = rows_here * span_count
    cell_count = float(channels // GROUPS * rows_here * peers * columns)
    padded = span_count != peers
    frames_t = jnp.transpose(frames, (0, 2, 1, 3))
    cache_t = jnp.transpose(causal_cache[0], (0, 1, 3, 2, 4))
    frames_span = [gather_span(frames_t[0], 0, span_count)]
    first_hist = tuple(with_rim(gather_span(cache_t[0, k], 0, span_count), 0, span_count) for k in range(2))
    second_hist = tuple(with_rim(gather_span(cache_t[1, k], 0, span_count), 0, span_count) for k in range(2))
    frames_span += [gather_span(frames_t[f], 0, span_count) for f in range(1, frame_count)]
    local_taps = (arrange_taps(conv_weight[0, 0]), arrange_taps(conv_weight[0, 1]))
    incoming = jnp.zeros_like(frames_span[0])
    produced = [jnp.zeros_like(frames_span[0]) for _ in range(frame_count)]
    tick_count = frame_count + phase_count - 1
    for tick_no in range(tick_count):
        frame_no = tick_no - phase_no
        active_now = jnp.logical_and(frame_no >= 0, frame_no < frame_count)
        source = jnp.where(phase_no == 0, frames_span[min(tick_no, frame_count - 1)], incoming)
        result, first_next, second_next = run_frame(
            source, first_hist, second_hist, local_taps, conv_bias[0], norm_gain[0], norm_shift[0],
            cell_count, span_count,
        )
        first_hist = tuple(jnp.where(active_now, a, b) for a, b in zip(first_next, first_hist))
        second_hist = tuple(jnp.where(active_now, a, b) for a, b in zip(second_next, second_hist))
        for f in range(frame_count):
            if 0 <= tick_no - f < phase_count:
                produced[f] = jnp.where(frame_no == f, result, produced[f])
        if tick_no + 1 < tick_count:
            incoming = pass_on(result, span_count)
    start = (lax.axis_index("rows") % span_count) * rows_here
    rim = 1 if padded else 0
    produced = jnp.stack([lax.dynamic_slice_in_dim(p, start, rows_here, axis=0) for p in produced])
    new_cache = jnp.stack(
        [
            jnp.stack([lax.dynamic_slice_in_dim(h, start + rim, rows_here, axis=0) for h in hist])
            for hist in (first_hist, second_hist)
        ]
    )
    produced = jnp.transpose(produced, (0, 2, 1, 3))
    new_cache = jnp.transpose(new_cache, (0, 1, 3, 2, 4))
    return (produced[None], new_cache[None])


def solution(mesh):
    in_specs = (
        P(None, None, "rows", None),
        P("phase", None, None, None, "rows", None),
        P("phase", None, None, None, None, None, None),
        P("phase", None, None),
        P("phase", None, None),
        P("phase", None, None),
    )
    out_specs = (P("phase", None, None, "rows", None), P("phase", None, None, None, "rows", None))
    return jax.shard_map(shards, mesh=mesh, in_specs=in_specs, out_specs=out_specs, check_vma=False)
```

```python
import jax
import jax.numpy as jnp
from jax import lax
from jax.sharding import PartitionSpec as P
from jax.experimental import pallas as pl
from jax.experimental.pallas import tpu as pltpu
import functools

GROUPS = 32
EPS = 1e-06
MAX_SPAN = 16


def span_devices(peers, rows_here):
    count = 1
    while count * 2 <= peers and peers % (count * 2) == 0 and count * 2 * rows_here <= MAX_SPAN:
        count *= 2
    return count


def gather_span(array, dim, span_count):
    if span_count == 1:
        return array
    peers = lax.axis_size("rows")
    if span_count == peers:
        return lax.all_gather(array, "rows", axis=dim, tiled=True)
    place = lax.axis_index("rows") % span_count
    pieces = [array]
    for shift in range(1, span_count):
        pairs = [
            (b * span_count + p, b * span_count + (p + shift) % span_count)
            for b in range(peers // span_count)
            for p in range(span_count)
        ]
        pieces.append(lax.ppermute(array, "rows", pairs))
    stacked = jnp.stack(pieces)
    order = (place - jnp.arange(span_count)) % span_count
    picked = jnp.take(stacked, order, axis=0)
    picked = jnp.moveaxis(picked, 0, dim)
    shape = list(array.shape)
    shape[dim] = shape[dim] * span_count
    return picked.reshape(shape)


def with_rim(array, dim, span_count):
    peers = lax.axis_size("rows")
    length = array.shape[dim]
    if span_count == peers:
        return array
    up = [(i, i + span_count) for i in range(peers - span_count)]
    down = [(j, i) for i, j in up]
    last = lax.slice_in_dim(array, length - 1, length, axis=dim)
    leading = lax.slice_in_dim(array, 0, 1, axis=dim)
    before = lax.ppermute(last, "rows", up)
    after = lax.ppermute(leading, "rows", down)
    return jnp.concatenate([before, array, after], axis=dim)


def pass_on(result, span_count):
    phase_count = lax.axis_size("phase")
    forward = [(s, s + 1) for s in range(phase_count - 1)]
    length = result.shape[0]
    if span_count % 2 or length % 2:
        return lax.ppermute(result, "phase", forward)
    peers = lax.axis_size("rows")
    half = length // 2
    core = lax.axis_index("rows") % 2
    mine = lax.dynamic_slice_in_dim(result, core * half, half, axis=0)
    got = lax.ppermute(mine, "phase", forward)
    other = lax.ppermute(got, "rows", [(i, i ^ 1) for i in range(peers)])
    return jnp.where(core == 0, jnp.concatenate([got, other]), jnp.concatenate([other, got]))


def arrange_taps(weight):
    outputs = weight.shape[3]
    channels = weight.shape[4]
    return jnp.transpose(weight, (2, 3, 0, 1, 4)).reshape(3 * outputs, 9 * channels)


def conv_body(x0, x1, x2, taps, bias, *rest, rows_out, pair, with_res, padded):
    if with_res:
        res, out = rest
    else:
        (out,) = rest
    outputs = out.shape[1]
    channels = x0.shape[1]
    columns = out.shape[2]
    lanes = pair * columns
    lane = lax.broadcasted_iota(jnp.int32, (outputs, lanes), 1) % columns
    frames = (x0, x1, x2)

    def column(r):
        if padded or 0 < r < rows_out - 1:
            base = r if padded else r - 1
            parts = [x[pl.ds(base, 3)] for x in frames]
            return jnp.concatenate(parts, axis=0).reshape(9 * channels, columns)
        zero = jnp.zeros((1, channels, columns), x0.dtype)
        parts = []
        for x in frames:
            for dy in range(3):
                q = r + dy - 1
                parts.append(zero if q < 0 or q >= rows_out else x[pl.ds(q, 1)])
        return jnp.concatenate(parts, axis=0).reshape(9 * channels, columns)

    for r in range(0, rows_out, pair):
        cols = [column(r + k) for k in range(pair)]
        rhs = cols[0] if pair == 1 else jnp.concatenate(cols, axis=1)
        acc = jnp.dot(taps[...], rhs, preferred_element_type=jnp.float32)
        left = pltpu.roll(acc[:outputs], 1, 1)
        right = pltpu.roll(acc[2 * outputs :], lanes - 1, 1)
        total = acc[outputs : 2 * outputs] + jnp.where(lane == 0, 0.0, left)
        total = total + jnp.where(lane == columns - 1, 0.0, right) + bias[...]
        for k in range(pair):
            piece = total[:, k * columns : (k + 1) * columns]
            if with_res:
                piece = piece + res[r + k].astype(jnp.float32)
            out[r + k] = piece.astype(out.dtype)


def causal_conv(x0, x1, x2, taps, bias_vec, res, padded):
    rows_out = x0.shape[0] - 2 if padded else x0.shape[0]
    outputs = taps.shape[0] // 3
    pair = 4 if rows_out % 4 == 0 else (2 if rows_out % 2 == 0 else 1)
    args = [x0, x1, x2, taps, bias_vec.reshape(outputs, 1)]
    if res is not None:
        args.append(res)
    body = functools.partial(
        conv_body, rows_out=rows_out, pair=pair, with_res=res is not None, padded=padded
    )
    shape = jax.ShapeDtypeStruct((rows_out, outputs, x0.shape[2]), jnp.bfloat16)
    return pl.pallas_call(body, out_shape=shape)(*args)


def block_sum(values, span_count):
    peers = lax.axis_size("rows")
    if span_count == peers:
        return values
    lead = (lax.axis_index("rows") % span_count == 0).astype(values.dtype)
    return lax.psum(values * lead, "rows")


def activate(source, gain_vec, shift_vec, cell_count, span_count):
    height, channels, columns = source.shape
    grouped = source.astype(jnp.float32).reshape(height, GROUPS, channels // GROUPS, columns)
    average = block_sum(jnp.sum(grouped, axis=(0, 2, 3)), span_count) / cell_count
    centred = grouped - average[None, :, None, None]
    spread = block_sum(jnp.sum(centred * centred, axis=(0, 2, 3)), span_count) / cell_count
    inverse = lax.rsqrt(spread + EPS)
    normed = (centred * inverse[None, :, None, None]).reshape(height, channels, columns)
    normed = normed * gain_vec[None, :, None] + shift_vec[None, :, None]
    return jax.nn.silu(normed).astype(jnp.bfloat16)


def run_frame(source, first_hist, second_hist, kernels, biases, gains, shifts, cell_count, span_count):
    padded = span_count != lax.axis_size("rows")
    first_in = with_rim(activate(source, gains[0], shifts[0], cell_count, span_count), 0, span_count)
    hidden = causal_conv(first_hist[0], first_hist[1], first_in, kernels[0], biases[0], None, padded)
    second_in = with_rim(activate(hidden, gains[1], shifts[1], cell_count, span_count), 0, span_count)
    result = causal_conv(second_hist[0], second_hist[1], second_in, kernels[1], biases[1], source, padded)
    return (result, (first_hist[1], first_in), (second_hist[1], second_in))


def shards(frames, causal_cache, conv_weight, conv_bias, norm_gain, norm_shift):
    phase_no = lax.axis_index("phase")
    phase_count = lax.axis_size("phase")
    peers = lax.axis_size("rows")
    frame_count = frames.shape[0]
    channels = frames.shape[1]
    rows_here = frames.shape[2]
    columns = frames.shape[3]
    span_count = span_devices(peers, rows_here)
    span = rows_here * span_count
    cell_count = float(channels // GROUPS * rows_here * peers * columns)
    padded = span_count != peers
    frames_t = jnp.transpose(frames, (0, 2, 1, 3))
    cache_t = jnp.transpose(causal_cache[0], (0, 1, 3, 2, 4))
    early = gather_span(jnp.stack([frames_t[0], cache_t[0, 0], cache_t[0, 1]]), 1, span_count)
    late = gather_span(jnp.stack([cache_t[1, 0], cache_t[1, 1]] + list(frames_t[1:])), 1, span_count)
    frames_span = [early[0]] + [late[2 + f] for f in range(frame_count - 1)]
    first_hist = tuple(with_rim(early[1 + k], 0, span_count) for k in range(2))
    second_hist = tuple(with_rim(late[k], 0, span_count) for k in range(2))
    local_taps = (arrange_taps(conv_weight[0, 0]), arrange_taps(conv_weight[0, 1]))
    incoming = jnp.zeros_like(frames_span[0])
    produced = [jnp.zeros_like(frames_span[0]) for _ in range(frame_count)]
    tick_count = frame_count + phase_count - 1
    for tick_no in range(tick_count):
        frame_no = tick_no - phase_no
        active_now = jnp.logical_and(frame_no >= 0, frame_no < frame_count)
        source = jnp.where(phase_no == 0, frames_span[min(tick_no, frame_count - 1)], incoming)
        result, first_next, second_next = run_frame(
            source, first_hist, second_hist, local_taps, conv_bias[0], norm_gain[0], norm_shift[0],
            cell_count, span_count,
        )
        first_hist = tuple(jnp.where(active_now, a, b) for a, b in zip(first_next, first_hist))
        second_hist = tuple(jnp.where(active_now, a, b) for a, b in zip(second_next, second_hist))
        for f in range(frame_count):
            if 0 <= tick_no - f < phase_count:
                produced[f] = jnp.where(frame_no == f, result, produced[f])
        if tick_no + 1 < tick_count:
            incoming = pass_on(result, span_count)
    start = (lax.axis_index("rows") % span_count) * rows_here
    rim = 1 if padded else 0
    produced = jnp.stack([lax.dynamic_slice_in_dim(p, start, rows_here, axis=0) for p in produced])
    new_cache = jnp.stack(
        [
            jnp.stack([lax.dynamic_slice_in_dim(h, start + rim, rows_here, axis=0) for h in hist])
            for hist in (first_hist, second_hist)
        ]
    )
    produced = jnp.transpose(produced, (0, 2, 1, 3))
    new_cache = jnp.transpose(new_cache, (0, 1, 3, 2, 4))
    return (produced[None], new_cache[None])


def solution(mesh):
    in_specs = (
        P(None, None, "rows", None),
        P("phase", None, None, None, "rows", None),
        P("phase", None, None, None, None, None, None),
        P("phase", None, None),
        P("phase", None, None),
        P("phase", None, None),
    )
    out_specs = (P("phase", None, None, "rows", None), P("phase", None, None, None, "rows", None))
    return jax.shard_map(shards, mesh=mesh, in_specs=in_specs, out_specs=out_specs, check_vma=False)
```

```python
import jax
import jax.numpy as jnp
from jax import lax
from jax.sharding import PartitionSpec as P
from jax.experimental import pallas as pl
from jax.experimental.pallas import tpu as pltpu
import functools

GROUPS = 32
EPS = 1e-06
MAX_SPAN = 16


def span_devices(peers, rows_here):
    count = 1
    while count * 2 <= peers and peers % (count * 2) == 0 and count * 2 * rows_here <= MAX_SPAN:
        count *= 2
    return count


def gather_span(array, dim, span_count):
    if span_count == 1:
        return array
    peers = lax.axis_size("rows")
    if span_count == peers:
        return lax.all_gather(array, "rows", axis=dim, tiled=True)
    place = lax.axis_index("rows") % span_count
    pieces = [array]
    for shift in range(1, span_count):
        pairs = [
            (b * span_count + p, b * span_count + (p + shift) % span_count)
            for b in range(peers // span_count)
            for p in range(span_count)
        ]
        pieces.append(lax.ppermute(array, "rows", pairs))
    stacked = jnp.stack(pieces)
    order = (place - jnp.arange(span_count)) % span_count
    picked = jnp.take(stacked, order, axis=0)
    picked = jnp.moveaxis(picked, 0, dim)
    shape = list(array.shape)
    shape[dim] = shape[dim] * span_count
    return picked.reshape(shape)


def with_rim(array, dim, span_count):
    peers = lax.axis_size("rows")
    length = array.shape[dim]
    if span_count == peers:
        return array
    up = [(i, i + span_count) for i in range(peers - span_count)]
    down = [(j, i) for i, j in up]
    last = lax.slice_in_dim(array, length - 1, length, axis=dim)
    leading = lax.slice_in_dim(array, 0, 1, axis=dim)
    before = lax.ppermute(last, "rows", up)
    after = lax.ppermute(leading, "rows", down)
    return jnp.concatenate([before, array, after], axis=dim)


def pass_on(result, span_count):
    phase_count = lax.axis_size("phase")
    forward = [(s, s + 1) for s in range(phase_count - 1)]
    length = result.shape[0]
    if span_count % 2 or length % 2:
        return lax.ppermute(result, "phase", forward)
    peers = lax.axis_size("rows")
    half = length // 2
    core = lax.axis_index("rows") % 2
    mine = lax.dynamic_slice_in_dim(result, core * half, half, axis=0)
    got = lax.ppermute(mine, "phase", forward)
    other = lax.ppermute(got, "rows", [(i, i ^ 1) for i in range(peers)])
    return jnp.where(core == 0, jnp.concatenate([got, other]), jnp.concatenate([other, got]))


def arrange_taps(weight):
    outputs = weight.shape[3]
    channels = weight.shape[4]
    return jnp.transpose(weight, (2, 3, 0, 1, 4)).reshape(3 * outputs, 9 * channels)


def conv_body(x0, x1, x2, taps, bias, *rest, rows_out, pair, with_res, padded, fused):
    rest = list(rest)
    if fused:
        average, inverse, gain, shift = rest[:4]
        rest = rest[4:]
    res = rest.pop(0) if with_res else None
    out = rest[0]
    if fused:
        raw = x2
        x2 = rest[1]
        for r in range(rows_out):
            value = (raw[r].astype(jnp.float32) - average[...]) * inverse[...]
            value = value * gain[...] + shift[...]
            x2[r] = (value / (1.0 + jnp.exp(-value))).astype(x2.dtype)
    outputs = out.shape[1]
    channels = x0.shape[1]
    columns = out.shape[2]
    lanes = pair * columns
    lane = lax.broadcasted_iota(jnp.int32, (outputs, lanes), 1) % columns
    frames = (x0, x1, x2)

    def column(r):
        if padded or 0 < r < rows_out - 1:
            base = r if padded else r - 1
            parts = [x[pl.ds(base, 3)] for x in frames]
            return jnp.concatenate(parts, axis=0).reshape(9 * channels, columns)
        zero = jnp.zeros((1, channels, columns), x0.dtype)
        parts = []
        for x in frames:
            for dy in range(3):
                q = r + dy - 1
                parts.append(zero if q < 0 or q >= rows_out else x[pl.ds(q, 1)])
        return jnp.concatenate(parts, axis=0).reshape(9 * channels, columns)

    for r in range(0, rows_out, pair):
        cols = [column(r + k) for k in range(pair)]
        rhs = cols[0] if pair == 1 else jnp.concatenate(cols, axis=1)
        acc = jnp.dot(taps[...], rhs, preferred_element_type=jnp.float32)
        left = pltpu.roll(acc[:outputs], 1, 1)
        right = pltpu.roll(acc[2 * outputs :], lanes - 1, 1)
        total = acc[outputs : 2 * outputs] + jnp.where(lane == 0, 0.0, left)
        total = total + jnp.where(lane == columns - 1, 0.0, right) + bias[...]
        for k in range(pair):
            piece = total[:, k * columns : (k + 1) * columns]
            if with_res:
                piece = piece + res[r + k].astype(jnp.float32)
            out[r + k] = piece.astype(out.dtype)


def causal_conv(x0, x1, x2, taps, bias_vec, res, padded, norm=None):
    rows_out = x0.shape[0] - 2 if padded else x0.shape[0]
    outputs = taps.shape[0] // 3
    pair = 4 if rows_out % 4 == 0 else (2 if rows_out % 2 == 0 else 1)
    args = [x0, x1, x2, taps, bias_vec.reshape(outputs, 1)]
    if norm is not None:
        args += [v.reshape(-1, 1).astype(jnp.float32) for v in norm]
    if res is not None:
        args.append(res)
    body = functools.partial(
        conv_body, rows_out=rows_out, pair=pair, with_res=res is not None, padded=padded,
        fused=norm is not None,
    )
    shape = jax.ShapeDtypeStruct((rows_out, outputs, x0.shape[2]), jnp.bfloat16)
    if norm is None:
        return pl.pallas_call(body, out_shape=shape)(*args)
    return pl.pallas_call(body, out_shape=(shape, jax.ShapeDtypeStruct(x2.shape, x2.dtype)))(*args)


def block_sum(values, span_count):
    peers = lax.axis_size("rows")
    if span_count == peers:
        return values
    lead = (lax.axis_index("rows") % span_count == 0).astype(values.dtype)
    return lax.psum(values * lead, "rows")


def statistics(source, cell_count, span_count):
    height, channels, columns = source.shape
    grouped = source.astype(jnp.float32).reshape(height, GROUPS, channels // GROUPS, columns)
    average = block_sum(jnp.sum(grouped, axis=(0, 2, 3)), span_count) / cell_count
    centred = grouped - average[None, :, None, None]
    spread = block_sum(jnp.sum(centred * centred, axis=(0, 2, 3)), span_count) / cell_count
    inverse = lax.rsqrt(spread + EPS)
    per = channels // GROUPS
    return jnp.repeat(average, per), jnp.repeat(inverse, per)


def activate(source, gain_vec, shift_vec, cell_count, span_count):
    height, channels, columns = source.shape
    grouped = source.astype(jnp.float32).reshape(height, GROUPS, channels // GROUPS, columns)
    average = block_sum(jnp.sum(grouped, axis=(0, 2, 3)), span_count) / cell_count
    centred = grouped - average[None, :, None, None]
    spread = block_sum(jnp.sum(centred * centred, axis=(0, 2, 3)), span_count) / cell_count
    inverse = lax.rsqrt(spread + EPS)
    normed = (centred * inverse[None, :, None, None]).reshape(height, channels, columns)
    normed = normed * gain_vec[None, :, None] + shift_vec[None, :, None]
    return jax.nn.silu(normed).astype(jnp.bfloat16)


def run_frame(source, first_hist, second_hist, kernels, biases, gains, shifts, cell_count, span_count):
    padded = span_count != lax.axis_size("rows")
    if not padded:
        average, inverse = statistics(source, cell_count, span_count)
        norm = (average, inverse, gains[0], shifts[0])
        hidden, first_in = causal_conv(
            first_hist[0], first_hist[1], source, kernels[0], biases[0], None, False, norm
        )
        average, inverse = statistics(hidden, cell_count, span_count)
        norm = (average, inverse, gains[1], shifts[1])
        result, second_in = causal_conv(
            second_hist[0], second_hist[1], hidden, kernels[1], biases[1], source, False, norm
        )
        return (result, (first_hist[1], first_in), (second_hist[1], second_in))
    first_in = with_rim(activate(source, gains[0], shifts[0], cell_count, span_count), 0, span_count)
    hidden = causal_conv(first_hist[0], first_hist[1], first_in, kernels[0], biases[0], None, padded)
    second_in = with_rim(activate(hidden, gains[1], shifts[1], cell_count, span_count), 0, span_count)
    result = causal_conv(second_hist[0], second_hist[1], second_in, kernels[1], biases[1], source, padded)
    return (result, (first_hist[1], first_in), (second_hist[1], second_in))


def shards(frames, causal_cache, conv_weight, conv_bias, norm_gain, norm_shift):
    phase_no = lax.axis_index("phase")
    phase_count = lax.axis_size("phase")
    peers = lax.axis_size("rows")
    frame_count = frames.shape[0]
    channels = frames.shape[1]
    rows_here = frames.shape[2]
    columns = frames.shape[3]
    span_count = span_devices(peers, rows_here)
    span = rows_here * span_count
    cell_count = float(channels // GROUPS * rows_here * peers * columns)
    padded = span_count != peers
    frames_t = jnp.transpose(frames, (0, 2, 1, 3))
    cache_t = jnp.transpose(causal_cache[0], (0, 1, 3, 2, 4))
    early = gather_span(jnp.stack([frames_t[0], cache_t[0, 0], cache_t[0, 1]]), 1, span_count)
    late = gather_span(jnp.stack([cache_t[1, 0], cache_t[1, 1]] + list(frames_t[1:])), 1, span_count)
    frames_span = [early[0]] + [late[2 + f] for f in range(frame_count - 1)]
    first_hist = tuple(with_rim(early[1 + k], 0, span_count) for k in range(2))
    second_hist = tuple(with_rim(late[k], 0, span_count) for k in range(2))
    local_taps = (arrange_taps(conv_weight[0, 0]), arrange_taps(conv_weight[0, 1]))
    incoming = jnp.zeros_like(frames_span[0])
    produced = [jnp.zeros_like(frames_span[0]) for _ in range(frame_count)]
    tick_count = frame_count + phase_count - 1
    for tick_no in range(tick_count):
        frame_no = tick_no - phase_no
        active_now = jnp.logical_and(frame_no >= 0, frame_no < frame_count)
        source = jnp.where(phase_no == 0, frames_span[min(tick_no, frame_count - 1)], incoming)
        result, first_next, second_next = run_frame(
            source, first_hist, second_hist, local_taps, conv_bias[0], norm_gain[0], norm_shift[0],
            cell_count, span_count,
        )
        first_hist = tuple(jnp.where(active_now, a, b) for a, b in zip(first_next, first_hist))
        second_hist = tuple(jnp.where(active_now, a, b) for a, b in zip(second_next, second_hist))
        for f in range(frame_count):
            if 0 <= tick_no - f < phase_count:
                produced[f] = jnp.where(frame_no == f, result, produced[f])
        if tick_no + 1 < tick_count:
            incoming = pass_on(result, span_count)
    start = (lax.axis_index("rows") % span_count) * rows_here
    rim = 1 if padded else 0
    produced = jnp.stack([lax.dynamic_slice_in_dim(p, start, rows_here, axis=0) for p in produced])
    new_cache = jnp.stack(
        [
            jnp.stack([lax.dynamic_slice_in_dim(h, start + rim, rows_here, axis=0) for h in hist])
            for hist in (first_hist, second_hist)
        ]
    )
    produced = jnp.transpose(produced, (0, 2, 1, 3))
    new_cache = jnp.transpose(new_cache, (0, 1, 3, 2, 4))
    return (produced[None], new_cache[None])


def solution(mesh):
    in_specs = (
        P(None, None, "rows", None),
        P("phase", None, None, None, "rows", None),
        P("phase", None, None, None, None, None, None),
        P("phase", None, None),
        P("phase", None, None),
        P("phase", None, None),
    )
    out_specs = (P("phase", None, None, "rows", None), P("phase", None, None, None, "rows", None))
    return jax.shard_map(shards, mesh=mesh, in_specs=in_specs, out_specs=out_specs, check_vma=False)
```

```python
import jax
import jax.numpy as jnp
from jax import lax
from jax.sharding import PartitionSpec as P
from jax.experimental import pallas as pl
from jax.experimental.pallas import tpu as pltpu
import functools

GROUPS = 32
EPS = 1e-06
MAX_SPAN = 16


def span_devices(peers, rows_here):
    count = 1
    while count * 2 <= peers and peers % (count * 2) == 0 and count * 2 * rows_here <= MAX_SPAN:
        count *= 2
    return count


def gather_span(array, dim, span_count):
    if span_count == 1:
        return array
    peers = lax.axis_size("rows")
    if span_count == peers:
        return lax.all_gather(array, "rows", axis=dim, tiled=True)
    place = lax.axis_index("rows") % span_count
    pieces = [array]
    for shift in range(1, span_count):
        pairs = [
            (b * span_count + p, b * span_count + (p + shift) % span_count)
            for b in range(peers // span_count)
            for p in range(span_count)
        ]
        pieces.append(lax.ppermute(array, "rows", pairs))
    stacked = jnp.stack(pieces)
    order = (place - jnp.arange(span_count)) % span_count
    picked = jnp.take(stacked, order, axis=0)
    picked = jnp.moveaxis(picked, 0, dim)
    shape = list(array.shape)
    shape[dim] = shape[dim] * span_count
    return picked.reshape(shape)


def with_rim(array, dim, span_count):
    peers = lax.axis_size("rows")
    length = array.shape[dim]
    if span_count == peers:
        return array
    up = [(i, i + span_count) for i in range(peers - span_count)]
    down = [(j, i) for i, j in up]
    last = lax.slice_in_dim(array, length - 1, length, axis=dim)
    leading = lax.slice_in_dim(array, 0, 1, axis=dim)
    before = lax.ppermute(last, "rows", up)
    after = lax.ppermute(leading, "rows", down)
    return jnp.concatenate([before, array, after], axis=dim)


def pass_on(result, span_count):
    phase_count = lax.axis_size("phase")
    forward = [(s, s + 1) for s in range(phase_count - 1)]
    length = result.shape[0]
    if span_count % 2 or length % 2:
        return lax.ppermute(result, "phase", forward)
    peers = lax.axis_size("rows")
    half = length // 2
    core = lax.axis_index("rows") % 2
    mine = lax.dynamic_slice_in_dim(result, core * half, half, axis=0)
    got = lax.ppermute(mine, "phase", forward)
    other = lax.ppermute(got, "rows", [(i, i ^ 1) for i in range(peers)])
    return jnp.where(core == 0, jnp.concatenate([got, other]), jnp.concatenate([other, got]))


def arrange_taps(weight):
    outputs = weight.shape[3]
    channels = weight.shape[4]
    return jnp.transpose(weight, (2, 3, 0, 1, 4)).reshape(3 * outputs, 9 * channels)


def conv_body(x0, x1, x2, taps, bias, *rest, rows_out, pair, with_res, padded, fused):
    rest = list(rest)
    columns = x0.shape[2]
    if fused:
        member, gain, shift = rest[:3]
        rest = rest[3:]
    res = rest.pop(0) if with_res else None
    out = rest[0]
    if fused:
        raw = x2
        x2 = rest[1]
        count = float(rows_out * columns * (raw.shape[1] // GROUPS))

        def group_total(acc):
            spread = jnp.dot(member[...], acc, precision=lax.Precision.HIGHEST, preferred_element_type=jnp.float32)
            return jnp.sum(spread, axis=1, keepdims=True)

        acc = raw[0].astype(jnp.float32)
        for r in range(1, rows_out):
            acc = acc + raw[r].astype(jnp.float32)
        average = group_total(acc) / count
        acc = jnp.square(raw[0].astype(jnp.float32) - average)
        for r in range(1, rows_out):
            acc = acc + jnp.square(raw[r].astype(jnp.float32) - average)
        inverse = lax.rsqrt(group_total(acc) / count + EPS)
        for r in range(rows_out):
            value = (raw[r].astype(jnp.float32) - average) * inverse
            value = value * gain[...] + shift[...]
            x2[r] = (value / (1.0 + jnp.exp(-value))).astype(x2.dtype)
    outputs = out.shape[1]
    channels = x0.shape[1]
    lanes = pair * columns
    lane = lax.broadcasted_iota(jnp.int32, (outputs, lanes), 1) % columns
    frames = (x0, x1, x2)

    def column(r):
        if padded or 0 < r < rows_out - 1:
            base = r if padded else r - 1
            parts = [x[pl.ds(base, 3)] for x in frames]
            return jnp.concatenate(parts, axis=0).reshape(9 * channels, columns)
        zero = jnp.zeros((1, channels, columns), x0.dtype)
        parts = []
        for x in frames:
            for dy in range(3):
                q = r + dy - 1
                parts.append(zero if q < 0 or q >= rows_out else x[pl.ds(q, 1)])
        return jnp.concatenate(parts, axis=0).reshape(9 * channels, columns)

    for r in range(0, rows_out, pair):
        cols = [column(r + k) for k in range(pair)]
        rhs = cols[0] if pair == 1 else jnp.concatenate(cols, axis=1)
        acc = jnp.dot(taps[...], rhs, preferred_element_type=jnp.float32)
        left = pltpu.roll(acc[:outputs], 1, 1)
        right = pltpu.roll(acc[2 * outputs :], lanes - 1, 1)
        total = acc[outputs : 2 * outputs] + jnp.where(lane == 0, 0.0, left)
        total = total + jnp.where(lane == columns - 1, 0.0, right) + bias[...]
        for k in range(pair):
            piece = total[:, k * columns : (k + 1) * columns]
            if with_res:
                piece = piece + res[r + k].astype(jnp.float32)
            out[r + k] = piece.astype(out.dtype)


def causal_conv(x0, x1, x2, taps, bias_vec, res, padded, norm=None):
    rows_out = x0.shape[0] - 2 if padded else x0.shape[0]
    outputs = taps.shape[0] // 3
    pair = 4 if rows_out % 4 == 0 else (2 if rows_out % 2 == 0 else 1)
    args = [x0, x1, x2, taps, bias_vec.reshape(outputs, 1)]
    if norm is not None:
        channels = x2.shape[1]
        group_of = jnp.arange(channels) // (channels // GROUPS)
        args.append((group_of[:, None] == group_of[None, :]).astype(jnp.float32))
        args += [v.reshape(-1, 1).astype(jnp.float32) for v in norm]
    if res is not None:
        args.append(res)
    body = functools.partial(
        conv_body, rows_out=rows_out, pair=pair, with_res=res is not None, padded=padded,
        fused=norm is not None,
    )
    shape = jax.ShapeDtypeStruct((rows_out, outputs, x0.shape[2]), jnp.bfloat16)
    if norm is None:
        return pl.pallas_call(body, out_shape=shape)(*args)
    return pl.pallas_call(body, out_shape=(shape, jax.ShapeDtypeStruct(x2.shape, x2.dtype)))(*args)


def block_sum(values, span_count):
    peers = lax.axis_size("rows")
    if span_count == peers:
        return values
    lead = (lax.axis_index("rows") % span_count == 0).astype(values.dtype)
    return lax.psum(values * lead, "rows")


def activate(source, gain_vec, shift_vec, cell_count, span_count):
    height, channels, columns = source.shape
    grouped = source.astype(jnp.float32).reshape(height, GROUPS, channels // GROUPS, columns)
    average = block_sum(jnp.sum(grouped, axis=(0, 2, 3)), span_count) / cell_count
    centred = grouped - average[None, :, None, None]
    spread = block_sum(jnp.sum(centred * centred, axis=(0, 2, 3)), span_count) / cell_count
    inverse = lax.rsqrt(spread + EPS)
    normed = (centred * inverse[None, :, None, None]).reshape(height, channels, columns)
    normed = normed * gain_vec[None, :, None] + shift_vec[None, :, None]
    return jax.nn.silu(normed).astype(jnp.bfloat16)


def run_frame(source, first_hist, second_hist, kernels, biases, gains, shifts, cell_count, span_count):
    padded = span_count != lax.axis_size("rows")
    if not padded:
        norm = (gains[0], shifts[0])
        hidden, first_in = causal_conv(
            first_hist[0], first_hist[1], source, kernels[0], biases[0], None, False, norm
        )
        norm = (gains[1], shifts[1])
        result, second_in = causal_conv(
            second_hist[0], second_hist[1], hidden, kernels[1], biases[1], source, False, norm
        )
        return (result, (first_hist[1], first_in), (second_hist[1], second_in))
    first_in = with_rim(activate(source, gains[0], shifts[0], cell_count, span_count), 0, span_count)
    hidden = causal_conv(first_hist[0], first_hist[1], first_in, kernels[0], biases[0], None, padded)
    second_in = with_rim(activate(hidden, gains[1], shifts[1], cell_count, span_count), 0, span_count)
    result = causal_conv(second_hist[0], second_hist[1], second_in, kernels[1], biases[1], source, padded)
    return (result, (first_hist[1], first_in), (second_hist[1], second_in))


def shards(frames, causal_cache, conv_weight, conv_bias, norm_gain, norm_shift):
    phase_no = lax.axis_index("phase")
    phase_count = lax.axis_size("phase")
    peers = lax.axis_size("rows")
    frame_count = frames.shape[0]
    channels = frames.shape[1]
    rows_here = frames.shape[2]
    columns = frames.shape[3]
    span_count = span_devices(peers, rows_here)
    span = rows_here * span_count
    cell_count = float(channels // GROUPS * rows_here * peers * columns)
    padded = span_count != peers
    frames_t = jnp.transpose(frames, (0, 2, 1, 3))
    cache_t = jnp.transpose(causal_cache[0], (0, 1, 3, 2, 4))
    early = gather_span(jnp.stack([frames_t[0], cache_t[0, 0], cache_t[0, 1]]), 1, span_count)
    late = gather_span(jnp.stack([cache_t[1, 0], cache_t[1, 1]] + list(frames_t[1:])), 1, span_count)
    frames_span = [early[0]] + [late[2 + f] for f in range(frame_count - 1)]
    first_hist = tuple(with_rim(early[1 + k], 0, span_count) for k in range(2))
    second_hist = tuple(with_rim(late[k], 0, span_count) for k in range(2))
    local_taps = (arrange_taps(conv_weight[0, 0]), arrange_taps(conv_weight[0, 1]))
    incoming = jnp.zeros_like(frames_span[0])
    produced = [jnp.zeros_like(frames_span[0]) for _ in range(frame_count)]
    tick_count = frame_count + phase_count - 1
    for tick_no in range(tick_count):
        frame_no = tick_no - phase_no
        active_now = jnp.logical_and(frame_no >= 0, frame_no < frame_count)
        source = jnp.where(phase_no == 0, frames_span[min(tick_no, frame_count - 1)], incoming)
        result, first_next, second_next = run_frame(
            source, first_hist, second_hist, local_taps, conv_bias[0], norm_gain[0], norm_shift[0],
            cell_count, span_count,
        )
        first_hist = tuple(jnp.where(active_now, a, b) for a, b in zip(first_next, first_hist))
        second_hist = tuple(jnp.where(active_now, a, b) for a, b in zip(second_next, second_hist))
        for f in range(frame_count):
            if 0 <= tick_no - f < phase_count:
                produced[f] = jnp.where(frame_no == f, result, produced[f])
        if tick_no + 1 < tick_count:
            incoming = pass_on(result, span_count)
    start = (lax.axis_index("rows") % span_count) * rows_here
    rim = 1 if padded else 0
    produced = jnp.stack([lax.dynamic_slice_in_dim(p, start, rows_here, axis=0) for p in produced])
    new_cache = jnp.stack(
        [
            jnp.stack([lax.dynamic_slice_in_dim(h, start + rim, rows_here, axis=0) for h in hist])
            for hist in (first_hist, second_hist)
        ]
    )
    produced = jnp.transpose(produced, (0, 2, 1, 3))
    new_cache = jnp.transpose(new_cache, (0, 1, 3, 2, 4))
    return (produced[None], new_cache[None])


def solution(mesh):
    in_specs = (
        P(None, None, "rows", None),
        P("phase", None, None, None, "rows", None),
        P("phase", None, None, None, None, None, None),
        P("phase", None, None),
        P("phase", None, None),
        P("phase", None, None),
    )
    out_specs = (P("phase", None, None, "rows", None), P("phase", None, None, None, "rows", None))
    return jax.shard_map(shards, mesh=mesh, in_specs=in_specs, out_specs=out_specs, check_vma=False)
```

```python
import jax
import jax.numpy as jnp
from jax import lax
from jax.sharding import PartitionSpec as P
from jax.experimental import pallas as pl
from jax.experimental.pallas import tpu as pltpu
import functools

GROUPS = 32
EPS = 1e-06
MAX_SPAN = 16


def span_devices(peers, rows_here):
    count = 1
    while count * 2 <= peers and peers % (count * 2) == 0 and count * 2 * rows_here <= MAX_SPAN:
        count *= 2
    return count


def gather_span(array, dim, span_count):
    if span_count == 1:
        return array
    peers = lax.axis_size("rows")
    if span_count == peers:
        return lax.all_gather(array, "rows", axis=dim, tiled=True)
    place = lax.axis_index("rows") % span_count
    pieces = [array]
    for shift in range(1, span_count):
        pairs = [
            (b * span_count + p, b * span_count + (p + shift) % span_count)
            for b in range(peers // span_count)
            for p in range(span_count)
        ]
        pieces.append(lax.ppermute(array, "rows", pairs))
    stacked = jnp.stack(pieces)
    order = (place - jnp.arange(span_count)) % span_count
    picked = jnp.take(stacked, order, axis=0)
    picked = jnp.moveaxis(picked, 0, dim)
    shape = list(array.shape)
    shape[dim] = shape[dim] * span_count
    return picked.reshape(shape)


def with_rim(array, dim, span_count):
    peers = lax.axis_size("rows")
    length = array.shape[dim]
    if span_count == peers:
        return array
    up = [(i, i + span_count) for i in range(peers - span_count)]
    down = [(j, i) for i, j in up]
    last = lax.slice_in_dim(array, length - 1, length, axis=dim)
    leading = lax.slice_in_dim(array, 0, 1, axis=dim)
    before = lax.ppermute(last, "rows", up)
    after = lax.ppermute(leading, "rows", down)
    return jnp.concatenate([before, array, after], axis=dim)


def pass_on(result, span_count):
    phase_count = lax.axis_size("phase")
    forward = [(s, s + 1) for s in range(phase_count - 1)]
    length = result.shape[0]
    if span_count % 2 or length % 2:
        return lax.ppermute(result, "phase", forward)
    peers = lax.axis_size("rows")
    half = length // 2
    core = lax.axis_index("rows") % 2
    mine = lax.dynamic_slice_in_dim(result, core * half, half, axis=0)
    got = lax.ppermute(mine, "phase", forward)
    other = lax.ppermute(got, "rows", [(i, i ^ 1) for i in range(peers)])
    return jnp.where(core == 0, jnp.concatenate([got, other]), jnp.concatenate([other, got]))


def arrange_taps(weight):
    outputs = weight.shape[3]
    channels = weight.shape[4]
    return jnp.transpose(weight, (2, 3, 0, 1, 4)).reshape(3 * outputs, 9 * channels)


def conv_rows(x0, x1, x2, taps, bias, res, out, rows_out, padded):
    outputs = out.shape[1]
    channels = x0.shape[1]
    columns = x0.shape[2]
    pair = 4 if rows_out % 4 == 0 else (2 if rows_out % 2 == 0 else 1)
    lanes = pair * columns
    lane = lax.broadcasted_iota(jnp.int32, (outputs, lanes), 1) % columns
    frames = (x0, x1, x2)

    def column(r):
        if padded or 0 < r < rows_out - 1:
            base = r if padded else r - 1
            parts = [x[pl.ds(base, 3)] for x in frames]
            return jnp.concatenate(parts, axis=0).reshape(9 * channels, columns)
        zero = jnp.zeros((1, channels, columns), x0.dtype)
        parts = []
        for x in frames:
            for dy in range(3):
                q = r + dy - 1
                parts.append(zero if q < 0 or q >= rows_out else x[pl.ds(q, 1)])
        return jnp.concatenate(parts, axis=0).reshape(9 * channels, columns)

    for r in range(0, rows_out, pair):
        cols = [column(r + k) for k in range(pair)]
        rhs = cols[0] if pair == 1 else jnp.concatenate(cols, axis=1)
        acc = jnp.dot(taps[...], rhs, preferred_element_type=jnp.float32)
        left = pltpu.roll(acc[:outputs], 1, 1)
        right = pltpu.roll(acc[2 * outputs :], lanes - 1, 1)
        total = acc[outputs : 2 * outputs] + jnp.where(lane == 0, 0.0, left)
        total = total + jnp.where(lane == columns - 1, 0.0, right) + bias[...]
        for k in range(pair):
            piece = total[:, k * columns : (k + 1) * columns]
            if res is not None:
                piece = piece + res[r + k].astype(jnp.float32)
            out[r + k] = piece.astype(out.dtype)


def conv_body(x0, x1, x2, taps, bias, *rest, rows_out, with_res, padded):
    res = rest[0] if with_res else None
    conv_rows(x0, x1, x2, taps, bias, res, rest[-1], rows_out, padded)


def causal_conv(x0, x1, x2, taps, bias_vec, res, padded):
    rows_out = x0.shape[0] - 2 if padded else x0.shape[0]
    outputs = taps.shape[0] // 3
    args = [x0, x1, x2, taps, bias_vec.reshape(outputs, 1)]
    if res is not None:
        args.append(res)
    body = functools.partial(conv_body, rows_out=rows_out, with_res=res is not None, padded=padded)
    shape = jax.ShapeDtypeStruct((rows_out, outputs, x0.shape[2]), jnp.bfloat16)
    return pl.pallas_call(body, out_shape=shape)(*args)


def fused_body(flags, c0, c1, a_p, a_pp, src_a, src_b, src_c, taps, bias, member, gain, shift, *rest,
               pick_raw):
    rest = list(rest)
    own = None if pick_raw else rest.pop(0)
    out, act, x0, x1, rawbuf, sems = rest
    rows_out, channels, columns = out.shape[0], x0.shape[1], x0.shape[2]
    half = rows_out // 2
    first, second, mode = flags[0], flags[1], flags[2]

    def copies(pairs):
        started = [pltpu.make_async_copy(a, b, sems.at[i]) for i, (a, b) in enumerate(pairs)]
        for c in started:
            c.start()
        for c in started:
            c.wait()

    @pl.when(mode == 0)
    def _():
        copies([(src_a, rawbuf)])

    @pl.when(mode == 1)
    def _():
        copies([(src_b, rawbuf.at[pl.ds(0, half)]), (src_c, rawbuf.at[pl.ds(half, half)])])

    @pl.when(mode == 2)
    def _():
        copies([(src_c, rawbuf.at[pl.ds(0, half)]), (src_b, rawbuf.at[pl.ds(half, half)])])

    raw, res = (rawbuf, None) if pick_raw else (own, rawbuf)

    count = float(rows_out * columns * (channels // GROUPS))

    def group_total(acc):
        spread = jnp.dot(member[...], acc, precision=lax.Precision.HIGHEST, preferred_element_type=jnp.float32)
        return jnp.sum(spread, axis=1, keepdims=True)

    acc = raw[0].astype(jnp.float32)
    for r in range(1, rows_out):
        acc = acc + raw[r].astype(jnp.float32)
    average = group_total(acc) / count
    acc = jnp.square(raw[0].astype(jnp.float32) - average)
    for r in range(1, rows_out):
        acc = acc + jnp.square(raw[r].astype(jnp.float32) - average)
    inverse = lax.rsqrt(group_total(acc) / count + EPS)
    for r in range(rows_out):
        value = (raw[r].astype(jnp.float32) - average) * inverse
        value = value * gain[...] + shift[...]
        act[r] = (value / (1.0 + jnp.exp(-value))).astype(act.dtype)

    @pl.when(first == 1)
    def _():
        copies([(c0, x0), (c1, x1)])

    @pl.when(jnp.logical_and(first == 0, second == 1))
    def _():
        copies([(c1, x0), (a_p, x1)])

    @pl.when(jnp.logical_and(first == 0, second == 0))
    def _():
        copies([(a_pp, x0), (a_p, x1)])

    conv_rows(x0, x1, act, taps, bias, res, out, rows_out, False)


def fused_conv(flags, hist, sources, taps, bias_vec, norm, own=None):
    c0 = hist[0]
    rows_out, channels, columns = c0.shape
    outputs = taps.shape[0] // 3
    group_of = jnp.arange(channels) // (channels // GROUPS)
    member = (group_of[:, None] == group_of[None, :]).astype(jnp.float32)
    vmem = pl.BlockSpec(memory_space=pltpu.VMEM)
    anywhere = pl.BlockSpec(memory_space=pl.ANY)
    args = [flags] + list(hist) + list(sources) + [taps, bias_vec.reshape(outputs, 1), member]
    args += [v.reshape(-1, 1).astype(jnp.float32) for v in norm]
    specs = [pl.BlockSpec(memory_space=pltpu.SMEM)] + [anywhere] * 7 + [vmem] * 5
    if own is not None:
        args.append(own)
        specs.append(vmem)
    frame = jax.ShapeDtypeStruct((rows_out, channels, columns), jnp.bfloat16)
    body = functools.partial(fused_body, pick_raw=own is None)
    return pl.pallas_call(
        body,
        out_shape=(jax.ShapeDtypeStruct((rows_out, outputs, columns), jnp.bfloat16), frame),
        in_specs=specs,
        out_specs=(vmem, vmem),
        scratch_shapes=[
            pltpu.VMEM((rows_out, channels, columns), jnp.bfloat16),
            pltpu.VMEM((rows_out, channels, columns), jnp.bfloat16),
            pltpu.VMEM((rows_out, channels, columns), jnp.bfloat16),
            pltpu.SemaphoreType.DMA((2,)),
        ],
    )(*args)


def block_sum(values, span_count):
    peers = lax.axis_size("rows")
    if span_count == peers:
        return values
    lead = (lax.axis_index("rows") % span_count == 0).astype(values.dtype)
    return lax.psum(values * lead, "rows")


def activate(source, gain_vec, shift_vec, cell_count, span_count):
    height, channels, columns = source.shape
    grouped = source.astype(jnp.float32).reshape(height, GROUPS, channels // GROUPS, columns)
    average = block_sum(jnp.sum(grouped, axis=(0, 2, 3)), span_count) / cell_count
    centred = grouped - average[None, :, None, None]
    spread = block_sum(jnp.sum(centred * centred, axis=(0, 2, 3)), span_count) / cell_count
    inverse = lax.rsqrt(spread + EPS)
    normed = (centred * inverse[None, :, None, None]).reshape(height, channels, columns)
    normed = normed * gain_vec[None, :, None] + shift_vec[None, :, None]
    return jax.nn.silu(normed).astype(jnp.bfloat16)


def run_frame(source, first_hist, second_hist, kernels, biases, gains, shifts, cell_count, span_count):
    padded = span_count != lax.axis_size("rows")
    first_in = with_rim(activate(source, gains[0], shifts[0], cell_count, span_count), 0, span_count)
    hidden = causal_conv(first_hist[0], first_hist[1], first_in, kernels[0], biases[0], None, padded)
    second_in = with_rim(activate(hidden, gains[1], shifts[1], cell_count, span_count), 0, span_count)
    result = causal_conv(second_hist[0], second_hist[1], second_in, kernels[1], biases[1], source, padded)
    return (result, (first_hist[1], first_in), (second_hist[1], second_in))


def shards_whole(frames, causal_cache, conv_weight, conv_bias, norm_gain, norm_shift):
    phase_no = lax.axis_index("phase")
    phase_count = lax.axis_size("phase")
    peers = lax.axis_size("rows")
    frame_count, channels, rows_here, columns = frames.shape
    span = rows_here * peers
    half = span // 2
    core = lax.axis_index("rows") % 2
    start = lax.axis_index("rows") * rows_here
    forward = [(s, s + 1) for s in range(phase_count - 1)]
    frames_t = jnp.transpose(frames, (0, 2, 1, 3))
    cache_t = jnp.transpose(causal_cache[0], (0, 1, 3, 2, 4))
    early = lax.all_gather(jnp.stack([frames_t[0], cache_t[0, 0], cache_t[0, 1]]), "rows", axis=1, tiled=True)
    late = lax.all_gather(
        jnp.stack([cache_t[1, 0], cache_t[1, 1]] + list(frames_t[1:])), "rows", axis=1, tiled=True
    )
    frames_span = [early[0]] + [late[2 + f] for f in range(frame_count - 1)]
    caches = ((early[1], early[2]), (late[0], late[1]))
    taps = (arrange_taps(conv_weight[0, 0]), arrange_taps(conv_weight[0, 1]))

    def own_rows(x):
        return lax.dynamic_slice_in_dim(x, start, rows_here, axis=0)

    got = other = jnp.zeros((half, channels, columns), jnp.bfloat16)
    acts = ([], [])
    blank = jnp.zeros((rows_here, channels, columns), jnp.bfloat16)
    produced = [blank] * frame_count
    kept = [[blank, blank], [blank, blank]]
    mode = jnp.where(phase_no == 0, 0, 1 + core)
    tick_count = frame_count + phase_count - 1
    for tick_no in range(tick_count):
        frame_no = tick_no - phase_no
        flags = jnp.stack([frame_no == 0, frame_no == 1, mode]).astype(jnp.int32)
        sources = (frames_span[min(tick_no, frame_count - 1)], got, other)
        hists = []
        for j in range(2):
            c0, c1 = caches[j]
            a_p = acts[j][-1] if acts[j] else c0
            a_pp = acts[j][-2] if len(acts[j]) > 1 else c0
            hists.append((c0, c1, a_p, a_pp))
        hidden, first_in = fused_conv(
            flags, hists[0], sources, taps[0], conv_bias[0, 0], (norm_gain[0, 0], norm_shift[0, 0])
        )
        result, second_in = fused_conv(
            flags, hists[1], sources, taps[1], conv_bias[0, 1], (norm_gain[0, 1], norm_shift[0, 1]), hidden
        )
        last = frame_no == frame_count - 1
        for j, a in enumerate((first_in, second_in)):
            c0, c1, a_p, _ = hists[j]
            newer = jnp.where(frame_no == 0, own_rows(c1), own_rows(a_p))
            kept[j] = [jnp.where(last, newer, kept[j][0]), jnp.where(last, own_rows(a), kept[j][1])]
            acts[j].append(a)
        for f in range(frame_count):
            if 0 <= tick_no - f < phase_count:
                produced[f] = jnp.where(frame_no == f, own_rows(result), produced[f])
        if tick_no + 1 < tick_count:
            mine = lax.dynamic_slice_in_dim(result, core * half, half, axis=0)
            got = lax.ppermute(mine, "phase", forward)
            other = lax.ppermute(got, "rows", [(i, i ^ 1) for i in range(peers)])
    produced = jnp.transpose(jnp.stack(produced), (0, 2, 1, 3))
    new_cache = jnp.transpose(jnp.stack([jnp.stack(k) for k in kept]), (0, 1, 3, 2, 4))
    return (produced[None], new_cache[None])


def shards(frames, causal_cache, conv_weight, conv_bias, norm_gain, norm_shift):
    peers = lax.axis_size("rows")
    rows_here = frames.shape[2]
    if span_devices(peers, rows_here) == peers and (rows_here * peers) % 2 == 0:
        return shards_whole(frames, causal_cache, conv_weight, conv_bias, norm_gain, norm_shift)
    return shards_split(frames, causal_cache, conv_weight, conv_bias, norm_gain, norm_shift)


def shards_split(frames, causal_cache, conv_weight, conv_bias, norm_gain, norm_shift):
    phase_no = lax.axis_index("phase")
    phase_count = lax.axis_size("phase")
    peers = lax.axis_size("rows")
    frame_count = frames.shape[0]
    channels = frames.shape[1]
    rows_here = frames.shape[2]
    columns = frames.shape[3]
    span_count = span_devices(peers, rows_here)
    span = rows_here * span_count
    cell_count = float(channels // GROUPS * rows_here * peers * columns)
    padded = span_count != peers
    frames_t = jnp.transpose(frames, (0, 2, 1, 3))
    cache_t = jnp.transpose(causal_cache[0], (0, 1, 3, 2, 4))
    early = gather_span(jnp.stack([frames_t[0], cache_t[0, 0], cache_t[0, 1]]), 1, span_count)
    late = gather_span(jnp.stack([cache_t[1, 0], cache_t[1, 1]] + list(frames_t[1:])), 1, span_count)
    frames_span = [early[0]] + [late[2 + f] for f in range(frame_count - 1)]
    first_hist = tuple(with_rim(early[1 + k], 0, span_count) for k in range(2))
    second_hist = tuple(with_rim(late[k], 0, span_count) for k in range(2))
    local_taps = (arrange_taps(conv_weight[0, 0]), arrange_taps(conv_weight[0, 1]))
    incoming = jnp.zeros_like(frames_span[0])
    produced = [jnp.zeros_like(frames_span[0]) for _ in range(frame_count)]
    tick_count = frame_count + phase_count - 1
    for tick_no in range(tick_count):
        frame_no = tick_no - phase_no
        active_now = jnp.logical_and(frame_no >= 0, frame_no < frame_count)
        source = jnp.where(phase_no == 0, frames_span[min(tick_no, frame_count - 1)], incoming)
        result, first_next, second_next = run_frame(
            source, first_hist, second_hist, local_taps, conv_bias[0], norm_gain[0], norm_shift[0],
            cell_count, span_count,
        )
        first_hist = tuple(jnp.where(active_now, a, b) for a, b in zip(first_next, first_hist))
        second_hist = tuple(jnp.where(active_now, a, b) for a, b in zip(second_next, second_hist))
        for f in range(frame_count):
            if 0 <= tick_no - f < phase_count:
                produced[f] = jnp.where(frame_no == f, result, produced[f])
        if tick_no + 1 < tick_count:
            incoming = pass_on(result, span_count)
    start = (lax.axis_index("rows") % span_count) * rows_here
    rim = 1 if padded else 0
    produced = jnp.stack([lax.dynamic_slice_in_dim(p, start, rows_here, axis=0) for p in produced])
    new_cache = jnp.stack(
        [
            jnp.stack([lax.dynamic_slice_in_dim(h, start + rim, rows_here, axis=0) for h in hist])
            for hist in (first_hist, second_hist)
        ]
    )
    produced = jnp.transpose(produced, (0, 2, 1, 3))
    new_cache = jnp.transpose(new_cache, (0, 1, 3, 2, 4))
    return (produced[None], new_cache[None])


def solution(mesh):
    in_specs = (
        P(None, None, "rows", None),
        P("phase", None, None, None, "rows", None),
        P("phase", None, None, None, None, None, None),
        P("phase", None, None),
        P("phase", None, None),
        P("phase", None, None),
    )
    out_specs = (P("phase", None, None, "rows", None), P("phase", None, None, None, "rows", None))
    return jax.shard_map(shards, mesh=mesh, in_specs=in_specs, out_specs=out_specs, check_vma=False)
```

```python
import jax
import jax.numpy as jnp
from jax import lax
from jax.sharding import PartitionSpec as P
from jax.experimental import pallas as pl
from jax.experimental.pallas import tpu as pltpu
import functools

GROUPS = 32
EPS = 1e-06
MAX_SPAN = 16


def span_devices(peers, rows_here):
    count = 1
    while count * 2 <= peers and peers % (count * 2) == 0 and count * 2 * rows_here <= MAX_SPAN:
        count *= 2
    return count


def gather_span(array, dim, span_count):
    if span_count == 1:
        return array
    peers = lax.axis_size("rows")
    if span_count == peers:
        return lax.all_gather(array, "rows", axis=dim, tiled=True)
    place = lax.axis_index("rows") % span_count
    pieces = [array]
    for shift in range(1, span_count):
        pairs = [
            (b * span_count + p, b * span_count + (p + shift) % span_count)
            for b in range(peers // span_count)
            for p in range(span_count)
        ]
        pieces.append(lax.ppermute(array, "rows", pairs))
    stacked = jnp.stack(pieces)
    order = (place - jnp.arange(span_count)) % span_count
    picked = jnp.take(stacked, order, axis=0)
    picked = jnp.moveaxis(picked, 0, dim)
    shape = list(array.shape)
    shape[dim] = shape[dim] * span_count
    return picked.reshape(shape)


def with_rim(array, dim, span_count):
    peers = lax.axis_size("rows")
    length = array.shape[dim]
    if span_count == peers:
        return array
    up = [(i, i + span_count) for i in range(peers - span_count)]
    down = [(j, i) for i, j in up]
    last = lax.slice_in_dim(array, length - 1, length, axis=dim)
    leading = lax.slice_in_dim(array, 0, 1, axis=dim)
    before = lax.ppermute(last, "rows", up)
    after = lax.ppermute(leading, "rows", down)
    return jnp.concatenate([before, array, after], axis=dim)


def pass_on(result, span_count):
    phase_count = lax.axis_size("phase")
    forward = [(s, s + 1) for s in range(phase_count - 1)]
    length = result.shape[0]
    if span_count % 2 or length % 2:
        return lax.ppermute(result, "phase", forward)
    peers = lax.axis_size("rows")
    half = length // 2
    core = lax.axis_index("rows") % 2
    mine = lax.dynamic_slice_in_dim(result, core * half, half, axis=0)
    got = lax.ppermute(mine, "phase", forward)
    other = lax.ppermute(got, "rows", [(i, i ^ 1) for i in range(peers)])
    return jnp.where(core == 0, jnp.concatenate([got, other]), jnp.concatenate([other, got]))


def arrange_taps(weight):
    outputs = weight.shape[3]
    channels = weight.shape[4]
    return jnp.transpose(weight, (2, 3, 0, 1, 4)).reshape(3 * outputs, 9 * channels)


def conv_rows(x0, x1, x2, taps, bias, res, out, rows_out, padded):
    outputs = out.shape[1]
    channels = x0.shape[1]
    columns = x0.shape[2]
    pair = 4 if rows_out % 4 == 0 else (2 if rows_out % 2 == 0 else 1)
    lanes = pair * columns
    lane = lax.broadcasted_iota(jnp.int32, (outputs, lanes), 1) % columns
    frames = (x0, x1, x2)

    def column(r):
        if padded or 0 < r < rows_out - 1:
            base = r if padded else r - 1
            parts = [x[pl.ds(base, 3)] for x in frames]
            return jnp.concatenate(parts, axis=0).reshape(9 * channels, columns)
        zero = jnp.zeros((1, channels, columns), x0.dtype)
        parts = []
        for x in frames:
            for dy in range(3):
                q = r + dy - 1
                parts.append(zero if q < 0 or q >= rows_out else x[pl.ds(q, 1)])
        return jnp.concatenate(parts, axis=0).reshape(9 * channels, columns)

    for r in range(0, rows_out, pair):
        cols = [column(r + k) for k in range(pair)]
        rhs = cols[0] if pair == 1 else jnp.concatenate(cols, axis=1)
        acc = jnp.dot(taps[...], rhs, preferred_element_type=jnp.float32)
        left = pltpu.roll(acc[:outputs], 1, 1)
        right = pltpu.roll(acc[2 * outputs :], lanes - 1, 1)
        total = acc[outputs : 2 * outputs] + jnp.where(lane == 0, 0.0, left)
        total = total + jnp.where(lane == columns - 1, 0.0, right) + bias[...]
        for k in range(pair):
            piece = total[:, k * columns : (k + 1) * columns]
            if res is not None:
                piece = piece + res[r + k].astype(jnp.float32)
            out[r + k] = piece.astype(out.dtype)


def conv_body(x0, x1, x2, taps, bias, *rest, rows_out, with_res, padded):
    res = rest[0] if with_res else None
    conv_rows(x0, x1, x2, taps, bias, res, rest[-1], rows_out, padded)


def causal_conv(x0, x1, x2, taps, bias_vec, res, padded):
    rows_out = x0.shape[0] - 2 if padded else x0.shape[0]
    outputs = taps.shape[0] // 3
    args = [x0, x1, x2, taps, bias_vec.reshape(outputs, 1)]
    if res is not None:
        args.append(res)
    body = functools.partial(conv_body, rows_out=rows_out, with_res=res is not None, padded=padded)
    shape = jax.ShapeDtypeStruct((rows_out, outputs, x0.shape[2]), jnp.bfloat16)
    return pl.pallas_call(body, out_shape=shape)(*args)


def fused_body(flags, caches, a_p, a_pp, frames, src_b, src_c, taps, bias, member, gain, shift, *rest,
               pick_raw, cache_at, frame_at):
    rest = list(rest)
    own = None if pick_raw else rest.pop(0)
    out, act, x0, x1, rawbuf, sems = rest
    rows_out, channels, columns = out.shape[0], x0.shape[1], x0.shape[2]
    half = rows_out // 2
    first, second, mode = flags[0], flags[1], flags[2]
    c0, c1 = caches.at[cache_at[0]], caches.at[cache_at[1]]
    whole = frames.at[frame_at]
    top, bottom = rawbuf.at[pl.ds(0, half)], rawbuf.at[pl.ds(half, half)]

    def begin(pairs, base):
        for i, (a, b) in enumerate(pairs):
            pltpu.make_async_copy(a, b, sems.at[base + i]).start()

    def finish(pairs, base):
        for i, (a, b) in enumerate(pairs):
            pltpu.make_async_copy(a, b, sems.at[base + i]).wait()

    @pl.when(mode == 0)
    def _():
        begin([(whole.at[pl.ds(0, half)], top), (whole.at[pl.ds(half, half)], bottom)], 0)

    @pl.when(mode == 1)
    def _():
        begin([(src_b, top), (src_c, bottom)], 0)

    @pl.when(mode == 2)
    def _():
        begin([(src_c, top), (src_b, bottom)], 0)

    @pl.when(first == 1)
    def _():
        begin([(c0, x0), (c1, x1)], 2)

    @pl.when(jnp.logical_and(first == 0, second == 1))
    def _():
        begin([(c1, x0), (a_p, x1)], 2)

    @pl.when(jnp.logical_and(first == 0, second == 0))
    def _():
        begin([(a_pp, x0), (a_p, x1)], 2)

    source_copies = [(src_b, top), (src_c, bottom)]
    history_copies = [(a_pp, x0), (a_p, x1)]
    if pick_raw:
        finish(source_copies, 0)
        raw, res = rawbuf, None
    else:
        raw, res = own, rawbuf

    count = float(rows_out * columns * (channels // GROUPS))

    def group_total(acc):
        spread = jnp.dot(member[...], acc, precision=lax.Precision.HIGHEST, preferred_element_type=jnp.float32)
        return jnp.sum(spread, axis=1, keepdims=True)

    acc = raw[0].astype(jnp.float32)
    for r in range(1, rows_out):
        acc = acc + raw[r].astype(jnp.float32)
    average = group_total(acc) / count
    acc = jnp.square(raw[0].astype(jnp.float32) - average)
    for r in range(1, rows_out):
        acc = acc + jnp.square(raw[r].astype(jnp.float32) - average)
    inverse = lax.rsqrt(group_total(acc) / count + EPS)
    for r in range(rows_out):
        value = (raw[r].astype(jnp.float32) - average) * inverse
        value = value * gain[...] + shift[...]
        act[r] = (value / (1.0 + jnp.exp(-value))).astype(act.dtype)

    finish(history_copies, 2)
    if not pick_raw:
        finish(source_copies, 0)
    conv_rows(x0, x1, act, taps, bias, res, out, rows_out, False)


def fused_conv(flags, caches, cache_at, recent, frames, frame_at, halves, taps, bias_vec, norm, own=None):
    rows_out, channels, columns = recent[0].shape
    outputs = taps.shape[0] // 3
    group_of = jnp.arange(channels) // (channels // GROUPS)
    member = (group_of[:, None] == group_of[None, :]).astype(jnp.float32)
    vmem = pl.BlockSpec(memory_space=pltpu.VMEM)
    anywhere = pl.BlockSpec(memory_space=pl.ANY)
    args = [flags, caches, recent[0], recent[1], frames, halves[0], halves[1]]
    args += [taps, bias_vec.reshape(outputs, 1), member]
    args += [v.reshape(-1, 1).astype(jnp.float32) for v in norm]
    specs = [pl.BlockSpec(memory_space=pltpu.SMEM)] + [anywhere] * 6 + [vmem] * 5
    if own is not None:
        args.append(own)
        specs.append(vmem)
    frame = jax.ShapeDtypeStruct((rows_out, channels, columns), jnp.bfloat16)
    body = functools.partial(
        fused_body, pick_raw=own is None, cache_at=tuple(cache_at), frame_at=frame_at
    )
    return pl.pallas_call(
        body,
        out_shape=(jax.ShapeDtypeStruct((rows_out, outputs, columns), jnp.bfloat16), frame),
        in_specs=specs,
        out_specs=(vmem, vmem),
        scratch_shapes=[
            pltpu.VMEM((rows_out, channels, columns), jnp.bfloat16),
            pltpu.VMEM((rows_out, channels, columns), jnp.bfloat16),
            pltpu.VMEM((rows_out, channels, columns), jnp.bfloat16),
            pltpu.SemaphoreType.DMA((4,)),
        ],
    )(*args)


def block_sum(values, span_count):
    peers = lax.axis_size("rows")
    if span_count == peers:
        return values
    lead = (lax.axis_index("rows") % span_count == 0).astype(values.dtype)
    return lax.psum(values * lead, "rows")


def activate(source, gain_vec, shift_vec, cell_count, span_count):
    height, channels, columns = source.shape
    grouped = source.astype(jnp.float32).reshape(height, GROUPS, channels // GROUPS, columns)
    average = block_sum(jnp.sum(grouped, axis=(0, 2, 3)), span_count) / cell_count
    centred = grouped - average[None, :, None, None]
    spread = block_sum(jnp.sum(centred * centred, axis=(0, 2, 3)), span_count) / cell_count
    inverse = lax.rsqrt(spread + EPS)
    normed = (centred * inverse[None, :, None, None]).reshape(height, channels, columns)
    normed = normed * gain_vec[None, :, None] + shift_vec[None, :, None]
    return jax.nn.silu(normed).astype(jnp.bfloat16)


def run_frame(source, first_hist, second_hist, kernels, biases, gains, shifts, cell_count, span_count):
    padded = span_count != lax.axis_size("rows")
    first_in = with_rim(activate(source, gains[0], shifts[0], cell_count, span_count), 0, span_count)
    hidden = causal_conv(first_hist[0], first_hist[1], first_in, kernels[0], biases[0], None, padded)
    second_in = with_rim(activate(hidden, gains[1], shifts[1], cell_count, span_count), 0, span_count)
    result = causal_conv(second_hist[0], second_hist[1], second_in, kernels[1], biases[1], source, padded)
    return (result, (first_hist[1], first_in), (second_hist[1], second_in))


def shards_whole(frames, causal_cache, conv_weight, conv_bias, norm_gain, norm_shift):
    phase_no = lax.axis_index("phase")
    phase_count = lax.axis_size("phase")
    peers = lax.axis_size("rows")
    frame_count, channels, rows_here, columns = frames.shape
    span = rows_here * peers
    half = span // 2
    core = lax.axis_index("rows") % 2
    start = lax.axis_index("rows") * rows_here
    forward = [(s, s + 1) for s in range(phase_count - 1)]
    frames_t = jnp.transpose(frames, (0, 2, 1, 3))
    cache_t = jnp.transpose(causal_cache[0], (0, 1, 3, 2, 4))
    early = lax.all_gather(jnp.stack([frames_t[0], cache_t[0, 0], cache_t[0, 1]]), "rows", axis=1, tiled=True)
    late = lax.all_gather(
        jnp.stack([cache_t[1, 0], cache_t[1, 1]] + list(frames_t[1:])), "rows", axis=1, tiled=True
    )
    frame_of = [(early, 0)] + [(late, 2 + f) for f in range(frame_count - 1)]
    cache_of = ((early, (1, 2)), (late, (0, 1)))
    taps = (arrange_taps(conv_weight[0, 0]), arrange_taps(conv_weight[0, 1]))

    def own_rows(x):
        return lax.dynamic_slice_in_dim(x, start, rows_here, axis=0)

    got = other = jnp.zeros((half, channels, columns), jnp.bfloat16)
    acts = ([], [])
    blank = jnp.zeros((rows_here, channels, columns), jnp.bfloat16)
    blank_frame = jnp.zeros((span, channels, columns), jnp.bfloat16)
    produced = [blank] * frame_count
    kept = [[blank, blank], [blank, blank]]
    mode = jnp.where(phase_no == 0, 0, 1 + core)
    tick_count = frame_count + phase_count - 1
    for tick_no in range(tick_count):
        frame_no = tick_no - phase_no
        flags = jnp.stack([frame_no == 0, frame_no == 1, mode]).astype(jnp.int32)
        frame_stack, frame_at = frame_of[min(tick_no, frame_count - 1)]
        recents = []
        for j in range(2):
            a_p = acts[j][-1] if acts[j] else blank_frame
            a_pp = acts[j][-2] if len(acts[j]) > 1 else blank_frame
            recents.append((a_p, a_pp))
        hidden, first_in = fused_conv(
            flags, cache_of[0][0], cache_of[0][1], recents[0], frame_stack, frame_at, (got, other),
            taps[0], conv_bias[0, 0], (norm_gain[0, 0], norm_shift[0, 0]),
        )
        result, second_in = fused_conv(
            flags, cache_of[1][0], cache_of[1][1], recents[1], frame_stack, frame_at, (got, other),
            taps[1], conv_bias[0, 1], (norm_gain[0, 1], norm_shift[0, 1]), hidden,
        )
        last = frame_no == frame_count - 1
        for j, a in enumerate((first_in, second_in)):
            stack, (_, k1) = cache_of[j]
            newer = jnp.where(frame_no == 0, own_rows(stack[k1]), own_rows(recents[j][0]))
            kept[j] = [jnp.where(last, newer, kept[j][0]), jnp.where(last, own_rows(a), kept[j][1])]
            acts[j].append(a)
        for f in range(frame_count):
            if 0 <= tick_no - f < phase_count:
                produced[f] = jnp.where(frame_no == f, own_rows(result), produced[f])
        if tick_no + 1 < tick_count:
            mine = lax.dynamic_slice_in_dim(result, core * half, half, axis=0)
            got = lax.ppermute(mine, "phase", forward)
            other = lax.ppermute(got, "rows", [(i, i ^ 1) for i in range(peers)])
    produced = jnp.transpose(jnp.stack(produced), (0, 2, 1, 3))
    new_cache = jnp.transpose(jnp.stack([jnp.stack(k) for k in kept]), (0, 1, 3, 2, 4))
    return (produced[None], new_cache[None])


def shards(frames, causal_cache, conv_weight, conv_bias, norm_gain, norm_shift):
    peers = lax.axis_size("rows")
    rows_here = frames.shape[2]
    if span_devices(peers, rows_here) == peers and (rows_here * peers) % 2 == 0:
        return shards_whole(frames, causal_cache, conv_weight, conv_bias, norm_gain, norm_shift)
    return shards_split(frames, causal_cache, conv_weight, conv_bias, norm_gain, norm_shift)


def shards_split(frames, causal_cache, conv_weight, conv_bias, norm_gain, norm_shift):
    phase_no = lax.axis_index("phase")
    phase_count = lax.axis_size("phase")
    peers = lax.axis_size("rows")
    frame_count = frames.shape[0]
    channels = frames.shape[1]
    rows_here = frames.shape[2]
    columns = frames.shape[3]
    span_count = span_devices(peers, rows_here)
    span = rows_here * span_count
    cell_count = float(channels // GROUPS * rows_here * peers * columns)
    padded = span_count != peers
    frames_t = jnp.transpose(frames, (0, 2, 1, 3))
    cache_t = jnp.transpose(causal_cache[0], (0, 1, 3, 2, 4))
    early = gather_span(jnp.stack([frames_t[0], cache_t[0, 0], cache_t[0, 1]]), 1, span_count)
    late = gather_span(jnp.stack([cache_t[1, 0], cache_t[1, 1]] + list(frames_t[1:])), 1, span_count)
    frames_span = [early[0]] + [late[2 + f] for f in range(frame_count - 1)]
    first_hist = tuple(with_rim(early[1 + k], 0, span_count) for k in range(2))
    second_hist = tuple(with_rim(late[k], 0, span_count) for k in range(2))
    local_taps = (arrange_taps(conv_weight[0, 0]), arrange_taps(conv_weight[0, 1]))
    incoming = jnp.zeros_like(frames_span[0])
    produced = [jnp.zeros_like(frames_span[0]) for _ in range(frame_count)]
    tick_count = frame_count + phase_count - 1
    for tick_no in range(tick_count):
        frame_no = tick_no - phase_no
        active_now = jnp.logical_and(frame_no >= 0, frame_no < frame_count)
        source = jnp.where(phase_no == 0, frames_span[min(tick_no, frame_count - 1)], incoming)
        result, first_next, second_next = run_frame(
            source, first_hist, second_hist, local_taps, conv_bias[0], norm_gain[0], norm_shift[0],
            cell_count, span_count,
        )
        first_hist = tuple(jnp.where(active_now, a, b) for a, b in zip(first_next, first_hist))
        second_hist = tuple(jnp.where(active_now, a, b) for a, b in zip(second_next, second_hist))
        for f in range(frame_count):
            if 0 <= tick_no - f < phase_count:
                produced[f] = jnp.where(frame_no == f, result, produced[f])
        if tick_no + 1 < tick_count:
            incoming = pass_on(result, span_count)
    start = (lax.axis_index("rows") % span_count) * rows_here
    rim = 1 if padded else 0
    produced = jnp.stack([lax.dynamic_slice_in_dim(p, start, rows_here, axis=0) for p in produced])
    new_cache = jnp.stack(
        [
            jnp.stack([lax.dynamic_slice_in_dim(h, start + rim, rows_here, axis=0) for h in hist])
            for hist in (first_hist, second_hist)
        ]
    )
    produced = jnp.transpose(produced, (0, 2, 1, 3))
    new_cache = jnp.transpose(new_cache, (0, 1, 3, 2, 4))
    return (produced[None], new_cache[None])


def solution(mesh):
    in_specs = (
        P(None, None, "rows", None),
        P("phase", None, None, None, "rows", None),
        P("phase", None, None, None, None, None, None),
        P("phase", None, None),
        P("phase", None, None),
        P("phase", None, None),
    )
    out_specs = (P("phase", None, None, "rows", None), P("phase", None, None, None, "rows", None))
    return jax.shard_map(shards, mesh=mesh, in_specs=in_specs, out_specs=out_specs, check_vma=False)
```

```python
import jax
import jax.numpy as jnp
from jax import lax
from jax.sharding import PartitionSpec as P
from jax.experimental import pallas as pl
from jax.experimental.pallas import tpu as pltpu
import functools

GROUPS = 32
EPS = 1e-06
MAX_SPAN = 16


def span_devices(peers, rows_here):
    count = 1
    while count * 2 <= peers and peers % (count * 2) == 0 and count * 2 * rows_here <= MAX_SPAN:
        count *= 2
    return count


def gather_span(array, dim, span_count):
    if span_count == 1:
        return array
    peers = lax.axis_size("rows")
    if span_count == peers:
        return lax.all_gather(array, "rows", axis=dim, tiled=True)
    place = lax.axis_index("rows") % span_count
    pieces = [array]
    for shift in range(1, span_count):
        pairs = [
            (b * span_count + p, b * span_count + (p + shift) % span_count)
            for b in range(peers // span_count)
            for p in range(span_count)
        ]
        pieces.append(lax.ppermute(array, "rows", pairs))
    stacked = jnp.stack(pieces)
    order = (place - jnp.arange(span_count)) % span_count
    picked = jnp.take(stacked, order, axis=0)
    picked = jnp.moveaxis(picked, 0, dim)
    shape = list(array.shape)
    shape[dim] = shape[dim] * span_count
    return picked.reshape(shape)


def with_rim(array, dim, span_count):
    peers = lax.axis_size("rows")
    length = array.shape[dim]
    if span_count == peers:
        return array
    up = [(i, i + span_count) for i in range(peers - span_count)]
    down = [(j, i) for i, j in up]
    last = lax.slice_in_dim(array, length - 1, length, axis=dim)
    leading = lax.slice_in_dim(array, 0, 1, axis=dim)
    before = lax.ppermute(last, "rows", up)
    after = lax.ppermute(leading, "rows", down)
    return jnp.concatenate([before, array, after], axis=dim)


def pass_on(result, span_count):
    phase_count = lax.axis_size("phase")
    forward = [(s, s + 1) for s in range(phase_count - 1)]
    length = result.shape[0]
    if span_count % 2 or length % 2:
        return lax.ppermute(result, "phase", forward)
    peers = lax.axis_size("rows")
    half = length // 2
    core = lax.axis_index("rows") % 2
    mine = lax.dynamic_slice_in_dim(result, core * half, half, axis=0)
    got = lax.ppermute(mine, "phase", forward)
    other = lax.ppermute(got, "rows", [(i, i ^ 1) for i in range(peers)])
    return jnp.where(core == 0, jnp.concatenate([got, other]), jnp.concatenate([other, got]))


def arrange_taps(weight):
    outputs = weight.shape[3]
    channels = weight.shape[4]
    return jnp.transpose(weight, (2, 3, 0, 1, 4)).reshape(3 * outputs, 9 * channels)


def conv_rows(x0, x1, x2, taps, bias, res, out, rows_out, padded):
    outputs = out.shape[1]
    channels = x0.shape[1]
    columns = x0.shape[2]
    pair = 4 if rows_out % 4 == 0 else (2 if rows_out % 2 == 0 else 1)
    lanes = pair * columns
    lane = lax.broadcasted_iota(jnp.int32, (outputs, lanes), 1) % columns
    frames = (x0, x1, x2)

    def column(r):
        if padded or 0 < r < rows_out - 1:
            base = r if padded else r - 1
            parts = [x[pl.ds(base, 3)] for x in frames]
            return jnp.concatenate(parts, axis=0).reshape(9 * channels, columns)
        zero = jnp.zeros((1, channels, columns), x0.dtype)
        parts = []
        for x in frames:
            for dy in range(3):
                q = r + dy - 1
                parts.append(zero if q < 0 or q >= rows_out else x[pl.ds(q, 1)])
        return jnp.concatenate(parts, axis=0).reshape(9 * channels, columns)

    for r in range(0, rows_out, pair):
        cols = [column(r + k) for k in range(pair)]
        rhs = cols[0] if pair == 1 else jnp.concatenate(cols, axis=1)
        acc = jnp.dot(taps[...], rhs, preferred_element_type=jnp.float32)
        left = pltpu.roll(acc[:outputs], 1, 1)
        right = pltpu.roll(acc[2 * outputs :], lanes - 1, 1)
        total = acc[outputs : 2 * outputs] + jnp.where(lane == 0, 0.0, left)
        total = total + jnp.where(lane == columns - 1, 0.0, right) + bias[...]
        for k in range(pair):
            piece = total[:, k * columns : (k + 1) * columns]
            if res is not None:
                piece = piece + res[r + k].astype(jnp.float32)
            out[r + k] = piece.astype(out.dtype)


def conv_body(x0, x1, x2, taps, bias, *rest, rows_out, with_res, padded):
    res = rest[0] if with_res else None
    conv_rows(x0, x1, x2, taps, bias, res, rest[-1], rows_out, padded)


def causal_conv(x0, x1, x2, taps, bias_vec, res, padded):
    rows_out = x0.shape[0] - 2 if padded else x0.shape[0]
    outputs = taps.shape[0] // 3
    args = [x0, x1, x2, taps, bias_vec.reshape(outputs, 1)]
    if res is not None:
        args.append(res)
    body = functools.partial(conv_body, rows_out=rows_out, with_res=res is not None, padded=padded)
    shape = jax.ShapeDtypeStruct((rows_out, outputs, x0.shape[2]), jnp.bfloat16)
    return pl.pallas_call(body, out_shape=shape)(*args)


def conv_span(x0, x1, x2, taps, bias, res, out, base, count):
    outputs = out.shape[1]
    channels = x0.shape[1]
    columns = x0.shape[2]
    pair = 4 if count % 4 == 0 else (2 if count % 2 == 0 else 1)
    lanes = pair * columns
    lane = lax.broadcasted_iota(jnp.int32, (outputs, lanes), 1) % columns

    def step(i, carry):
        r = base + i * pair
        cols = []
        for k in range(pair):
            parts = [x[pl.ds(r + k, 3)] for x in (x0, x1, x2)]
            cols.append(jnp.concatenate(parts, axis=0).reshape(9 * channels, columns))
        rhs = cols[0] if pair == 1 else jnp.concatenate(cols, axis=1)
        acc = jnp.dot(taps[...], rhs, preferred_element_type=jnp.float32)
        left = pltpu.roll(acc[:outputs], 1, 1)
        right = pltpu.roll(acc[2 * outputs :], lanes - 1, 1)
        total = acc[outputs : 2 * outputs] + jnp.where(lane == 0, 0.0, left)
        total = total + jnp.where(lane == columns - 1, 0.0, right) + bias[...]
        for k in range(pair):
            piece = total[:, k * columns : (k + 1) * columns]
            if res is not None:
                piece = piece + res[r + k].astype(jnp.float32)
            out[i * pair + k] = piece.astype(out.dtype)
        return carry

    lax.fori_loop(0, count // pair, step, 0)


def fused_body(flags, caches, a_p, a_pp, frames, src_b, src_c, taps, bias, member, gain, shift, *rest, kind):
    rest = list(rest)
    own = rest.pop(0) if kind != "first" else None
    if kind == "tail":
        out, x0, x1, rawbuf, sems = rest
        act = own
    else:
        out, act, x0, x1, rawbuf, sems = rest
    span, channels, columns = rawbuf.shape
    half = span // 2
    first, second, mode, core = flags[0], flags[1], flags[2], flags[6]
    c0, c1 = caches.at[flags[4]], caches.at[flags[5]]
    whole = frames.at[flags[3]]
    top, bottom = rawbuf.at[pl.ds(0, half)], rawbuf.at[pl.ds(half, half)]
    inner0, inner1 = x0.at[pl.ds(1, span)], x1.at[pl.ds(1, span)]

    def inner(x):
        return x.at[pl.ds(1, span)]

    def begin(pairs, base):
        for i, (a, b) in enumerate(pairs):
            pltpu.make_async_copy(a, b, sems.at[base + i]).start()

    def finish(pairs, base):
        for i, (a, b) in enumerate(pairs):
            pltpu.make_async_copy(a, b, sems.at[base + i]).wait()

    @pl.when(mode == 0)
    def _():
        begin([(whole.at[pl.ds(0, half)], top), (whole.at[pl.ds(half, half)], bottom)], 0)

    @pl.when(mode == 1)
    def _():
        begin([(src_b, top), (src_c, bottom)], 0)

    @pl.when(mode == 2)
    def _():
        begin([(src_c, top), (src_b, bottom)], 0)

    @pl.when(first == 1)
    def _():
        begin([(c0, inner0), (c1, inner1)], 2)

    @pl.when(jnp.logical_and(first == 0, second == 1))
    def _():
        begin([(c1, inner0), (inner(a_p), inner1)], 2)

    @pl.when(jnp.logical_and(first == 0, second == 0))
    def _():
        begin([(inner(a_pp), inner0), (inner(a_p), inner1)], 2)

    zero = jnp.zeros((channels, columns), x0.dtype)
    for x in (x0, x1):
        x[0] = zero
        x[span + 1] = zero
    source_copies = [(src_b, top), (src_c, bottom)]
    history_copies = [(inner(a_pp), inner0), (inner(a_p), inner1)]

    if kind != "tail":
        if kind == "first":
            finish(source_copies, 0)
            raw = rawbuf
        else:
            raw = own
        count = float(span * columns * (channels // GROUPS))

        def group_total(acc):
            spread = jnp.dot(member[...], acc, precision=lax.Precision.HIGHEST, preferred_element_type=jnp.float32)
            return jnp.sum(spread, axis=1, keepdims=True)

        acc = raw[0].astype(jnp.float32)
        for r in range(1, span):
            acc = acc + raw[r].astype(jnp.float32)
        average = group_total(acc) / count
        acc = jnp.square(raw[0].astype(jnp.float32) - average)
        for r in range(1, span):
            acc = acc + jnp.square(raw[r].astype(jnp.float32) - average)
        inverse = lax.rsqrt(group_total(acc) / count + EPS)
        act[0] = zero
        act[span + 1] = zero
        for r in range(span):
            value = (raw[r].astype(jnp.float32) - average) * inverse
            value = value * gain[...] + shift[...]
            act[r + 1] = (value / (1.0 + jnp.exp(-value))).astype(act.dtype)

    finish(history_copies, 2)
    if kind == "first":
        conv_span(x0, x1, act, taps, bias, None, out, 0, span)
    else:
        finish(source_copies, 0)
        base = core * half if kind == "lead" else (1 - core) * half
        conv_span(x0, x1, act, taps, bias, rawbuf, out, base, half)


def fused_conv(flags, caches, cache_at, recent, frames, frame_at, halves, taps, bias_vec, norm, kind, own=None):
    span, channels, columns = caches.shape[1:]
    outputs = taps.shape[0] // 3
    group_of = jnp.arange(channels) // (channels // GROUPS)
    member = (group_of[:, None] == group_of[None, :]).astype(jnp.float32)
    vmem = pl.BlockSpec(memory_space=pltpu.VMEM)
    anywhere = pl.BlockSpec(memory_space=pl.ANY)
    flags = jnp.concatenate([flags[:3], jnp.array([frame_at, cache_at[0], cache_at[1]], jnp.int32), flags[3:]])
    args = [flags, caches, recent[0], recent[1], frames, halves[0], halves[1]]
    args += [taps, bias_vec.reshape(outputs, 1), member]
    args += [v.reshape(-1, 1).astype(jnp.float32) for v in norm]
    specs = [pl.BlockSpec(memory_space=pltpu.SMEM)] + [anywhere] * 6 + [vmem] * 5
    if own is not None:
        args.append(own)
        specs.append(vmem)
    rows_out = span if kind == "first" else span // 2
    result = jax.ShapeDtypeStruct((rows_out, outputs, columns), jnp.bfloat16)
    padded = jax.ShapeDtypeStruct((span + 2, channels, columns), jnp.bfloat16)
    shapes = result if kind == "tail" else (result, padded)
    body = functools.partial(fused_body, kind=kind)
    return pl.pallas_call(
        body,
        out_shape=shapes,
        in_specs=specs,
        out_specs=vmem if kind == "tail" else (vmem, vmem),
        scratch_shapes=[
            pltpu.VMEM((span + 2, channels, columns), jnp.bfloat16),
            pltpu.VMEM((span + 2, channels, columns), jnp.bfloat16),
            pltpu.VMEM((span, channels, columns), jnp.bfloat16),
            pltpu.SemaphoreType.DMA((4,)),
        ],
    )(*args)


def block_sum(values, span_count):
    peers = lax.axis_size("rows")
    if span_count == peers:
        return values
    lead = (lax.axis_index("rows") % span_count == 0).astype(values.dtype)
    return lax.psum(values * lead, "rows")


def activate(source, gain_vec, shift_vec, cell_count, span_count):
    height, channels, columns = source.shape
    grouped = source.astype(jnp.float32).reshape(height, GROUPS, channels // GROUPS, columns)
    average = block_sum(jnp.sum(grouped, axis=(0, 2, 3)), span_count) / cell_count
    centred = grouped - average[None, :, None, None]
    spread = block_sum(jnp.sum(centred * centred, axis=(0, 2, 3)), span_count) / cell_count
    inverse = lax.rsqrt(spread + EPS)
    normed = (centred * inverse[None, :, None, None]).reshape(height, channels, columns)
    normed = normed * gain_vec[None, :, None] + shift_vec[None, :, None]
    return jax.nn.silu(normed).astype(jnp.bfloat16)


def run_frame(source, first_hist, second_hist, kernels, biases, gains, shifts, cell_count, span_count):
    padded = span_count != lax.axis_size("rows")
    first_in = with_rim(activate(source, gains[0], shifts[0], cell_count, span_count), 0, span_count)
    hidden = causal_conv(first_hist[0], first_hist[1], first_in, kernels[0], biases[0], None, padded)
    second_in = with_rim(activate(hidden, gains[1], shifts[1], cell_count, span_count), 0, span_count)
    result = causal_conv(second_hist[0], second_hist[1], second_in, kernels[1], biases[1], source, padded)
    return (result, (first_hist[1], first_in), (second_hist[1], second_in))


def shards_whole(frames, causal_cache, conv_weight, conv_bias, norm_gain, norm_shift):
    phase_no = lax.axis_index("phase")
    phase_count = lax.axis_size("phase")
    peers = lax.axis_size("rows")
    frame_count, channels, rows_here, columns = frames.shape
    span = rows_here * peers
    half = span // 2
    core = lax.axis_index("rows") % 2
    start = lax.axis_index("rows") * rows_here
    forward = [(s, s + 1) for s in range(phase_count - 1)]
    frames_t = jnp.transpose(frames, (0, 2, 1, 3))
    cache_t = jnp.transpose(causal_cache[0], (0, 1, 3, 2, 4))
    early = lax.all_gather(jnp.stack([frames_t[0], cache_t[0, 0], cache_t[0, 1]]), "rows", axis=1, tiled=True)
    late = lax.all_gather(
        jnp.stack([cache_t[1, 0], cache_t[1, 1]] + list(frames_t[1:])), "rows", axis=1, tiled=True
    )
    frame_of = [(early, 0)] + [(late, 2 + f) for f in range(frame_count - 1)]
    cache_of = ((early, (1, 2)), (late, (0, 1)))
    taps = (arrange_taps(conv_weight[0, 0]), arrange_taps(conv_weight[0, 1]))

    def own_rows(x, rim=0):
        return lax.dynamic_slice_in_dim(x, start + rim, rows_here, axis=0)

    got = other = jnp.zeros((half, channels, columns), jnp.bfloat16)
    acts = ([], [])
    blank = jnp.zeros((rows_here, channels, columns), jnp.bfloat16)
    blank_frame = jnp.zeros((span + 2, channels, columns), jnp.bfloat16)
    produced = [blank] * frame_count
    kept = [[blank, blank], [blank, blank]]
    mode = jnp.where(phase_no == 0, 0, 1 + core)
    tick_count = frame_count + phase_count - 1
    for tick_no in range(tick_count):
        frame_no = tick_no - phase_no
        flags = jnp.stack([frame_no == 0, frame_no == 1, mode, core]).astype(jnp.int32)
        frame_stack, frame_at = frame_of[min(tick_no, frame_count - 1)]
        recents = []
        for j in range(2):
            a_p = acts[j][-1] if acts[j] else blank_frame
            a_pp = acts[j][-2] if len(acts[j]) > 1 else blank_frame
            recents.append((a_p, a_pp))
        common = (frame_stack, frame_at, (got, other))
        hidden, first_in = fused_conv(
            flags, cache_of[0][0], cache_of[0][1], recents[0], *common,
            taps[0], conv_bias[0, 0], (norm_gain[0, 0], norm_shift[0, 0]), "first",
        )
        second = (flags, cache_of[1][0], cache_of[1][1], recents[1], *common, taps[1], conv_bias[0, 1])
        lead, second_in = fused_conv(*second, (norm_gain[0, 1], norm_shift[0, 1]), "lead", hidden)
        tail = fused_conv(*second, (norm_gain[0, 1], norm_shift[0, 1]), "tail", second_in)
        if tick_no + 1 < tick_count:
            got = lax.ppermute(lead, "phase", forward)
            got, tail = lax.optimization_barrier((got, tail))
            other = lax.ppermute(got, "rows", [(i, i ^ 1) for i in range(peers)])
        last = frame_no == frame_count - 1
        for j, a in enumerate((first_in, second_in)):
            stack, (_, k1) = cache_of[j]
            newer = jnp.where(frame_no == 0, own_rows(stack[k1]), own_rows(recents[j][0], 1))
            kept[j] = [jnp.where(last, newer, kept[j][0]), jnp.where(last, own_rows(a, 1), kept[j][1])]
            acts[j].append(a)
        mine = lax.dynamic_slice_in_dim(lead, start - core * half, rows_here, axis=0)
        theirs = lax.dynamic_slice_in_dim(tail, start - (1 - core) * half, rows_here, axis=0)
        result_rows = jnp.where(start // half == core, mine, theirs)
        for f in range(frame_count):
            if 0 <= tick_no - f < phase_count:
                produced[f] = jnp.where(frame_no == f, result_rows, produced[f])
    produced = jnp.transpose(jnp.stack(produced), (0, 2, 1, 3))
    new_cache = jnp.transpose(jnp.stack([jnp.stack(k) for k in kept]), (0, 1, 3, 2, 4))
    return (produced[None], new_cache[None])


def shards(frames, causal_cache, conv_weight, conv_bias, norm_gain, norm_shift):
    peers = lax.axis_size("rows")
    rows_here = frames.shape[2]
    if span_devices(peers, rows_here) == peers and (rows_here * peers) % 2 == 0:
        return shards_whole(frames, causal_cache, conv_weight, conv_bias, norm_gain, norm_shift)
    return shards_split(frames, causal_cache, conv_weight, conv_bias, norm_gain, norm_shift)


def shards_split(frames, causal_cache, conv_weight, conv_bias, norm_gain, norm_shift):
    phase_no = lax.axis_index("phase")
    phase_count = lax.axis_size("phase")
    peers = lax.axis_size("rows")
    frame_count = frames.shape[0]
    channels = frames.shape[1]
    rows_here = frames.shape[2]
    columns = frames.shape[3]
    span_count = span_devices(peers, rows_here)
    span = rows_here * span_count
    cell_count = float(channels // GROUPS * rows_here * peers * columns)
    padded = span_count != peers
    frames_t = jnp.transpose(frames, (0, 2, 1, 3))
    cache_t = jnp.transpose(causal_cache[0], (0, 1, 3, 2, 4))
    early = gather_span(jnp.stack([frames_t[0], cache_t[0, 0], cache_t[0, 1]]), 1, span_count)
    late = gather_span(jnp.stack([cache_t[1, 0], cache_t[1, 1]] + list(frames_t[1:])), 1, span_count)
    frames_span = [early[0]] + [late[2 + f] for f in range(frame_count - 1)]
    first_hist = tuple(with_rim(early[1 + k], 0, span_count) for k in range(2))
    second_hist = tuple(with_rim(late[k], 0, span_count) for k in range(2))
    local_taps = (arrange_taps(conv_weight[0, 0]), arrange_taps(conv_weight[0, 1]))
    incoming = jnp.zeros_like(frames_span[0])
    produced = [jnp.zeros_like(frames_span[0]) for _ in range(frame_count)]
    tick_count = frame_count + phase_count - 1
    for tick_no in range(tick_count):
        frame_no = tick_no - phase_no
        active_now = jnp.logical_and(frame_no >= 0, frame_no < frame_count)
        source = jnp.where(phase_no == 0, frames_span[min(tick_no, frame_count - 1)], incoming)
        result, first_next, second_next = run_frame(
            source, first_hist, second_hist, local_taps, conv_bias[0], norm_gain[0], norm_shift[0],
            cell_count, span_count,
        )
        first_hist = tuple(jnp.where(active_now, a, b) for a, b in zip(first_next, first_hist))
        second_hist = tuple(jnp.where(active_now, a, b) for a, b in zip(second_next, second_hist))
        for f in range(frame_count):
            if 0 <= tick_no - f < phase_count:
                produced[f] = jnp.where(frame_no == f, result, produced[f])
        if tick_no + 1 < tick_count:
            incoming = pass_on(result, span_count)
    start = (lax.axis_index("rows") % span_count) * rows_here
    rim = 1 if padded else 0
    produced = jnp.stack([lax.dynamic_slice_in_dim(p, start, rows_here, axis=0) for p in produced])
    new_cache = jnp.stack(
        [
            jnp.stack([lax.dynamic_slice_in_dim(h, start + rim, rows_here, axis=0) for h in hist])
            for hist in (first_hist, second_hist)
        ]
    )
    produced = jnp.transpose(produced, (0, 2, 1, 3))
    new_cache = jnp.transpose(new_cache, (0, 1, 3, 2, 4))
    return (produced[None], new_cache[None])


def solution(mesh):
    in_specs = (
        P(None, None, "rows", None),
        P("phase", None, None, None, "rows", None),
        P("phase", None, None, None, None, None, None),
        P("phase", None, None),
        P("phase", None, None),
        P("phase", None, None),
    )
    out_specs = (P("phase", None, None, "rows", None), P("phase", None, None, None, "rows", None))
    return jax.shard_map(shards, mesh=mesh, in_specs=in_specs, out_specs=out_specs, check_vma=False)
```

```python
import jax
import jax.numpy as jnp
from jax import lax
from jax.sharding import PartitionSpec as P
from jax.experimental import pallas as pl
from jax.experimental.pallas import tpu as pltpu
import functools

GROUPS = 32
EPS = 1e-06
MAX_SPAN = 16


def span_devices(peers, rows_here):
    count = 1
    while count * 2 <= peers and peers % (count * 2) == 0 and count * 2 * rows_here <= MAX_SPAN:
        count *= 2
    return count


def gather_span(array, dim, span_count):
    if span_count == 1:
        return array
    peers = lax.axis_size("rows")
    if span_count == peers:
        return lax.all_gather(array, "rows", axis=dim, tiled=True)
    place = lax.axis_index("rows") % span_count
    pieces = [array]
    for shift in range(1, span_count):
        pairs = [
            (b * span_count + p, b * span_count + (p + shift) % span_count)
            for b in range(peers // span_count)
            for p in range(span_count)
        ]
        pieces.append(lax.ppermute(array, "rows", pairs))
    stacked = jnp.stack(pieces)
    order = (place - jnp.arange(span_count)) % span_count
    picked = jnp.take(stacked, order, axis=0)
    picked = jnp.moveaxis(picked, 0, dim)
    shape = list(array.shape)
    shape[dim] = shape[dim] * span_count
    return picked.reshape(shape)


def with_rim(array, dim, span_count):
    peers = lax.axis_size("rows")
    length = array.shape[dim]
    if span_count == peers:
        return array
    up = [(i, i + span_count) for i in range(peers - span_count)]
    down = [(j, i) for i, j in up]
    last = lax.slice_in_dim(array, length - 1, length, axis=dim)
    leading = lax.slice_in_dim(array, 0, 1, axis=dim)
    before = lax.ppermute(last, "rows", up)
    after = lax.ppermute(leading, "rows", down)
    return jnp.concatenate([before, array, after], axis=dim)


def pass_on(result, span_count):
    phase_count = lax.axis_size("phase")
    forward = [(s, s + 1) for s in range(phase_count - 1)]
    length = result.shape[0]
    if span_count % 2 or length % 2:
        return lax.ppermute(result, "phase", forward)
    peers = lax.axis_size("rows")
    half = length // 2
    core = lax.axis_index("rows") % 2
    mine = lax.dynamic_slice_in_dim(result, core * half, half, axis=0)
    got = lax.ppermute(mine, "phase", forward)
    other = lax.ppermute(got, "rows", [(i, i ^ 1) for i in range(peers)])
    return jnp.where(core == 0, jnp.concatenate([got, other]), jnp.concatenate([other, got]))


def arrange_taps(weight):
    outputs = weight.shape[3]
    channels = weight.shape[4]
    return jnp.transpose(weight, (2, 3, 0, 1, 4)).reshape(3 * outputs, 9 * channels)


def conv_rows(x0, x1, x2, taps, bias, res, out, rows_out, padded):
    outputs = out.shape[1]
    channels = x0.shape[1]
    columns = x0.shape[2]
    pair = 4 if rows_out % 4 == 0 else (2 if rows_out % 2 == 0 else 1)
    lanes = pair * columns
    lane = lax.broadcasted_iota(jnp.int32, (outputs, lanes), 1) % columns
    frames = (x0, x1, x2)

    def column(r):
        if padded or 0 < r < rows_out - 1:
            base = r if padded else r - 1
            parts = [x[pl.ds(base, 3)] for x in frames]
            return jnp.concatenate(parts, axis=0).reshape(9 * channels, columns)
        zero = jnp.zeros((1, channels, columns), x0.dtype)
        parts = []
        for x in frames:
            for dy in range(3):
                q = r + dy - 1
                parts.append(zero if q < 0 or q >= rows_out else x[pl.ds(q, 1)])
        return jnp.concatenate(parts, axis=0).reshape(9 * channels, columns)

    for r in range(0, rows_out, pair):
        cols = [column(r + k) for k in range(pair)]
        rhs = cols[0] if pair == 1 else jnp.concatenate(cols, axis=1)
        acc = jnp.dot(taps[...], rhs, preferred_element_type=jnp.float32)
        left = pltpu.roll(acc[:outputs], 1, 1)
        right = pltpu.roll(acc[2 * outputs :], lanes - 1, 1)
        total = acc[outputs : 2 * outputs] + jnp.where(lane == 0, 0.0, left)
        total = total + jnp.where(lane == columns - 1, 0.0, right) + bias[...]
        for k in range(pair):
            piece = total[:, k * columns : (k + 1) * columns]
            if res is not None:
                piece = piece + res[r + k].astype(jnp.float32)
            out[r + k] = piece.astype(out.dtype)


def conv_body(x0, x1, x2, taps, bias, *rest, rows_out, with_res, padded):
    res = rest[0] if with_res else None
    conv_rows(x0, x1, x2, taps, bias, res, rest[-1], rows_out, padded)


def causal_conv(x0, x1, x2, taps, bias_vec, res, padded):
    rows_out = x0.shape[0] - 2 if padded else x0.shape[0]
    outputs = taps.shape[0] // 3
    args = [x0, x1, x2, taps, bias_vec.reshape(outputs, 1)]
    if res is not None:
        args.append(res)
    body = functools.partial(conv_body, rows_out=rows_out, with_res=res is not None, padded=padded)
    shape = jax.ShapeDtypeStruct((rows_out, outputs, x0.shape[2]), jnp.bfloat16)
    return pl.pallas_call(body, out_shape=shape)(*args)


def conv_span(x0, x1, x2, taps, bias, res, out, base, count):
    outputs = out.shape[1]
    channels = x0.shape[1]
    columns = x0.shape[2]
    pair = 4 if count % 4 == 0 else (2 if count % 2 == 0 else 1)
    lanes = pair * columns
    lane = lax.broadcasted_iota(jnp.int32, (outputs, lanes), 1) % columns

    def step(i, carry):
        r = base + i * pair
        cols = []
        for k in range(pair):
            parts = [x[pl.ds(r + k, 3)] for x in (x0, x1, x2)]
            cols.append(jnp.concatenate(parts, axis=0).reshape(9 * channels, columns))
        rhs = cols[0] if pair == 1 else jnp.concatenate(cols, axis=1)
        acc = jnp.dot(taps[...], rhs, preferred_element_type=jnp.float32)
        left = pltpu.roll(acc[:outputs], 1, 1)
        right = pltpu.roll(acc[2 * outputs :], lanes - 1, 1)
        total = acc[outputs : 2 * outputs] + jnp.where(lane == 0, 0.0, left)
        total = total + jnp.where(lane == columns - 1, 0.0, right) + bias[...]
        for k in range(pair):
            piece = total[:, k * columns : (k + 1) * columns]
            if res is not None:
                piece = piece + res[r + k].astype(jnp.float32)
            out[i * pair + k] = piece.astype(out.dtype)
        return carry

    lax.fori_loop(0, count // pair, step, 0)


def fused_body(flags, caches, a_p, a_pp, frames, src_b, src_c, taps, bias, member, gain, shift, *rest,
               kind, tick, frame_at, cache_at):
    rest = list(rest)
    own = rest.pop(0) if kind != "first" else None
    if kind == "tail":
        out, x0, x1, rawbuf, sems = rest
        act = own
    else:
        out, act, x0, x1, rawbuf, sems = rest
    span, channels, columns = rawbuf.shape
    half = span // 2
    first, second, mode, core = flags[tick, 0], flags[tick, 1], flags[tick, 2], flags[tick, 3]
    c0, c1 = caches.at[cache_at[0]], caches.at[cache_at[1]]
    whole = frames.at[frame_at]
    top, bottom = rawbuf.at[pl.ds(0, half)], rawbuf.at[pl.ds(half, half)]
    inner0, inner1 = x0.at[pl.ds(1, span)], x1.at[pl.ds(1, span)]

    def inner(x):
        return x.at[pl.ds(1, span)]

    def begin(pairs, base):
        for i, (a, b) in enumerate(pairs):
            pltpu.make_async_copy(a, b, sems.at[base + i]).start()

    def finish(pairs, base):
        for i, (a, b) in enumerate(pairs):
            pltpu.make_async_copy(a, b, sems.at[base + i]).wait()

    @pl.when(mode == 0)
    def _():
        begin([(whole.at[pl.ds(0, half)], top), (whole.at[pl.ds(half, half)], bottom)], 0)

    @pl.when(mode == 1)
    def _():
        begin([(src_b, top), (src_c, bottom)], 0)

    @pl.when(mode == 2)
    def _():
        begin([(src_c, top), (src_b, bottom)], 0)

    @pl.when(first == 1)
    def _():
        begin([(c0, inner0), (c1, inner1)], 2)

    @pl.when(jnp.logical_and(first == 0, second == 1))
    def _():
        begin([(c1, inner0), (inner(a_p), inner1)], 2)

    @pl.when(jnp.logical_and(first == 0, second == 0))
    def _():
        begin([(inner(a_pp), inner0), (inner(a_p), inner1)], 2)

    zero = jnp.zeros((channels, columns), x0.dtype)
    for x in (x0, x1):
        x[0] = zero
        x[span + 1] = zero
    source_copies = [(src_b, top), (src_c, bottom)]
    history_copies = [(inner(a_pp), inner0), (inner(a_p), inner1)]

    if kind != "tail":
        if kind == "first":
            finish(source_copies, 0)
            raw = rawbuf
        else:
            raw = own
        count = float(span * columns * (channels // GROUPS))

        def group_total(acc):
            spread = jnp.dot(member[...], acc, precision=lax.Precision.HIGHEST, preferred_element_type=jnp.float32)
            return jnp.sum(spread, axis=1, keepdims=True)

        acc = raw[0].astype(jnp.float32)
        for r in range(1, span):
            acc = acc + raw[r].astype(jnp.float32)
        average = group_total(acc) / count
        acc = jnp.square(raw[0].astype(jnp.float32) - average)
        for r in range(1, span):
            acc = acc + jnp.square(raw[r].astype(jnp.float32) - average)
        inverse = lax.rsqrt(group_total(acc) / count + EPS)
        act[0] = zero
        act[span + 1] = zero
        for r in range(span):
            value = (raw[r].astype(jnp.float32) - average) * inverse
            value = value * gain[...] + shift[...]
            act[r + 1] = (value / (1.0 + jnp.exp(-value))).astype(act.dtype)

    finish(history_copies, 2)
    if kind == "first":
        conv_span(x0, x1, act, taps, bias, None, out, 0, span)
    else:
        finish(source_copies, 0)
        base = core * half if kind == "lead" else (1 - core) * half
        conv_span(x0, x1, act, taps, bias, rawbuf, out, base, half)


def fused_conv(flags, tick, caches, cache_at, recent, frames, frame_at, halves, taps, bias_vec, norm, kind, own=None):
    span, channels, columns = caches.shape[1:]
    outputs = taps.shape[0] // 3
    group_of = jnp.arange(channels) // (channels // GROUPS)
    member = (group_of[:, None] == group_of[None, :]).astype(jnp.float32)
    vmem = pl.BlockSpec(memory_space=pltpu.VMEM)
    anywhere = pl.BlockSpec(memory_space=pl.ANY)
    args = [flags, caches, recent[0], recent[1], frames, halves[0], halves[1]]
    args += [taps, bias_vec.reshape(outputs, 1), member]
    args += [v.reshape(-1, 1).astype(jnp.float32) for v in norm]
    specs = [pl.BlockSpec(memory_space=pltpu.SMEM)] + [anywhere] * 6 + [vmem] * 5
    if own is not None:
        args.append(own)
        specs.append(vmem)
    rows_out = span if kind == "first" else span // 2
    result = jax.ShapeDtypeStruct((rows_out, outputs, columns), jnp.bfloat16)
    padded = jax.ShapeDtypeStruct((span + 2, channels, columns), jnp.bfloat16)
    shapes = result if kind == "tail" else (result, padded)
    body = functools.partial(
        fused_body, kind=kind, tick=tick, frame_at=frame_at, cache_at=tuple(cache_at)
    )
    return pl.pallas_call(
        body,
        out_shape=shapes,
        in_specs=specs,
        out_specs=vmem if kind == "tail" else (vmem, vmem),
        scratch_shapes=[
            pltpu.VMEM((span + 2, channels, columns), jnp.bfloat16),
            pltpu.VMEM((span + 2, channels, columns), jnp.bfloat16),
            pltpu.VMEM((span, channels, columns), jnp.bfloat16),
            pltpu.SemaphoreType.DMA((4,)),
        ],
    )(*args)


def block_sum(values, span_count):
    peers = lax.axis_size("rows")
    if span_count == peers:
        return values
    lead = (lax.axis_index("rows") % span_count == 0).astype(values.dtype)
    return lax.psum(values * lead, "rows")


def activate(source, gain_vec, shift_vec, cell_count, span_count):
    height, channels, columns = source.shape
    grouped = source.astype(jnp.float32).reshape(height, GROUPS, channels // GROUPS, columns)
    average = block_sum(jnp.sum(grouped, axis=(0, 2, 3)), span_count) / cell_count
    centred = grouped - average[None, :, None, None]
    spread = block_sum(jnp.sum(centred * centred, axis=(0, 2, 3)), span_count) / cell_count
    inverse = lax.rsqrt(spread + EPS)
    normed = (centred * inverse[None, :, None, None]).reshape(height, channels, columns)
    normed = normed * gain_vec[None, :, None] + shift_vec[None, :, None]
    return jax.nn.silu(normed).astype(jnp.bfloat16)


def run_frame(source, first_hist, second_hist, kernels, biases, gains, shifts, cell_count, span_count):
    padded = span_count != lax.axis_size("rows")
    first_in = with_rim(activate(source, gains[0], shifts[0], cell_count, span_count), 0, span_count)
    hidden = causal_conv(first_hist[0], first_hist[1], first_in, kernels[0], biases[0], None, padded)
    second_in = with_rim(activate(hidden, gains[1], shifts[1], cell_count, span_count), 0, span_count)
    result = causal_conv(second_hist[0], second_hist[1], second_in, kernels[1], biases[1], source, padded)
    return (result, (first_hist[1], first_in), (second_hist[1], second_in))


def shards_whole(frames, causal_cache, conv_weight, conv_bias, norm_gain, norm_shift):
    phase_no = lax.axis_index("phase")
    phase_count = lax.axis_size("phase")
    peers = lax.axis_size("rows")
    frame_count, channels, rows_here, columns = frames.shape
    span = rows_here * peers
    half = span // 2
    core = lax.axis_index("rows") % 2
    start = lax.axis_index("rows") * rows_here
    forward = [(s, s + 1) for s in range(phase_count - 1)]
    frames_t = jnp.transpose(frames, (0, 2, 1, 3))
    cache_t = jnp.transpose(causal_cache[0], (0, 1, 3, 2, 4))
    early = lax.all_gather(jnp.stack([frames_t[0], cache_t[0, 0], cache_t[0, 1]]), "rows", axis=1, tiled=True)
    second_cache = lax.all_gather(cache_t[1], "rows", axis=1, tiled=True)
    later = list(frames_t[1:])
    if len(later) == 1:
        later = later * 2
    later = lax.all_gather(jnp.stack(later), "rows", axis=1, tiled=True) if later else early
    frame_of = [(early, 0)] + [(later, f) for f in range(frame_count - 1)]
    cache_of = ((early, (1, 2)), (second_cache, (0, 1)))
    taps = (arrange_taps(conv_weight[0, 0]), arrange_taps(conv_weight[0, 1]))

    def own_rows(x, rim=0):
        return lax.dynamic_slice_in_dim(x, start + rim, rows_here, axis=0)

    got = other = jnp.zeros((half, channels, columns), jnp.bfloat16)
    acts = ([], [])
    blank = jnp.zeros((rows_here, channels, columns), jnp.bfloat16)
    blank_frame = jnp.zeros((span + 2, channels, columns), jnp.bfloat16)
    produced = [blank] * frame_count
    kept = [[blank, blank], [blank, blank]]
    mode = jnp.where(phase_no == 0, 0, 1 + core)
    tick_count = frame_count + phase_count - 1
    frame_nos = jnp.arange(tick_count) - phase_no
    flags = jnp.stack(
        [frame_nos == 0, frame_nos == 1, jnp.full((tick_count,), mode), jnp.full((tick_count,), core)], axis=1
    ).astype(jnp.int32)
    for tick_no in range(tick_count):
        frame_no = tick_no - phase_no
        frame_stack, frame_at = frame_of[min(tick_no, frame_count - 1)]
        recents = []
        for j in range(2):
            a_p = acts[j][-1] if acts[j] else blank_frame
            a_pp = acts[j][-2] if len(acts[j]) > 1 else blank_frame
            recents.append((a_p, a_pp))
        common = (frame_stack, frame_at, (got, other))
        hidden, first_in = fused_conv(
            flags, tick_no, cache_of[0][0], cache_of[0][1], recents[0], *common,
            taps[0], conv_bias[0, 0], (norm_gain[0, 0], norm_shift[0, 0]), "first",
        )
        second = (flags, tick_no, cache_of[1][0], cache_of[1][1], recents[1], *common, taps[1], conv_bias[0, 1])
        lead, second_in = fused_conv(*second, (norm_gain[0, 1], norm_shift[0, 1]), "lead", hidden)
        tail = fused_conv(*second, (norm_gain[0, 1], norm_shift[0, 1]), "tail", second_in)
        if tick_no + 1 < tick_count:
            got = lax.ppermute(lead, "phase", forward)
            got, tail = lax.optimization_barrier((got, tail))
            other = lax.ppermute(got, "rows", [(i, i ^ 1) for i in range(peers)])
        last = frame_no == frame_count - 1
        for j, a in enumerate((first_in, second_in)):
            stack, (_, k1) = cache_of[j]
            newer = jnp.where(frame_no == 0, own_rows(stack[k1]), own_rows(recents[j][0], 1))
            kept[j] = [jnp.where(last, newer, kept[j][0]), jnp.where(last, own_rows(a, 1), kept[j][1])]
            acts[j].append(a)
        mine = lax.dynamic_slice_in_dim(lead, start - core * half, rows_here, axis=0)
        theirs = lax.dynamic_slice_in_dim(tail, start - (1 - core) * half, rows_here, axis=0)
        result_rows = jnp.where(start // half == core, mine, theirs)
        for f in range(frame_count):
            if 0 <= tick_no - f < phase_count:
                produced[f] = jnp.where(frame_no == f, result_rows, produced[f])
    produced = jnp.transpose(jnp.stack(produced), (0, 2, 1, 3))
    new_cache = jnp.transpose(jnp.stack([jnp.stack(k) for k in kept]), (0, 1, 3, 2, 4))
    return (produced[None], new_cache[None])


def shards(frames, causal_cache, conv_weight, conv_bias, norm_gain, norm_shift):
    peers = lax.axis_size("rows")
    rows_here = frames.shape[2]
    if span_devices(peers, rows_here) == peers and (rows_here * peers) % 2 == 0:
        return shards_whole(frames, causal_cache, conv_weight, conv_bias, norm_gain, norm_shift)
    return shards_split(frames, causal_cache, conv_weight, conv_bias, norm_gain, norm_shift)


def shards_split(frames, causal_cache, conv_weight, conv_bias, norm_gain, norm_shift):
    phase_no = lax.axis_index("phase")
    phase_count = lax.axis_size("phase")
    peers = lax.axis_size("rows")
    frame_count = frames.shape[0]
    channels = frames.shape[1]
    rows_here = frames.shape[2]
    columns = frames.shape[3]
    span_count = span_devices(peers, rows_here)
    span = rows_here * span_count
    cell_count = float(channels // GROUPS * rows_here * peers * columns)
    padded = span_count != peers
    frames_t = jnp.transpose(frames, (0, 2, 1, 3))
    cache_t = jnp.transpose(causal_cache[0], (0, 1, 3, 2, 4))
    early = gather_span(jnp.stack([frames_t[0], cache_t[0, 0], cache_t[0, 1]]), 1, span_count)
    late = gather_span(jnp.stack([cache_t[1, 0], cache_t[1, 1]] + list(frames_t[1:])), 1, span_count)
    frames_span = [early[0]] + [late[2 + f] for f in range(frame_count - 1)]
    first_hist = tuple(with_rim(early[1 + k], 0, span_count) for k in range(2))
    second_hist = tuple(with_rim(late[k], 0, span_count) for k in range(2))
    local_taps = (arrange_taps(conv_weight[0, 0]), arrange_taps(conv_weight[0, 1]))
    incoming = jnp.zeros_like(frames_span[0])
    produced = [jnp.zeros_like(frames_span[0]) for _ in range(frame_count)]
    tick_count = frame_count + phase_count - 1
    for tick_no in range(tick_count):
        frame_no = tick_no - phase_no
        active_now = jnp.logical_and(frame_no >= 0, frame_no < frame_count)
        source = jnp.where(phase_no == 0, frames_span[min(tick_no, frame_count - 1)], incoming)
        result, first_next, second_next = run_frame(
            source, first_hist, second_hist, local_taps, conv_bias[0], norm_gain[0], norm_shift[0],
            cell_count, span_count,
        )
        first_hist = tuple(jnp.where(active_now, a, b) for a, b in zip(first_next, first_hist))
        second_hist = tuple(jnp.where(active_now, a, b) for a, b in zip(second_next, second_hist))
        for f in range(frame_count):
            if 0 <= tick_no - f < phase_count:
                produced[f] = jnp.where(frame_no == f, result, produced[f])
        if tick_no + 1 < tick_count:
            incoming = pass_on(result, span_count)
    start = (lax.axis_index("rows") % span_count) * rows_here
    rim = 1 if padded else 0
    produced = jnp.stack([lax.dynamic_slice_in_dim(p, start, rows_here, axis=0) for p in produced])
    new_cache = jnp.stack(
        [
            jnp.stack([lax.dynamic_slice_in_dim(h, start + rim, rows_here, axis=0) for h in hist])
            for hist in (first_hist, second_hist)
        ]
    )
    produced = jnp.transpose(produced, (0, 2, 1, 3))
    new_cache = jnp.transpose(new_cache, (0, 1, 3, 2, 4))
    return (produced[None], new_cache[None])


def solution(mesh):
    in_specs = (
        P(None, None, "rows", None),
        P("phase", None, None, None, "rows", None),
        P("phase", None, None, None, None, None, None),
        P("phase", None, None),
        P("phase", None, None),
        P("phase", None, None),
    )
    out_specs = (P("phase", None, None, "rows", None), P("phase", None, None, None, "rows", None))
    return jax.shard_map(shards, mesh=mesh, in_specs=in_specs, out_specs=out_specs, check_vma=False)
```

```python
import jax
import jax.numpy as jnp
from jax import lax
from jax.sharding import PartitionSpec as P
from jax.experimental import pallas as pl
from jax.experimental.pallas import tpu as pltpu
import functools

GROUPS = 32
EPS = 1e-06
MAX_SPAN = 16


def span_devices(peers, rows_here):
    count = 1
    while count * 2 <= peers and peers % (count * 2) == 0 and count * 2 * rows_here <= MAX_SPAN:
        count *= 2
    return count


def gather_span(array, dim, span_count):
    if span_count == 1:
        return array
    peers = lax.axis_size("rows")
    if span_count == peers:
        return lax.all_gather(array, "rows", axis=dim, tiled=True)
    place = lax.axis_index("rows") % span_count
    pieces = [array]
    for shift in range(1, span_count):
        pairs = [
            (b * span_count + p, b * span_count + (p + shift) % span_count)
            for b in range(peers // span_count)
            for p in range(span_count)
        ]
        pieces.append(lax.ppermute(array, "rows", pairs))
    stacked = jnp.stack(pieces)
    order = (place - jnp.arange(span_count)) % span_count
    picked = jnp.take(stacked, order, axis=0)
    picked = jnp.moveaxis(picked, 0, dim)
    shape = list(array.shape)
    shape[dim] = shape[dim] * span_count
    return picked.reshape(shape)


def with_rim(array, dim, span_count):
    peers = lax.axis_size("rows")
    length = array.shape[dim]
    if span_count == peers:
        return array
    up = [(i, i + span_count) for i in range(peers - span_count)]
    down = [(j, i) for i, j in up]
    last = lax.slice_in_dim(array, length - 1, length, axis=dim)
    leading = lax.slice_in_dim(array, 0, 1, axis=dim)
    before = lax.ppermute(last, "rows", up)
    after = lax.ppermute(leading, "rows", down)
    return jnp.concatenate([before, array, after], axis=dim)


def pass_on(result, span_count):
    phase_count = lax.axis_size("phase")
    forward = [(s, s + 1) for s in range(phase_count - 1)]
    length = result.shape[0]
    if span_count % 2 or length % 2:
        return lax.ppermute(result, "phase", forward)
    peers = lax.axis_size("rows")
    half = length // 2
    core = lax.axis_index("rows") % 2
    mine = lax.dynamic_slice_in_dim(result, core * half, half, axis=0)
    got = lax.ppermute(mine, "phase", forward)
    other = lax.ppermute(got, "rows", [(i, i ^ 1) for i in range(peers)])
    return jnp.where(core == 0, jnp.concatenate([got, other]), jnp.concatenate([other, got]))


def arrange_taps(weight):
    outputs = weight.shape[3]
    channels = weight.shape[4]
    return jnp.transpose(weight, (2, 3, 0, 1, 4)).reshape(3 * outputs, 9 * channels)


def conv_rows(x0, x1, x2, taps, bias, res, out, rows_out, padded):
    outputs = out.shape[1]
    channels = x0.shape[1]
    columns = x0.shape[2]
    pair = 4 if rows_out % 4 == 0 else (2 if rows_out % 2 == 0 else 1)
    lanes = pair * columns
    lane = lax.broadcasted_iota(jnp.int32, (outputs, lanes), 1) % columns
    frames = (x0, x1, x2)

    def column(r):
        if padded or 0 < r < rows_out - 1:
            base = r if padded else r - 1
            parts = [x[pl.ds(base, 3)] for x in frames]
            return jnp.concatenate(parts, axis=0).reshape(9 * channels, columns)
        zero = jnp.zeros((1, channels, columns), x0.dtype)
        parts = []
        for x in frames:
            for dy in range(3):
                q = r + dy - 1
                parts.append(zero if q < 0 or q >= rows_out else x[pl.ds(q, 1)])
        return jnp.concatenate(parts, axis=0).reshape(9 * channels, columns)

    for r in range(0, rows_out, pair):
        cols = [column(r + k) for k in range(pair)]
        rhs = cols[0] if pair == 1 else jnp.concatenate(cols, axis=1)
        acc = jnp.dot(taps[...], rhs, preferred_element_type=jnp.float32)
        left = pltpu.roll(acc[:outputs], 1, 1)
        right = pltpu.roll(acc[2 * outputs :], lanes - 1, 1)
        total = acc[outputs : 2 * outputs] + jnp.where(lane == 0, 0.0, left)
        total = total + jnp.where(lane == columns - 1, 0.0, right) + bias[...]
        for k in range(pair):
            piece = total[:, k * columns : (k + 1) * columns]
            if res is not None:
                piece = piece + res[r + k].astype(jnp.float32)
            out[r + k] = piece.astype(out.dtype)


def conv_body(x0, x1, x2, taps, bias, *rest, rows_out, with_res, padded):
    res = rest[0] if with_res else None
    conv_rows(x0, x1, x2, taps, bias, res, rest[-1], rows_out, padded)


def causal_conv(x0, x1, x2, taps, bias_vec, res, padded):
    rows_out = x0.shape[0] - 2 if padded else x0.shape[0]
    outputs = taps.shape[0] // 3
    args = [x0, x1, x2, taps, bias_vec.reshape(outputs, 1)]
    if res is not None:
        args.append(res)
    body = functools.partial(conv_body, rows_out=rows_out, with_res=res is not None, padded=padded)
    shape = jax.ShapeDtypeStruct((rows_out, outputs, x0.shape[2]), jnp.bfloat16)
    return pl.pallas_call(body, out_shape=shape)(*args)


def conv_span(x0, x1, x2, taps, bias, res, out, base, count):
    outputs = out.shape[1]
    channels = x0.shape[1]
    columns = x0.shape[2]
    pair = 4 if count % 4 == 0 else (2 if count % 2 == 0 else 1)
    lanes = pair * columns
    lane = lax.broadcasted_iota(jnp.int32, (outputs, lanes), 1) % columns

    def step(i, carry):
        r = base + i * pair
        cols = []
        for k in range(pair):
            parts = [x[pl.ds(r + k, 3)] for x in (x0, x1, x2)]
            cols.append(jnp.concatenate(parts, axis=0).reshape(9 * channels, columns))
        rhs = cols[0] if pair == 1 else jnp.concatenate(cols, axis=1)
        acc = jnp.dot(taps[...], rhs, preferred_element_type=jnp.float32)
        left = pltpu.roll(acc[:outputs], 1, 1)
        right = pltpu.roll(acc[2 * outputs :], lanes - 1, 1)
        total = acc[outputs : 2 * outputs] + jnp.where(lane == 0, 0.0, left)
        total = total + jnp.where(lane == columns - 1, 0.0, right) + bias[...]
        for k in range(pair):
            piece = total[:, k * columns : (k + 1) * columns]
            if res is not None:
                piece = piece + res[r + k].astype(jnp.float32)
            out[i * pair + k] = piece.astype(out.dtype)
        return carry

    lax.fori_loop(0, count // pair, step, 0)


def fused_body(flags, caches, a_p, a_pp, frames, src_b, src_c, taps, bias, member, gain, shift, *rest,
               kind, tick, frame_at, cache_at):
    rest = list(rest)
    own = rest.pop(0) if kind != "first" else None
    if kind == "tail":
        out, x0, x1, rawbuf, sems = rest
        act = own
    else:
        out, act, x0, x1, rawbuf, sems = rest
    span, channels, columns = rawbuf.shape
    half = span // 2
    first, second, mode, core = flags[tick, 0], flags[tick, 1], flags[tick, 2], flags[tick, 3]
    c0, c1 = caches.at[cache_at[0]], caches.at[cache_at[1]]
    whole = frames.at[frame_at]
    top, bottom = rawbuf.at[pl.ds(0, half)], rawbuf.at[pl.ds(half, half)]
    inner0, inner1 = x0.at[pl.ds(1, span)], x1.at[pl.ds(1, span)]

    def inner(x):
        return x.at[pl.ds(1, span)]

    def begin(pairs, base):
        for i, (a, b) in enumerate(pairs):
            pltpu.make_async_copy(a, b, sems.at[base + i]).start()

    def finish(pairs, base):
        for i, (a, b) in enumerate(pairs):
            pltpu.make_async_copy(a, b, sems.at[base + i]).wait()

    @pl.when(mode == 0)
    def _():
        begin([(whole.at[pl.ds(0, half)], top), (whole.at[pl.ds(half, half)], bottom)], 0)

    @pl.when(mode == 1)
    def _():
        begin([(src_b, top), (src_c, bottom)], 0)

    @pl.when(mode == 2)
    def _():
        begin([(src_c, top), (src_b, bottom)], 0)

    @pl.when(first == 1)
    def _():
        begin([(c0, inner0), (c1, inner1)], 2)

    @pl.when(jnp.logical_and(first == 0, second == 1))
    def _():
        begin([(c1, inner0), (inner(a_p), inner1)], 2)

    @pl.when(jnp.logical_and(first == 0, second == 0))
    def _():
        begin([(inner(a_pp), inner0), (inner(a_p), inner1)], 2)

    zero = jnp.zeros((channels, columns), x0.dtype)
    for x in (x0, x1):
        x[0] = zero
        x[span + 1] = zero
    source_copies = [(src_b, top), (src_c, bottom)]
    history_copies = [(inner(a_pp), inner0), (inner(a_p), inner1)]

    if kind != "tail":
        if kind == "first":
            finish(source_copies, 0)
            raw = rawbuf
        else:
            raw = own
        count = float(span * columns * (channels // GROUPS))

        def group_total(acc):
            spread = jnp.dot(member[...], acc, precision=lax.Precision.HIGHEST, preferred_element_type=jnp.float32)
            return jnp.sum(spread, axis=1, keepdims=True)

        acc = raw[0].astype(jnp.float32)
        for r in range(1, span):
            acc = acc + raw[r].astype(jnp.float32)
        average = group_total(acc) / count
        acc = jnp.square(raw[0].astype(jnp.float32) - average)
        for r in range(1, span):
            acc = acc + jnp.square(raw[r].astype(jnp.float32) - average)
        inverse = lax.rsqrt(group_total(acc) / count + EPS)
        act[0] = zero
        act[span + 1] = zero
        for r in range(span):
            value = (raw[r].astype(jnp.float32) - average) * inverse
            value = value * gain[...] + shift[...]
            act[r + 1] = (value / (1.0 + jnp.exp(-value))).astype(act.dtype)

    finish(history_copies, 2)
    if kind == "first":
        conv_span(x0, x1, act, taps, bias, None, out, 0, span)
    elif kind == "all":
        finish(source_copies, 0)
        conv_span(x0, x1, act, taps, bias, rawbuf, out, 0, span)
    else:
        finish(source_copies, 0)
        base = core * half if kind == "lead" else (1 - core) * half
        conv_span(x0, x1, act, taps, bias, rawbuf, out, base, half)


def fused_conv(flags, tick, caches, cache_at, recent, frames, frame_at, halves, taps, bias_vec, norm, kind, own=None):
    span, channels, columns = caches.shape[1:]
    outputs = taps.shape[0] // 3
    group_of = jnp.arange(channels) // (channels // GROUPS)
    member = (group_of[:, None] == group_of[None, :]).astype(jnp.float32)
    vmem = pl.BlockSpec(memory_space=pltpu.VMEM)
    anywhere = pl.BlockSpec(memory_space=pl.ANY)
    args = [flags, caches, recent[0], recent[1], frames, halves[0], halves[1]]
    args += [taps, bias_vec.reshape(outputs, 1), member]
    args += [v.reshape(-1, 1).astype(jnp.float32) for v in norm]
    specs = [pl.BlockSpec(memory_space=pltpu.SMEM)] + [anywhere] * 6 + [vmem] * 5
    if own is not None:
        args.append(own)
        specs.append(vmem)
    rows_out = span if kind in ("first", "all") else span // 2
    result = jax.ShapeDtypeStruct((rows_out, outputs, columns), jnp.bfloat16)
    padded = jax.ShapeDtypeStruct((span + 2, channels, columns), jnp.bfloat16)
    shapes = result if kind == "tail" else (result, padded)
    body = functools.partial(
        fused_body, kind=kind, tick=tick, frame_at=frame_at, cache_at=tuple(cache_at)
    )
    return pl.pallas_call(
        body,
        out_shape=shapes,
        in_specs=specs,
        out_specs=vmem if kind == "tail" else (vmem, vmem),
        scratch_shapes=[
            pltpu.VMEM((span + 2, channels, columns), jnp.bfloat16),
            pltpu.VMEM((span + 2, channels, columns), jnp.bfloat16),
            pltpu.VMEM((span, channels, columns), jnp.bfloat16),
            pltpu.SemaphoreType.DMA((4,)),
        ],
    )(*args)


def block_sum(values, span_count):
    peers = lax.axis_size("rows")
    if span_count == peers:
        return values
    lead = (lax.axis_index("rows") % span_count == 0).astype(values.dtype)
    return lax.psum(values * lead, "rows")


def activate(source, gain_vec, shift_vec, cell_count, span_count):
    height, channels, columns = source.shape
    grouped = source.astype(jnp.float32).reshape(height, GROUPS, channels // GROUPS, columns)
    average = block_sum(jnp.sum(grouped, axis=(0, 2, 3)), span_count) / cell_count
    centred = grouped - average[None, :, None, None]
    spread = block_sum(jnp.sum(centred * centred, axis=(0, 2, 3)), span_count) / cell_count
    inverse = lax.rsqrt(spread + EPS)
    normed = (centred * inverse[None, :, None, None]).reshape(height, channels, columns)
    normed = normed * gain_vec[None, :, None] + shift_vec[None, :, None]
    return jax.nn.silu(normed).astype(jnp.bfloat16)


def run_frame(source, first_hist, second_hist, kernels, biases, gains, shifts, cell_count, span_count):
    padded = span_count != lax.axis_size("rows")
    first_in = with_rim(activate(source, gains[0], shifts[0], cell_count, span_count), 0, span_count)
    hidden = causal_conv(first_hist[0], first_hist[1], first_in, kernels[0], biases[0], None, padded)
    second_in = with_rim(activate(hidden, gains[1], shifts[1], cell_count, span_count), 0, span_count)
    result = causal_conv(second_hist[0], second_hist[1], second_in, kernels[1], biases[1], source, padded)
    return (result, (first_hist[1], first_in), (second_hist[1], second_in))


def shards_whole(frames, causal_cache, conv_weight, conv_bias, norm_gain, norm_shift):
    phase_no = lax.axis_index("phase")
    phase_count = lax.axis_size("phase")
    peers = lax.axis_size("rows")
    frame_count, channels, rows_here, columns = frames.shape
    span = rows_here * peers
    half = span // 2
    core = lax.axis_index("rows") % 2
    start = lax.axis_index("rows") * rows_here
    forward = [(s, s + 1) for s in range(phase_count - 1)]
    frames_t = jnp.transpose(frames, (0, 2, 1, 3))
    cache_t = jnp.transpose(causal_cache[0], (0, 1, 3, 2, 4))
    early = lax.all_gather(jnp.stack([frames_t[0], cache_t[0, 0], cache_t[0, 1]]), "rows", axis=1, tiled=True)
    second_cache = lax.all_gather(cache_t[1], "rows", axis=1, tiled=True)
    later = list(frames_t[1:])
    if len(later) == 1:
        later = later * 2
    later = lax.all_gather(jnp.stack(later), "rows", axis=1, tiled=True) if later else early
    frame_of = [(early, 0)] + [(later, f) for f in range(frame_count - 1)]
    cache_of = ((early, (1, 2)), (second_cache, (0, 1)))
    taps = (arrange_taps(conv_weight[0, 0]), arrange_taps(conv_weight[0, 1]))

    def own_rows(x, rim=0):
        return lax.dynamic_slice_in_dim(x, start + rim, rows_here, axis=0)

    got = other = jnp.zeros((half, channels, columns), jnp.bfloat16)
    acts = ([], [])
    blank = jnp.zeros((rows_here, channels, columns), jnp.bfloat16)
    blank_frame = jnp.zeros((span + 2, channels, columns), jnp.bfloat16)
    produced = [blank] * frame_count
    kept = [[blank, blank], [blank, blank]]
    mode = jnp.where(phase_no == 0, 0, 1 + core)
    tick_count = frame_count + phase_count - 1
    frame_nos = jnp.arange(tick_count) - phase_no
    flags = jnp.stack(
        [frame_nos == 0, frame_nos == 1, jnp.full((tick_count,), mode), jnp.full((tick_count,), core)], axis=1
    ).astype(jnp.int32)
    for tick_no in range(tick_count):
        frame_no = tick_no - phase_no
        frame_stack, frame_at = frame_of[min(tick_no, frame_count - 1)]
        recents = []
        for j in range(2):
            a_p = acts[j][-1] if acts[j] else blank_frame
            a_pp = acts[j][-2] if len(acts[j]) > 1 else blank_frame
            recents.append((a_p, a_pp))
        common = (frame_stack, frame_at, (got, other))
        hidden, first_in = fused_conv(
            flags, tick_no, cache_of[0][0], cache_of[0][1], recents[0], *common,
            taps[0], conv_bias[0, 0], (norm_gain[0, 0], norm_shift[0, 0]), "first",
        )
        second = (flags, tick_no, cache_of[1][0], cache_of[1][1], recents[1], *common, taps[1], conv_bias[0, 1])
        if tick_no + 1 == tick_count:
            whole_out, second_in = fused_conv(*second, (norm_gain[0, 1], norm_shift[0, 1]), "all", hidden)
            lead = lax.dynamic_slice_in_dim(whole_out, core * half, half, axis=0)
            tail = lax.dynamic_slice_in_dim(whole_out, (1 - core) * half, half, axis=0)
        else:
            lead, second_in = fused_conv(*second, (norm_gain[0, 1], norm_shift[0, 1]), "lead", hidden)
            tail = fused_conv(*second, (norm_gain[0, 1], norm_shift[0, 1]), "tail", second_in)
        if tick_no + 1 < tick_count:
            got = lax.ppermute(lead, "phase", forward)
            got, tail = lax.optimization_barrier((got, tail))
            other = lax.ppermute(got, "rows", [(i, i ^ 1) for i in range(peers)])
        last = frame_no == frame_count - 1
        for j, a in enumerate((first_in, second_in)):
            stack, (_, k1) = cache_of[j]
            newer = jnp.where(frame_no == 0, own_rows(stack[k1]), own_rows(recents[j][0], 1))
            kept[j] = [jnp.where(last, newer, kept[j][0]), jnp.where(last, own_rows(a, 1), kept[j][1])]
            acts[j].append(a)
        mine = lax.dynamic_slice_in_dim(lead, start - core * half, rows_here, axis=0)
        theirs = lax.dynamic_slice_in_dim(tail, start - (1 - core) * half, rows_here, axis=0)
        result_rows = jnp.where(start // half == core, mine, theirs)
        for f in range(frame_count):
            if 0 <= tick_no - f < phase_count:
                produced[f] = jnp.where(frame_no == f, result_rows, produced[f])
    produced = jnp.transpose(jnp.stack(produced), (0, 2, 1, 3))
    new_cache = jnp.transpose(jnp.stack([jnp.stack(k) for k in kept]), (0, 1, 3, 2, 4))
    return (produced[None], new_cache[None])


def shards(frames, causal_cache, conv_weight, conv_bias, norm_gain, norm_shift):
    peers = lax.axis_size("rows")
    rows_here = frames.shape[2]
    if span_devices(peers, rows_here) == peers and (rows_here * peers) % 2 == 0:
        return shards_whole(frames, causal_cache, conv_weight, conv_bias, norm_gain, norm_shift)
    return shards_split(frames, causal_cache, conv_weight, conv_bias, norm_gain, norm_shift)


def shards_split(frames, causal_cache, conv_weight, conv_bias, norm_gain, norm_shift):
    phase_no = lax.axis_index("phase")
    phase_count = lax.axis_size("phase")
    peers = lax.axis_size("rows")
    frame_count = frames.shape[0]
    channels = frames.shape[1]
    rows_here = frames.shape[2]
    columns = frames.shape[3]
    span_count = span_devices(peers, rows_here)
    span = rows_here * span_count
    cell_count = float(channels // GROUPS * rows_here * peers * columns)
    padded = span_count != peers
    frames_t = jnp.transpose(frames, (0, 2, 1, 3))
    cache_t = jnp.transpose(causal_cache[0], (0, 1, 3, 2, 4))
    early = gather_span(jnp.stack([frames_t[0], cache_t[0, 0], cache_t[0, 1]]), 1, span_count)
    late = gather_span(jnp.stack([cache_t[1, 0], cache_t[1, 1]] + list(frames_t[1:])), 1, span_count)
    frames_span = [early[0]] + [late[2 + f] for f in range(frame_count - 1)]
    first_hist = tuple(with_rim(early[1 + k], 0, span_count) for k in range(2))
    second_hist = tuple(with_rim(late[k], 0, span_count) for k in range(2))
    local_taps = (arrange_taps(conv_weight[0, 0]), arrange_taps(conv_weight[0, 1]))
    incoming = jnp.zeros_like(frames_span[0])
    produced = [jnp.zeros_like(frames_span[0]) for _ in range(frame_count)]
    tick_count = frame_count + phase_count - 1
    for tick_no in range(tick_count):
        frame_no = tick_no - phase_no
        active_now = jnp.logical_and(frame_no >= 0, frame_no < frame_count)
        source = jnp.where(phase_no == 0, frames_span[min(tick_no, frame_count - 1)], incoming)
        result, first_next, second_next = run_frame(
            source, first_hist, second_hist, local_taps, conv_bias[0], norm_gain[0], norm_shift[0],
            cell_count, span_count,
        )
        first_hist = tuple(jnp.where(active_now, a, b) for a, b in zip(first_next, first_hist))
        second_hist = tuple(jnp.where(active_now, a, b) for a, b in zip(second_next, second_hist))
        for f in range(frame_count):
            if 0 <= tick_no - f < phase_count:
                produced[f] = jnp.where(frame_no == f, result, produced[f])
        if tick_no + 1 < tick_count:
            incoming = pass_on(result, span_count)
    start = (lax.axis_index("rows") % span_count) * rows_here
    rim = 1 if padded else 0
    produced = jnp.stack([lax.dynamic_slice_in_dim(p, start, rows_here, axis=0) for p in produced])
    new_cache = jnp.stack(
        [
            jnp.stack([lax.dynamic_slice_in_dim(h, start + rim, rows_here, axis=0) for h in hist])
            for hist in (first_hist, second_hist)
        ]
    )
    produced = jnp.transpose(produced, (0, 2, 1, 3))
    new_cache = jnp.transpose(new_cache, (0, 1, 3, 2, 4))
    return (produced[None], new_cache[None])


def solution(mesh):
    in_specs = (
        P(None, None, "rows", None),
        P("phase", None, None, None, "rows", None),
        P("phase", None, None, None, None, None, None),
        P("phase", None, None),
        P("phase", None, None),
        P("phase", None, None),
    )
    out_specs = (P("phase", None, None, "rows", None), P("phase", None, None, None, "rows", None))
    return jax.shard_map(shards, mesh=mesh, in_specs=in_specs, out_specs=out_specs, check_vma=False)
```

```python
import jax
import jax.numpy as jnp
from jax import lax
from jax.sharding import PartitionSpec as P
from jax.experimental import pallas as pl
from jax.experimental.pallas import tpu as pltpu
import functools

GROUPS = 32
EPS = 1e-06
MAX_SPAN = 16


def span_devices(peers, rows_here):
    count = 1
    while count * 2 <= peers and peers % (count * 2) == 0 and count * 2 * rows_here <= MAX_SPAN:
        count *= 2
    return count


def gather_span(array, dim, span_count):
    if span_count == 1:
        return array
    peers = lax.axis_size("rows")
    if span_count == peers:
        return lax.all_gather(array, "rows", axis=dim, tiled=True)
    place = lax.axis_index("rows") % span_count
    pieces = [array]
    for shift in range(1, span_count):
        pairs = [
            (b * span_count + p, b * span_count + (p + shift) % span_count)
            for b in range(peers // span_count)
            for p in range(span_count)
        ]
        pieces.append(lax.ppermute(array, "rows", pairs))
    stacked = jnp.stack(pieces)
    order = (place - jnp.arange(span_count)) % span_count
    picked = jnp.take(stacked, order, axis=0)
    picked = jnp.moveaxis(picked, 0, dim)
    shape = list(array.shape)
    shape[dim] = shape[dim] * span_count
    return picked.reshape(shape)


def with_rim(array, dim, span_count):
    peers = lax.axis_size("rows")
    length = array.shape[dim]
    if span_count == peers:
        return array
    up = [(i, i + span_count) for i in range(peers - span_count)]
    down = [(j, i) for i, j in up]
    last = lax.slice_in_dim(array, length - 1, length, axis=dim)
    leading = lax.slice_in_dim(array, 0, 1, axis=dim)
    before = lax.ppermute(last, "rows", up)
    after = lax.ppermute(leading, "rows", down)
    return jnp.concatenate([before, array, after], axis=dim)


def pass_on(result, span_count):
    phase_count = lax.axis_size("phase")
    forward = [(s, s + 1) for s in range(phase_count - 1)]
    length = result.shape[0]
    if span_count % 2 or length % 2:
        return lax.ppermute(result, "phase", forward)
    peers = lax.axis_size("rows")
    half = length // 2
    core = lax.axis_index("rows") % 2
    mine = lax.dynamic_slice_in_dim(result, core * half, half, axis=0)
    got = lax.ppermute(mine, "phase", forward)
    other = lax.ppermute(got, "rows", [(i, i ^ 1) for i in range(peers)])
    return jnp.where(core == 0, jnp.concatenate([got, other]), jnp.concatenate([other, got]))


def arrange_taps(weight):
    outputs = weight.shape[3]
    channels = weight.shape[4]
    return jnp.transpose(weight, (2, 3, 0, 1, 4)).reshape(3 * outputs, 9 * channels)


def conv_rows(x0, x1, x2, taps, bias, res, out, rows_out, padded):
    outputs = out.shape[1]
    channels = x0.shape[1]
    columns = x0.shape[2]
    pair = 4 if rows_out % 4 == 0 else (2 if rows_out % 2 == 0 else 1)
    lanes = pair * columns
    lane = lax.broadcasted_iota(jnp.int32, (outputs, lanes), 1) % columns
    frames = (x0, x1, x2)

    def column(r):
        if padded or 0 < r < rows_out - 1:
            base = r if padded else r - 1
            parts = [x[pl.ds(base, 3)] for x in frames]
            return jnp.concatenate(parts, axis=0).reshape(9 * channels, columns)
        zero = jnp.zeros((1, channels, columns), x0.dtype)
        parts = []
        for x in frames:
            for dy in range(3):
                q = r + dy - 1
                parts.append(zero if q < 0 or q >= rows_out else x[pl.ds(q, 1)])
        return jnp.concatenate(parts, axis=0).reshape(9 * channels, columns)

    for r in range(0, rows_out, pair):
        cols = [column(r + k) for k in range(pair)]
        rhs = cols[0] if pair == 1 else jnp.concatenate(cols, axis=1)
        acc = jnp.dot(taps[...], rhs, preferred_element_type=jnp.float32)
        left = pltpu.roll(acc[:outputs], 1, 1)
        right = pltpu.roll(acc[2 * outputs :], lanes - 1, 1)
        total = acc[outputs : 2 * outputs] + jnp.where(lane == 0, 0.0, left)
        total = total + jnp.where(lane == columns - 1, 0.0, right) + bias[...]
        for k in range(pair):
            piece = total[:, k * columns : (k + 1) * columns]
            if res is not None:
                piece = piece + res[r + k].astype(jnp.float32)
            out[r + k] = piece.astype(out.dtype)


def conv_body(x0, x1, x2, taps, bias, *rest, rows_out, with_res, padded):
    res = rest[0] if with_res else None
    conv_rows(x0, x1, x2, taps, bias, res, rest[-1], rows_out, padded)


def causal_conv(x0, x1, x2, taps, bias_vec, res, padded):
    rows_out = x0.shape[0] - 2 if padded else x0.shape[0]
    outputs = taps.shape[0] // 3
    args = [x0, x1, x2, taps, bias_vec.reshape(outputs, 1)]
    if res is not None:
        args.append(res)
    body = functools.partial(conv_body, rows_out=rows_out, with_res=res is not None, padded=padded)
    shape = jax.ShapeDtypeStruct((rows_out, outputs, x0.shape[2]), jnp.bfloat16)
    return pl.pallas_call(body, out_shape=shape)(*args)


def conv_span(x0, x1, x2, taps, bias, res, out, base, count):
    outputs = out.shape[1]
    channels = x0.shape[1]
    columns = x0.shape[2]
    pair = 8 if count % 8 == 0 else (4 if count % 4 == 0 else (2 if count % 2 == 0 else 1))
    lanes = pair * columns
    lane = lax.broadcasted_iota(jnp.int32, (outputs, lanes), 1) % columns

    def step(i, carry):
        r = base + i * pair
        cols = []
        for k in range(pair):
            parts = [x[pl.ds(r + k, 3)] for x in (x0, x1, x2)]
            cols.append(jnp.concatenate(parts, axis=0).reshape(9 * channels, columns))
        rhs = cols[0] if pair == 1 else jnp.concatenate(cols, axis=1)
        acc = jnp.dot(taps[...], rhs, preferred_element_type=jnp.float32)
        left = pltpu.roll(acc[:outputs], 1, 1)
        right = pltpu.roll(acc[2 * outputs :], lanes - 1, 1)
        total = acc[outputs : 2 * outputs] + jnp.where(lane == 0, 0.0, left)
        total = total + jnp.where(lane == columns - 1, 0.0, right) + bias[...]
        for k in range(pair):
            piece = total[:, k * columns : (k + 1) * columns]
            if res is not None:
                piece = piece + res[r + k].astype(jnp.float32)
            out[i * pair + k] = piece.astype(out.dtype)
        return carry

    lax.fori_loop(0, count // pair, step, 0)


def fused_body(flags, caches, a_p, a_pp, frames, src_b, src_c, taps, bias, member, gain, shift, *rest,
               kind, tick, frame_at, cache_at):
    rest = list(rest)
    own = rest.pop(0) if kind != "first" else None
    if kind == "tail":
        out, x0, x1, rawbuf, sems = rest
        act = own
    else:
        out, act, x0, x1, rawbuf, sems = rest
    span, channels, columns = rawbuf.shape
    half = span // 2
    first, second, mode, core = flags[tick, 0], flags[tick, 1], flags[tick, 2], flags[tick, 3]
    c0, c1 = caches.at[cache_at[0]], caches.at[cache_at[1]]
    whole = frames.at[frame_at]
    top, bottom = rawbuf.at[pl.ds(0, half)], rawbuf.at[pl.ds(half, half)]
    inner0, inner1 = x0.at[pl.ds(1, span)], x1.at[pl.ds(1, span)]

    def inner(x):
        return x.at[pl.ds(1, span)]

    def begin(pairs, base):
        for i, (a, b) in enumerate(pairs):
            pltpu.make_async_copy(a, b, sems.at[base + i]).start()

    def finish(pairs, base):
        for i, (a, b) in enumerate(pairs):
            pltpu.make_async_copy(a, b, sems.at[base + i]).wait()

    @pl.when(mode == 0)
    def _():
        begin([(whole.at[pl.ds(0, half)], top), (whole.at[pl.ds(half, half)], bottom)], 0)

    @pl.when(mode == 1)
    def _():
        begin([(src_b, top), (src_c, bottom)], 0)

    @pl.when(mode == 2)
    def _():
        begin([(src_c, top), (src_b, bottom)], 0)

    @pl.when(first == 1)
    def _():
        begin([(c0, inner0), (c1, inner1)], 2)

    @pl.when(jnp.logical_and(first == 0, second == 1))
    def _():
        begin([(c1, inner0), (inner(a_p), inner1)], 2)

    @pl.when(jnp.logical_and(first == 0, second == 0))
    def _():
        begin([(inner(a_pp), inner0), (inner(a_p), inner1)], 2)

    zero = jnp.zeros((channels, columns), x0.dtype)
    for x in (x0, x1):
        x[0] = zero
        x[span + 1] = zero
    source_copies = [(src_b, top), (src_c, bottom)]
    history_copies = [(inner(a_pp), inner0), (inner(a_p), inner1)]

    if kind != "tail":
        if kind == "first":
            finish(source_copies, 0)
            raw = rawbuf
        else:
            raw = own
        count = float(span * columns * (channels // GROUPS))

        def group_total(acc):
            spread = jnp.dot(member[...], acc, precision=lax.Precision.HIGHEST, preferred_element_type=jnp.float32)
            return jnp.sum(spread, axis=1, keepdims=True)

        acc = raw[0].astype(jnp.float32)
        for r in range(1, span):
            acc = acc + raw[r].astype(jnp.float32)
        average = group_total(acc) / count
        acc = jnp.square(raw[0].astype(jnp.float32) - average)
        for r in range(1, span):
            acc = acc + jnp.square(raw[r].astype(jnp.float32) - average)
        inverse = lax.rsqrt(group_total(acc) / count + EPS)
        act[0] = zero
        act[span + 1] = zero
        for r in range(span):
            value = (raw[r].astype(jnp.float32) - average) * inverse
            value = value * gain[...] + shift[...]
            act[r + 1] = (value / (1.0 + jnp.exp(-value))).astype(act.dtype)

    finish(history_copies, 2)
    if kind == "first":
        conv_span(x0, x1, act, taps, bias, None, out, 0, span)
    elif kind == "all":
        finish(source_copies, 0)
        conv_span(x0, x1, act, taps, bias, rawbuf, out, 0, span)
    else:
        finish(source_copies, 0)
        base = core * half if kind == "lead" else (1 - core) * half
        conv_span(x0, x1, act, taps, bias, rawbuf, out, base, half)


def fused_conv(flags, tick, caches, cache_at, recent, frames, frame_at, halves, taps, bias_vec, norm, kind, own=None):
    span, channels, columns = caches.shape[1:]
    outputs = taps.shape[0] // 3
    group_of = jnp.arange(channels) // (channels // GROUPS)
    member = (group_of[:, None] == group_of[None, :]).astype(jnp.float32)
    vmem = pl.BlockSpec(memory_space=pltpu.VMEM)
    anywhere = pl.BlockSpec(memory_space=pl.ANY)
    args = [flags, caches, recent[0], recent[1], frames, halves[0], halves[1]]
    args += [taps, bias_vec.reshape(outputs, 1), member]
    args += [v.reshape(-1, 1).astype(jnp.float32) for v in norm]
    specs = [pl.BlockSpec(memory_space=pltpu.SMEM)] + [anywhere] * 6 + [vmem] * 5
    if own is not None:
        args.append(own)
        specs.append(vmem)
    rows_out = span if kind in ("first", "all") else span // 2
    result = jax.ShapeDtypeStruct((rows_out, outputs, columns), jnp.bfloat16)
    padded = jax.ShapeDtypeStruct((span + 2, channels, columns), jnp.bfloat16)
    shapes = result if kind == "tail" else (result, padded)
    body = functools.partial(
        fused_body, kind=kind, tick=tick, frame_at=frame_at, cache_at=tuple(cache_at)
    )
    return pl.pallas_call(
        body,
        out_shape=shapes,
        in_specs=specs,
        out_specs=vmem if kind == "tail" else (vmem, vmem),
        scratch_shapes=[
            pltpu.VMEM((span + 2, channels, columns), jnp.bfloat16),
            pltpu.VMEM((span + 2, channels, columns), jnp.bfloat16),
            pltpu.VMEM((span, channels, columns), jnp.bfloat16),
            pltpu.SemaphoreType.DMA((4,)),
        ],
    )(*args)


def block_sum(values, span_count):
    peers = lax.axis_size("rows")
    if span_count == peers:
        return values
    lead = (lax.axis_index("rows") % span_count == 0).astype(values.dtype)
    return lax.psum(values * lead, "rows")


def activate(source, gain_vec, shift_vec, cell_count, span_count):
    height, channels, columns = source.shape
    grouped = source.astype(jnp.float32).reshape(height, GROUPS, channels // GROUPS, columns)
    average = block_sum(jnp.sum(grouped, axis=(0, 2, 3)), span_count) / cell_count
    centred = grouped - average[None, :, None, None]
    spread = block_sum(jnp.sum(centred * centred, axis=(0, 2, 3)), span_count) / cell_count
    inverse = lax.rsqrt(spread + EPS)
    normed = (centred * inverse[None, :, None, None]).reshape(height, channels, columns)
    normed = normed * gain_vec[None, :, None] + shift_vec[None, :, None]
    return jax.nn.silu(normed).astype(jnp.bfloat16)


def run_frame(source, first_hist, second_hist, kernels, biases, gains, shifts, cell_count, span_count):
    padded = span_count != lax.axis_size("rows")
    first_in = with_rim(activate(source, gains[0], shifts[0], cell_count, span_count), 0, span_count)
    hidden = causal_conv(first_hist[0], first_hist[1], first_in, kernels[0], biases[0], None, padded)
    second_in = with_rim(activate(hidden, gains[1], shifts[1], cell_count, span_count), 0, span_count)
    result = causal_conv(second_hist[0], second_hist[1], second_in, kernels[1], biases[1], source, padded)
    return (result, (first_hist[1], first_in), (second_hist[1], second_in))


def shards_whole(frames, causal_cache, conv_weight, conv_bias, norm_gain, norm_shift):
    phase_no = lax.axis_index("phase")
    phase_count = lax.axis_size("phase")
    peers = lax.axis_size("rows")
    frame_count, channels, rows_here, columns = frames.shape
    span = rows_here * peers
    half = span // 2
    core = lax.axis_index("rows") % 2
    start = lax.axis_index("rows") * rows_here
    forward = [(s, s + 1) for s in range(phase_count - 1)]
    frames_t = jnp.transpose(frames, (0, 2, 1, 3))
    cache_t = jnp.transpose(causal_cache[0], (0, 1, 3, 2, 4))
    early = lax.all_gather(jnp.stack([frames_t[0], cache_t[0, 0], cache_t[0, 1]]), "rows", axis=1, tiled=True)
    second_cache = lax.all_gather(cache_t[1], "rows", axis=1, tiled=True)
    later = list(frames_t[1:])
    if len(later) == 1:
        later = later * 2
    later = lax.all_gather(jnp.stack(later), "rows", axis=1, tiled=True) if later else early
    frame_of = [(early, 0)] + [(later, f) for f in range(frame_count - 1)]
    cache_of = ((early, (1, 2)), (second_cache, (0, 1)))
    taps = (arrange_taps(conv_weight[0, 0]), arrange_taps(conv_weight[0, 1]))

    def own_rows(x, rim=0):
        return lax.dynamic_slice_in_dim(x, start + rim, rows_here, axis=0)

    got = other = jnp.zeros((half, channels, columns), jnp.bfloat16)
    acts = ([], [])
    blank = jnp.zeros((rows_here, channels, columns), jnp.bfloat16)
    blank_frame = jnp.zeros((span + 2, channels, columns), jnp.bfloat16)
    produced = [blank] * frame_count
    kept = [[blank, blank], [blank, blank]]
    mode = jnp.where(phase_no == 0, 0, 1 + core)
    tick_count = frame_count + phase_count - 1
    frame_nos = jnp.arange(tick_count) - phase_no
    flags = jnp.stack(
        [frame_nos == 0, frame_nos == 1, jnp.full((tick_count,), mode), jnp.full((tick_count,), core)], axis=1
    ).astype(jnp.int32)
    for tick_no in range(tick_count):
        frame_no = tick_no - phase_no
        frame_stack, frame_at = frame_of[min(tick_no, frame_count - 1)]
        recents = []
        for j in range(2):
            a_p = acts[j][-1] if acts[j] else blank_frame
            a_pp = acts[j][-2] if len(acts[j]) > 1 else blank_frame
            recents.append((a_p, a_pp))
        common = (frame_stack, frame_at, (got, other))
        hidden, first_in = fused_conv(
            flags, tick_no, cache_of[0][0], cache_of[0][1], recents[0], *common,
            taps[0], conv_bias[0, 0], (norm_gain[0, 0], norm_shift[0, 0]), "first",
        )
        second = (flags, tick_no, cache_of[1][0], cache_of[1][1], recents[1], *common, taps[1], conv_bias[0, 1])
        if tick_no + 1 == tick_count:
            whole_out, second_in = fused_conv(*second, (norm_gain[0, 1], norm_shift[0, 1]), "all", hidden)
            lead = lax.dynamic_slice_in_dim(whole_out, core * half, half, axis=0)
            tail = lax.dynamic_slice_in_dim(whole_out, (1 - core) * half, half, axis=0)
        else:
            lead, second_in = fused_conv(*second, (norm_gain[0, 1], norm_shift[0, 1]), "lead", hidden)
            tail = fused_conv(*second, (norm_gain[0, 1], norm_shift[0, 1]), "tail", second_in)
        if tick_no + 1 < tick_count:
            got = lax.ppermute(lead, "phase", forward)
            got, tail = lax.optimization_barrier((got, tail))
            other = lax.ppermute(got, "rows", [(i, i ^ 1) for i in range(peers)])
        last = frame_no == frame_count - 1
        for j, a in enumerate((first_in, second_in)):
            stack, (_, k1) = cache_of[j]
            newer = jnp.where(frame_no == 0, own_rows(stack[k1]), own_rows(recents[j][0], 1))
            kept[j] = [jnp.where(last, newer, kept[j][0]), jnp.where(last, own_rows(a, 1), kept[j][1])]
            acts[j].append(a)
        mine = lax.dynamic_slice_in_dim(lead, start - core * half, rows_here, axis=0)
        theirs = lax.dynamic_slice_in_dim(tail, start - (1 - core) * half, rows_here, axis=0)
        result_rows = jnp.where(start // half == core, mine, theirs)
        for f in range(frame_count):
            if 0 <= tick_no - f < phase_count:
                produced[f] = jnp.where(frame_no == f, result_rows, produced[f])
    produced = jnp.transpose(jnp.stack(produced), (0, 2, 1, 3))
    new_cache = jnp.transpose(jnp.stack([jnp.stack(k) for k in kept]), (0, 1, 3, 2, 4))
    return (produced[None], new_cache[None])


def shards(frames, causal_cache, conv_weight, conv_bias, norm_gain, norm_shift):
    peers = lax.axis_size("rows")
    rows_here = frames.shape[2]
    if span_devices(peers, rows_here) == peers and (rows_here * peers) % 2 == 0:
        return shards_whole(frames, causal_cache, conv_weight, conv_bias, norm_gain, norm_shift)
    return shards_split(frames, causal_cache, conv_weight, conv_bias, norm_gain, norm_shift)


def shards_split(frames, causal_cache, conv_weight, conv_bias, norm_gain, norm_shift):
    phase_no = lax.axis_index("phase")
    phase_count = lax.axis_size("phase")
    peers = lax.axis_size("rows")
    frame_count = frames.shape[0]
    channels = frames.shape[1]
    rows_here = frames.shape[2]
    columns = frames.shape[3]
    span_count = span_devices(peers, rows_here)
    span = rows_here * span_count
    cell_count = float(channels // GROUPS * rows_here * peers * columns)
    padded = span_count != peers
    frames_t = jnp.transpose(frames, (0, 2, 1, 3))
    cache_t = jnp.transpose(causal_cache[0], (0, 1, 3, 2, 4))
    early = gather_span(jnp.stack([frames_t[0], cache_t[0, 0], cache_t[0, 1]]), 1, span_count)
    late = gather_span(jnp.stack([cache_t[1, 0], cache_t[1, 1]] + list(frames_t[1:])), 1, span_count)
    frames_span = [early[0]] + [late[2 + f] for f in range(frame_count - 1)]
    first_hist = tuple(with_rim(early[1 + k], 0, span_count) for k in range(2))
    second_hist = tuple(with_rim(late[k], 0, span_count) for k in range(2))
    local_taps = (arrange_taps(conv_weight[0, 0]), arrange_taps(conv_weight[0, 1]))
    incoming = jnp.zeros_like(frames_span[0])
    produced = [jnp.zeros_like(frames_span[0]) for _ in range(frame_count)]
    tick_count = frame_count + phase_count - 1
    for tick_no in range(tick_count):
        frame_no = tick_no - phase_no
        active_now = jnp.logical_and(frame_no >= 0, frame_no < frame_count)
        source = jnp.where(phase_no == 0, frames_span[min(tick_no, frame_count - 1)], incoming)
        result, first_next, second_next = run_frame(
            source, first_hist, second_hist, local_taps, conv_bias[0], norm_gain[0], norm_shift[0],
            cell_count, span_count,
        )
        first_hist = tuple(jnp.where(active_now, a, b) for a, b in zip(first_next, first_hist))
        second_hist = tuple(jnp.where(active_now, a, b) for a, b in zip(second_next, second_hist))
        for f in range(frame_count):
            if 0 <= tick_no - f < phase_count:
                produced[f] = jnp.where(frame_no == f, result, produced[f])
        if tick_no + 1 < tick_count:
            incoming = pass_on(result, span_count)
    start = (lax.axis_index("rows") % span_count) * rows_here
    rim = 1 if padded else 0
    produced = jnp.stack([lax.dynamic_slice_in_dim(p, start, rows_here, axis=0) for p in produced])
    new_cache = jnp.stack(
        [
            jnp.stack([lax.dynamic_slice_in_dim(h, start + rim, rows_here, axis=0) for h in hist])
            for hist in (first_hist, second_hist)
        ]
    )
    produced = jnp.transpose(produced, (0, 2, 1, 3))
    new_cache = jnp.transpose(new_cache, (0, 1, 3, 2, 4))
    return (produced[None], new_cache[None])


def solution(mesh):
    in_specs = (
        P(None, None, "rows", None),
        P("phase", None, None, None, "rows", None),
        P("phase", None, None, None, None, None, None),
        P("phase", None, None),
        P("phase", None, None),
        P("phase", None, None),
    )
    out_specs = (P("phase", None, None, "rows", None), P("phase", None, None, None, "rows", None))
    return jax.shard_map(shards, mesh=mesh, in_specs=in_specs, out_specs=out_specs, check_vma=False)
```

```python
import jax
import jax.numpy as jnp
from jax import lax
from jax.sharding import PartitionSpec as P
from jax.experimental import pallas as pl
from jax.experimental.pallas import tpu as pltpu
import functools

GROUPS = 32
EPS = 1e-06
MAX_SPAN = 16


def span_devices(peers, rows_here):
    count = 1
    while count * 2 <= peers and peers % (count * 2) == 0 and count * 2 * rows_here <= MAX_SPAN:
        count *= 2
    return count


def gather_span(array, dim, span_count):
    if span_count == 1:
        return array
    peers = lax.axis_size("rows")
    if span_count == peers:
        return lax.all_gather(array, "rows", axis=dim, tiled=True)
    place = lax.axis_index("rows") % span_count
    pieces = [array]
    for shift in range(1, span_count):
        pairs = [
            (b * span_count + p, b * span_count + (p + shift) % span_count)
            for b in range(peers // span_count)
            for p in range(span_count)
        ]
        pieces.append(lax.ppermute(array, "rows", pairs))
    stacked = jnp.stack(pieces)
    order = (place - jnp.arange(span_count)) % span_count
    picked = jnp.take(stacked, order, axis=0)
    picked = jnp.moveaxis(picked, 0, dim)
    shape = list(array.shape)
    shape[dim] = shape[dim] * span_count
    return picked.reshape(shape)


def with_rim(array, dim, span_count):
    peers = lax.axis_size("rows")
    length = array.shape[dim]
    if span_count == peers:
        return array
    up = [(i, i + span_count) for i in range(peers - span_count)]
    down = [(j, i) for i, j in up]
    last = lax.slice_in_dim(array, length - 1, length, axis=dim)
    leading = lax.slice_in_dim(array, 0, 1, axis=dim)
    before = lax.ppermute(last, "rows", up)
    after = lax.ppermute(leading, "rows", down)
    return jnp.concatenate([before, array, after], axis=dim)


def pass_on(result, span_count):
    phase_count = lax.axis_size("phase")
    forward = [(s, s + 1) for s in range(phase_count - 1)]
    length = result.shape[0]
    if span_count % 2 or length % 2:
        return lax.ppermute(result, "phase", forward)
    peers = lax.axis_size("rows")
    half = length // 2
    core = lax.axis_index("rows") % 2
    mine = lax.dynamic_slice_in_dim(result, core * half, half, axis=0)
    got = lax.ppermute(mine, "phase", forward)
    other = lax.ppermute(got, "rows", [(i, i ^ 1) for i in range(peers)])
    return jnp.where(core == 0, jnp.concatenate([got, other]), jnp.concatenate([other, got]))


def arrange_taps(weight):
    outputs = weight.shape[3]
    channels = weight.shape[4]
    return jnp.transpose(weight, (2, 3, 0, 1, 4)).reshape(3 * outputs, 9 * channels)


def conv_rows(x0, x1, x2, taps, bias, res, out, rows_out, padded):
    outputs = out.shape[1]
    channels = x0.shape[1]
    columns = x0.shape[2]
    pair = 4 if rows_out % 4 == 0 else (2 if rows_out % 2 == 0 else 1)
    lanes = pair * columns
    lane = lax.broadcasted_iota(jnp.int32, (outputs, lanes), 1) % columns
    frames = (x0, x1, x2)

    def column(r):
        if padded or 0 < r < rows_out - 1:
            base = r if padded else r - 1
            parts = [x[pl.ds(base, 3)] for x in frames]
            return jnp.concatenate(parts, axis=0).reshape(9 * channels, columns)
        zero = jnp.zeros((1, channels, columns), x0.dtype)
        parts = []
        for x in frames:
            for dy in range(3):
                q = r + dy - 1
                parts.append(zero if q < 0 or q >= rows_out else x[pl.ds(q, 1)])
        return jnp.concatenate(parts, axis=0).reshape(9 * channels, columns)

    for r in range(0, rows_out, pair):
        cols = [column(r + k) for k in range(pair)]
        rhs = cols[0] if pair == 1 else jnp.concatenate(cols, axis=1)
        acc = jnp.dot(taps[...], rhs, preferred_element_type=jnp.float32)
        left = pltpu.roll(acc[:outputs], 1, 1)
        right = pltpu.roll(acc[2 * outputs :], lanes - 1, 1)
        total = acc[outputs : 2 * outputs] + jnp.where(lane == 0, 0.0, left)
        total = total + jnp.where(lane == columns - 1, 0.0, right) + bias[...]
        for k in range(pair):
            piece = total[:, k * columns : (k + 1) * columns]
            if res is not None:
                piece = piece + res[r + k].astype(jnp.float32)
            out[r + k] = piece.astype(out.dtype)


def conv_body(x0, x1, x2, taps, bias, *rest, rows_out, with_res, padded):
    res = rest[0] if with_res else None
    conv_rows(x0, x1, x2, taps, bias, res, rest[-1], rows_out, padded)


def causal_conv(x0, x1, x2, taps, bias_vec, res, padded):
    rows_out = x0.shape[0] - 2 if padded else x0.shape[0]
    outputs = taps.shape[0] // 3
    args = [x0, x1, x2, taps, bias_vec.reshape(outputs, 1)]
    if res is not None:
        args.append(res)
    body = functools.partial(conv_body, rows_out=rows_out, with_res=res is not None, padded=padded)
    shape = jax.ShapeDtypeStruct((rows_out, outputs, x0.shape[2]), jnp.bfloat16)
    return pl.pallas_call(body, out_shape=shape)(*args)


def conv_span(x0, x1, x2, taps, bias, res, out, base, count):
    outputs = out.shape[1]
    channels = x0.shape[1]
    columns = x0.shape[2]
    pair = 8 if count % 8 == 0 else (4 if count % 4 == 0 else (2 if count % 2 == 0 else 1))
    lanes = pair * columns
    lane = lax.broadcasted_iota(jnp.int32, (outputs, lanes), 1) % columns

    def step(i, carry):
        r = base + i * pair
        cols = []
        for k in range(pair):
            parts = [x[pl.ds(r + k, 3)] for x in (x0, x1, x2)]
            cols.append(jnp.concatenate(parts, axis=0).reshape(9 * channels, columns))
        rhs = cols[0] if pair == 1 else jnp.concatenate(cols, axis=1)
        acc = jnp.dot(taps[...], rhs, preferred_element_type=jnp.float32)
        left = pltpu.roll(acc[:outputs], 1, 1)
        right = pltpu.roll(acc[2 * outputs :], lanes - 1, 1)
        total = acc[outputs : 2 * outputs] + jnp.where(lane == 0, 0.0, left)
        total = total + jnp.where(lane == columns - 1, 0.0, right) + bias[...]
        for k in range(pair):
            piece = total[:, k * columns : (k + 1) * columns]
            if res is not None:
                piece = piece + res[r + k].astype(jnp.float32)
            out[i * pair + k] = piece.astype(out.dtype)
        return carry

    lax.fori_loop(0, count // pair, step, 0)


def fused_body(flags, caches, a_p, a_pp, frames, src_b, src_c, taps, bias, member, gain, shift, *rest,
               kind, tick, frame_at, cache_at):
    rest = list(rest)
    own = rest.pop(0) if kind != "first" else None
    if kind == "tail":
        out, x0, x1, rawbuf, sems = rest
        act = own
    else:
        out, act, x0, x1, rawbuf, sems = rest
    span, channels, columns = rawbuf.shape
    half = span // 2
    first, second, mode, core = flags[tick, 0], flags[tick, 1], flags[tick, 2], flags[tick, 3]
    c0, c1 = caches.at[cache_at[0]], caches.at[cache_at[1]]
    whole = frames.at[frame_at]
    top, bottom = rawbuf.at[pl.ds(0, half)], rawbuf.at[pl.ds(half, half)]
    inner0, inner1 = x0.at[pl.ds(1, span)], x1.at[pl.ds(1, span)]

    def inner(x):
        return x.at[pl.ds(1, span)]

    def begin(pairs, base):
        for i, (a, b) in enumerate(pairs):
            pltpu.make_async_copy(a, b, sems.at[base + i]).start()

    def finish(pairs, base):
        for i, (a, b) in enumerate(pairs):
            pltpu.make_async_copy(a, b, sems.at[base + i]).wait()

    @pl.when(mode == 0)
    def _():
        begin([(whole.at[pl.ds(0, half)], top), (whole.at[pl.ds(half, half)], bottom)], 0)

    @pl.when(mode == 1)
    def _():
        begin([(src_b, top), (src_c, bottom)], 0)

    @pl.when(mode == 2)
    def _():
        begin([(src_c, top), (src_b, bottom)], 0)

    if kind in ("lead", "tail"):
        base = core * half if kind == "lead" else (1 - core) * half
        low = base - 1 + (base == 0).astype(jnp.int32)
        length = half + 1

        def inner(x, rim=1):
            return x.at[pl.ds(low + rim, length)]

        inner0, inner1 = inner(x0), inner(x1)
        c0, c1 = inner(c0, 0), inner(c1, 0)

    @pl.when(first == 1)
    def _():
        begin([(c0, inner0), (c1, inner1)], 2)

    @pl.when(jnp.logical_and(first == 0, second == 1))
    def _():
        begin([(c1, inner0), (inner(a_p), inner1)], 2)

    @pl.when(jnp.logical_and(first == 0, second == 0))
    def _():
        begin([(inner(a_pp), inner0), (inner(a_p), inner1)], 2)

    zero = jnp.zeros((channels, columns), x0.dtype)
    for x in (x0, x1):
        x[0] = zero
        x[span + 1] = zero
    source_copies = [(src_b, top), (src_c, bottom)]
    history_copies = [(inner(a_pp), inner0), (inner(a_p), inner1)]

    if kind != "tail":
        if kind == "first":
            finish(source_copies, 0)
            raw = rawbuf
        else:
            raw = own
        count = float(span * columns * (channels // GROUPS))

        def group_total(acc):
            spread = jnp.dot(member[...], acc, precision=lax.Precision.HIGHEST, preferred_element_type=jnp.float32)
            return jnp.sum(spread, axis=1, keepdims=True)

        acc = raw[0].astype(jnp.float32)
        for r in range(1, span):
            acc = acc + raw[r].astype(jnp.float32)
        average = group_total(acc) / count
        acc = jnp.square(raw[0].astype(jnp.float32) - average)
        for r in range(1, span):
            acc = acc + jnp.square(raw[r].astype(jnp.float32) - average)
        inverse = lax.rsqrt(group_total(acc) / count + EPS)
        act[0] = zero
        act[span + 1] = zero
        for r in range(span):
            value = (raw[r].astype(jnp.float32) - average) * inverse
            value = value * gain[...] + shift[...]
            act[r + 1] = (value / (1.0 + jnp.exp(-value))).astype(act.dtype)

    finish(history_copies, 2)
    if kind == "first":
        conv_span(x0, x1, act, taps, bias, None, out, 0, span)
    elif kind == "all":
        finish(source_copies, 0)
        conv_span(x0, x1, act, taps, bias, rawbuf, out, 0, span)
    else:
        finish(source_copies, 0)
        base = core * half if kind == "lead" else (1 - core) * half
        conv_span(x0, x1, act, taps, bias, rawbuf, out, base, half)


def fused_conv(flags, tick, caches, cache_at, recent, frames, frame_at, halves, taps, bias_vec, norm, kind, own=None):
    span, channels, columns = caches.shape[1:]
    outputs = taps.shape[0] // 3
    group_of = jnp.arange(channels) // (channels // GROUPS)
    member = (group_of[:, None] == group_of[None, :]).astype(jnp.float32)
    vmem = pl.BlockSpec(memory_space=pltpu.VMEM)
    anywhere = pl.BlockSpec(memory_space=pl.ANY)
    args = [flags, caches, recent[0], recent[1], frames, halves[0], halves[1]]
    args += [taps, bias_vec.reshape(outputs, 1), member]
    args += [v.reshape(-1, 1).astype(jnp.float32) for v in norm]
    specs = [pl.BlockSpec(memory_space=pltpu.SMEM)] + [anywhere] * 6 + [vmem] * 5
    if own is not None:
        args.append(own)
        specs.append(vmem)
    rows_out = span if kind in ("first", "all") else span // 2
    result = jax.ShapeDtypeStruct((rows_out, outputs, columns), jnp.bfloat16)
    padded = jax.ShapeDtypeStruct((span + 2, channels, columns), jnp.bfloat16)
    shapes = result if kind == "tail" else (result, padded)
    body = functools.partial(
        fused_body, kind=kind, tick=tick, frame_at=frame_at, cache_at=tuple(cache_at)
    )
    return pl.pallas_call(
        body,
        out_shape=shapes,
        in_specs=specs,
        out_specs=vmem if kind == "tail" else (vmem, vmem),
        scratch_shapes=[
            pltpu.VMEM((span + 2, channels, columns), jnp.bfloat16),
            pltpu.VMEM((span + 2, channels, columns), jnp.bfloat16),
            pltpu.VMEM((span, channels, columns), jnp.bfloat16),
            pltpu.SemaphoreType.DMA((4,)),
        ],
    )(*args)


def block_sum(values, span_count):
    peers = lax.axis_size("rows")
    if span_count == peers:
        return values
    lead = (lax.axis_index("rows") % span_count == 0).astype(values.dtype)
    return lax.psum(values * lead, "rows")


def activate(source, gain_vec, shift_vec, cell_count, span_count):
    height, channels, columns = source.shape
    grouped = source.astype(jnp.float32).reshape(height, GROUPS, channels // GROUPS, columns)
    average = block_sum(jnp.sum(grouped, axis=(0, 2, 3)), span_count) / cell_count
    centred = grouped - average[None, :, None, None]
    spread = block_sum(jnp.sum(centred * centred, axis=(0, 2, 3)), span_count) / cell_count
    inverse = lax.rsqrt(spread + EPS)
    normed = (centred * inverse[None, :, None, None]).reshape(height, channels, columns)
    normed = normed * gain_vec[None, :, None] + shift_vec[None, :, None]
    return jax.nn.silu(normed).astype(jnp.bfloat16)


def run_frame(source, first_hist, second_hist, kernels, biases, gains, shifts, cell_count, span_count):
    padded = span_count != lax.axis_size("rows")
    first_in = with_rim(activate(source, gains[0], shifts[0], cell_count, span_count), 0, span_count)
    hidden = causal_conv(first_hist[0], first_hist[1], first_in, kernels[0], biases[0], None, padded)
    second_in = with_rim(activate(hidden, gains[1], shifts[1], cell_count, span_count), 0, span_count)
    result = causal_conv(second_hist[0], second_hist[1], second_in, kernels[1], biases[1], source, padded)
    return (result, (first_hist[1], first_in), (second_hist[1], second_in))


def shards_whole(frames, causal_cache, conv_weight, conv_bias, norm_gain, norm_shift):
    phase_no = lax.axis_index("phase")
    phase_count = lax.axis_size("phase")
    peers = lax.axis_size("rows")
    frame_count, channels, rows_here, columns = frames.shape
    span = rows_here * peers
    half = span // 2
    core = lax.axis_index("rows") % 2
    start = lax.axis_index("rows") * rows_here
    forward = [(s, s + 1) for s in range(phase_count - 1)]
    frames_t = jnp.transpose(frames, (0, 2, 1, 3))
    cache_t = jnp.transpose(causal_cache[0], (0, 1, 3, 2, 4))
    early = lax.all_gather(jnp.stack([frames_t[0], cache_t[0, 0], cache_t[0, 1]]), "rows", axis=1, tiled=True)
    second_cache = lax.all_gather(cache_t[1], "rows", axis=1, tiled=True)
    later = list(frames_t[1:])
    if len(later) == 1:
        later = later * 2
    later = lax.all_gather(jnp.stack(later), "rows", axis=1, tiled=True) if later else early
    frame_of = [(early, 0)] + [(later, f) for f in range(frame_count - 1)]
    cache_of = ((early, (1, 2)), (second_cache, (0, 1)))
    taps = (arrange_taps(conv_weight[0, 0]), arrange_taps(conv_weight[0, 1]))

    def own_rows(x, rim=0):
        return lax.dynamic_slice_in_dim(x, start + rim, rows_here, axis=0)

    got = other = jnp.zeros((half, channels, columns), jnp.bfloat16)
    acts = ([], [])
    blank = jnp.zeros((rows_here, channels, columns), jnp.bfloat16)
    blank_frame = jnp.zeros((span + 2, channels, columns), jnp.bfloat16)
    produced = [blank] * frame_count
    kept = [[blank, blank], [blank, blank]]
    mode = jnp.where(phase_no == 0, 0, 1 + core)
    tick_count = frame_count + phase_count - 1
    frame_nos = jnp.arange(tick_count) - phase_no
    flags = jnp.stack(
        [frame_nos == 0, frame_nos == 1, jnp.full((tick_count,), mode), jnp.full((tick_count,), core)], axis=1
    ).astype(jnp.int32)
    for tick_no in range(tick_count):
        frame_no = tick_no - phase_no
        frame_stack, frame_at = frame_of[min(tick_no, frame_count - 1)]
        recents = []
        for j in range(2):
            a_p = acts[j][-1] if acts[j] else blank_frame
            a_pp = acts[j][-2] if len(acts[j]) > 1 else blank_frame
            recents.append((a_p, a_pp))
        common = (frame_stack, frame_at, (got, other))
        hidden, first_in = fused_conv(
            flags, tick_no, cache_of[0][0], cache_of[0][1], recents[0], *common,
            taps[0], conv_bias[0, 0], (norm_gain[0, 0], norm_shift[0, 0]), "first",
        )
        second = (flags, tick_no, cache_of[1][0], cache_of[1][1], recents[1], *common, taps[1], conv_bias[0, 1])
        if tick_no + 1 == tick_count:
            whole_out, second_in = fused_conv(*second, (norm_gain[0, 1], norm_shift[0, 1]), "all", hidden)
            lead = lax.dynamic_slice_in_dim(whole_out, core * half, half, axis=0)
            tail = lax.dynamic_slice_in_dim(whole_out, (1 - core) * half, half, axis=0)
        else:
            lead, second_in = fused_conv(*second, (norm_gain[0, 1], norm_shift[0, 1]), "lead", hidden)
            tail = fused_conv(*second, (norm_gain[0, 1], norm_shift[0, 1]), "tail", second_in)
        if tick_no + 1 < tick_count:
            got = lax.ppermute(lead, "phase", forward)
            got, tail = lax.optimization_barrier((got, tail))
            other = lax.ppermute(got, "rows", [(i, i ^ 1) for i in range(peers)])
        last = frame_no == frame_count - 1
        for j, a in enumerate((first_in, second_in)):
            stack, (_, k1) = cache_of[j]
            newer = jnp.where(frame_no == 0, own_rows(stack[k1]), own_rows(recents[j][0], 1))
            kept[j] = [jnp.where(last, newer, kept[j][0]), jnp.where(last, own_rows(a, 1), kept[j][1])]
            acts[j].append(a)
        mine = lax.dynamic_slice_in_dim(lead, start - core * half, rows_here, axis=0)
        theirs = lax.dynamic_slice_in_dim(tail, start - (1 - core) * half, rows_here, axis=0)
        result_rows = jnp.where(start // half == core, mine, theirs)
        for f in range(frame_count):
            if 0 <= tick_no - f < phase_count:
                produced[f] = jnp.where(frame_no == f, result_rows, produced[f])
    produced = jnp.transpose(jnp.stack(produced), (0, 2, 1, 3))
    new_cache = jnp.transpose(jnp.stack([jnp.stack(k) for k in kept]), (0, 1, 3, 2, 4))
    return (produced[None], new_cache[None])


def shards(frames, causal_cache, conv_weight, conv_bias, norm_gain, norm_shift):
    peers = lax.axis_size("rows")
    rows_here = frames.shape[2]
    if span_devices(peers, rows_here) == peers and (rows_here * peers) % 2 == 0:
        return shards_whole(frames, causal_cache, conv_weight, conv_bias, norm_gain, norm_shift)
    return shards_split(frames, causal_cache, conv_weight, conv_bias, norm_gain, norm_shift)


def shards_split(frames, causal_cache, conv_weight, conv_bias, norm_gain, norm_shift):
    phase_no = lax.axis_index("phase")
    phase_count = lax.axis_size("phase")
    peers = lax.axis_size("rows")
    frame_count = frames.shape[0]
    channels = frames.shape[1]
    rows_here = frames.shape[2]
    columns = frames.shape[3]
    span_count = span_devices(peers, rows_here)
    span = rows_here * span_count
    cell_count = float(channels // GROUPS * rows_here * peers * columns)
    padded = span_count != peers
    frames_t = jnp.transpose(frames, (0, 2, 1, 3))
    cache_t = jnp.transpose(causal_cache[0], (0, 1, 3, 2, 4))
    early = gather_span(jnp.stack([frames_t[0], cache_t[0, 0], cache_t[0, 1]]), 1, span_count)
    late = gather_span(jnp.stack([cache_t[1, 0], cache_t[1, 1]] + list(frames_t[1:])), 1, span_count)
    frames_span = [early[0]] + [late[2 + f] for f in range(frame_count - 1)]
    first_hist = tuple(with_rim(early[1 + k], 0, span_count) for k in range(2))
    second_hist = tuple(with_rim(late[k], 0, span_count) for k in range(2))
    local_taps = (arrange_taps(conv_weight[0, 0]), arrange_taps(conv_weight[0, 1]))
    incoming = jnp.zeros_like(frames_span[0])
    produced = [jnp.zeros_like(frames_span[0]) for _ in range(frame_count)]
    tick_count = frame_count + phase_count - 1
    for tick_no in range(tick_count):
        frame_no = tick_no - phase_no
        active_now = jnp.logical_and(frame_no >= 0, frame_no < frame_count)
        source = jnp.where(phase_no == 0, frames_span[min(tick_no, frame_count - 1)], incoming)
        result, first_next, second_next = run_frame(
            source, first_hist, second_hist, local_taps, conv_bias[0], norm_gain[0], norm_shift[0],
            cell_count, span_count,
        )
        first_hist = tuple(jnp.where(active_now, a, b) for a, b in zip(first_next, first_hist))
        second_hist = tuple(jnp.where(active_now, a, b) for a, b in zip(second_next, second_hist))
        for f in range(frame_count):
            if 0 <= tick_no - f < phase_count:
                produced[f] = jnp.where(frame_no == f, result, produced[f])
        if tick_no + 1 < tick_count:
            incoming = pass_on(result, span_count)
    start = (lax.axis_index("rows") % span_count) * rows_here
    rim = 1 if padded else 0
    produced = jnp.stack([lax.dynamic_slice_in_dim(p, start, rows_here, axis=0) for p in produced])
    new_cache = jnp.stack(
        [
            jnp.stack([lax.dynamic_slice_in_dim(h, start + rim, rows_here, axis=0) for h in hist])
            for hist in (first_hist, second_hist)
        ]
    )
    produced = jnp.transpose(produced, (0, 2, 1, 3))
    new_cache = jnp.transpose(new_cache, (0, 1, 3, 2, 4))
    return (produced[None], new_cache[None])


def solution(mesh):
    in_specs = (
        P(None, None, "rows", None),
        P("phase", None, None, None, "rows", None),
        P("phase", None, None, None, None, None, None),
        P("phase", None, None),
        P("phase", None, None),
        P("phase", None, None),
    )
    out_specs = (P("phase", None, None, "rows", None), P("phase", None, None, None, "rows", None))
    return jax.shard_map(shards, mesh=mesh, in_specs=in_specs, out_specs=out_specs, check_vma=False)
```

```python
import jax
import jax.numpy as jnp
from jax import lax
from jax.sharding import PartitionSpec as P
from jax.experimental import pallas as pl
from jax.experimental.pallas import tpu as pltpu
import functools

GROUPS = 32
EPS = 1e-06
MAX_SPAN = 16


def span_devices(peers, rows_here):
    count = 1
    while count * 2 <= peers and peers % (count * 2) == 0 and count * 2 * rows_here <= MAX_SPAN:
        count *= 2
    return count


def gather_span(array, dim, span_count):
    if span_count == 1:
        return array
    peers = lax.axis_size("rows")
    if span_count == peers:
        return lax.all_gather(array, "rows", axis=dim, tiled=True)
    place = lax.axis_index("rows") % span_count
    pieces = [array]
    for shift in range(1, span_count):
        pairs = [
            (b * span_count + p, b * span_count + (p + shift) % span_count)
            for b in range(peers // span_count)
            for p in range(span_count)
        ]
        pieces.append(lax.ppermute(array, "rows", pairs))
    stacked = jnp.stack(pieces)
    order = (place - jnp.arange(span_count)) % span_count
    picked = jnp.take(stacked, order, axis=0)
    picked = jnp.moveaxis(picked, 0, dim)
    shape = list(array.shape)
    shape[dim] = shape[dim] * span_count
    return picked.reshape(shape)


def with_rim(array, dim, span_count):
    peers = lax.axis_size("rows")
    length = array.shape[dim]
    if span_count == peers:
        return array
    up = [(i, i + span_count) for i in range(peers - span_count)]
    down = [(j, i) for i, j in up]
    last = lax.slice_in_dim(array, length - 1, length, axis=dim)
    leading = lax.slice_in_dim(array, 0, 1, axis=dim)
    before = lax.ppermute(last, "rows", up)
    after = lax.ppermute(leading, "rows", down)
    return jnp.concatenate([before, array, after], axis=dim)


def pass_on(result, span_count):
    phase_count = lax.axis_size("phase")
    forward = [(s, s + 1) for s in range(phase_count - 1)]
    length = result.shape[0]
    if span_count % 2 or length % 2:
        return lax.ppermute(result, "phase", forward)
    peers = lax.axis_size("rows")
    half = length // 2
    core = lax.axis_index("rows") % 2
    mine = lax.dynamic_slice_in_dim(result, core * half, half, axis=0)
    got = lax.ppermute(mine, "phase", forward)
    other = lax.ppermute(got, "rows", [(i, i ^ 1) for i in range(peers)])
    return jnp.where(core == 0, jnp.concatenate([got, other]), jnp.concatenate([other, got]))


def arrange_taps(weight):
    outputs = weight.shape[3]
    channels = weight.shape[4]
    return jnp.transpose(weight, (2, 3, 0, 1, 4)).reshape(3 * outputs, 9 * channels)


def conv_rows(x0, x1, x2, taps, bias, res, out, rows_out, padded):
    outputs = out.shape[1]
    channels = x0.shape[1]
    columns = x0.shape[2]
    pair = 4 if rows_out % 4 == 0 else (2 if rows_out % 2 == 0 else 1)
    lanes = pair * columns
    lane = lax.broadcasted_iota(jnp.int32, (outputs, lanes), 1) % columns
    frames = (x0, x1, x2)

    def column(r):
        if padded or 0 < r < rows_out - 1:
            base = r if padded else r - 1
            parts = [x[pl.ds(base, 3)] for x in frames]
            return jnp.concatenate(parts, axis=0).reshape(9 * channels, columns)
        zero = jnp.zeros((1, channels, columns), x0.dtype)
        parts = []
        for x in frames:
            for dy in range(3):
                q = r + dy - 1
                parts.append(zero if q < 0 or q >= rows_out else x[pl.ds(q, 1)])
        return jnp.concatenate(parts, axis=0).reshape(9 * channels, columns)

    for r in range(0, rows_out, pair):
        cols = [column(r + k) for k in range(pair)]
        rhs = cols[0] if pair == 1 else jnp.concatenate(cols, axis=1)
        acc = jnp.dot(taps[...], rhs, preferred_element_type=jnp.float32)
        left = pltpu.roll(acc[:outputs], 1, 1)
        right = pltpu.roll(acc[2 * outputs :], lanes - 1, 1)
        total = acc[outputs : 2 * outputs] + jnp.where(lane == 0, 0.0, left)
        total = total + jnp.where(lane == columns - 1, 0.0, right) + bias[...]
        for k in range(pair):
            piece = total[:, k * columns : (k + 1) * columns]
            if res is not None:
                piece = piece + res[r + k].astype(jnp.float32)
            out[r + k] = piece.astype(out.dtype)


def conv_body(x0, x1, x2, taps, bias, *rest, rows_out, with_res, padded):
    res = rest[0] if with_res else None
    conv_rows(x0, x1, x2, taps, bias, res, rest[-1], rows_out, padded)


def causal_conv(x0, x1, x2, taps, bias_vec, res, padded):
    rows_out = x0.shape[0] - 2 if padded else x0.shape[0]
    outputs = taps.shape[0] // 3
    args = [x0, x1, x2, taps, bias_vec.reshape(outputs, 1)]
    if res is not None:
        args.append(res)
    body = functools.partial(conv_body, rows_out=rows_out, with_res=res is not None, padded=padded)
    shape = jax.ShapeDtypeStruct((rows_out, outputs, x0.shape[2]), jnp.bfloat16)
    return pl.pallas_call(body, out_shape=shape)(*args)


def conv_span(x0, x1, x2, taps, bias, res, out, base, count):
    outputs = out.shape[1]
    channels = x0.shape[1]
    columns = x0.shape[2]
    pair = next(p for p in (16, 8, 4, 2, 1) if count % p == 0)
    lanes = pair * columns
    lane = lax.broadcasted_iota(jnp.int32, (outputs, lanes), 1) % columns

    def step(i, carry):
        r = base + i * pair
        cols = []
        for k in range(pair):
            parts = [x[pl.ds(r + k, 3)] for x in (x0, x1, x2)]
            cols.append(jnp.concatenate(parts, axis=0).reshape(9 * channels, columns))
        rhs = cols[0] if pair == 1 else jnp.concatenate(cols, axis=1)
        acc = jnp.dot(taps[...], rhs, preferred_element_type=jnp.float32)
        left = pltpu.roll(acc[:outputs], 1, 1)
        right = pltpu.roll(acc[2 * outputs :], lanes - 1, 1)
        total = acc[outputs : 2 * outputs] + jnp.where(lane == 0, 0.0, left)
        total = total + jnp.where(lane == columns - 1, 0.0, right) + bias[...]
        for k in range(pair):
            piece = total[:, k * columns : (k + 1) * columns]
            if res is not None:
                piece = piece + res[r + k].astype(jnp.float32)
            out[i * pair + k] = piece.astype(out.dtype)
        return carry

    lax.fori_loop(0, count // pair, step, 0)


def fused_body(flags, caches, a_p, a_pp, frames, src_b, src_c, taps, bias, member, gain, shift, *rest,
               kind, tick, frame_at, cache_at):
    rest = list(rest)
    own = rest.pop(0) if kind != "first" else None
    if kind == "tail":
        out, x0, x1, rawbuf, sems = rest
        act = own
    else:
        out, act, x0, x1, rawbuf, sems = rest
    span, channels, columns = rawbuf.shape
    half = span // 2
    first, second, mode, core = flags[tick, 0], flags[tick, 1], flags[tick, 2], flags[tick, 3]
    c0, c1 = caches.at[cache_at[0]], caches.at[cache_at[1]]
    whole = frames.at[frame_at]
    top, bottom = rawbuf.at[pl.ds(0, half)], rawbuf.at[pl.ds(half, half)]
    inner0, inner1 = x0.at[pl.ds(1, span)], x1.at[pl.ds(1, span)]

    def inner(x):
        return x.at[pl.ds(1, span)]

    def begin(pairs, base):
        for i, (a, b) in enumerate(pairs):
            pltpu.make_async_copy(a, b, sems.at[base + i]).start()

    def finish(pairs, base):
        for i, (a, b) in enumerate(pairs):
            pltpu.make_async_copy(a, b, sems.at[base + i]).wait()

    @pl.when(mode == 0)
    def _():
        begin([(whole.at[pl.ds(0, half)], top), (whole.at[pl.ds(half, half)], bottom)], 0)

    @pl.when(mode == 1)
    def _():
        begin([(src_b, top), (src_c, bottom)], 0)

    @pl.when(mode == 2)
    def _():
        begin([(src_c, top), (src_b, bottom)], 0)

    @pl.when(first == 1)
    def _():
        begin([(c0, inner0), (c1, inner1)], 2)

    @pl.when(jnp.logical_and(first == 0, second == 1))
    def _():
        begin([(c1, inner0), (inner(a_p), inner1)], 2)

    @pl.when(jnp.logical_and(first == 0, second == 0))
    def _():
        begin([(inner(a_pp), inner0), (inner(a_p), inner1)], 2)

    zero = jnp.zeros((channels, columns), x0.dtype)
    for x in (x0, x1):
        x[0] = zero
        x[span + 1] = zero
    source_copies = [(src_b, top), (src_c, bottom)]
    history_copies = [(inner(a_pp), inner0), (inner(a_p), inner1)]

    if kind != "tail":
        if kind == "first":
            finish(source_copies, 0)
            raw = rawbuf
        else:
            raw = own
        count = float(span * columns * (channels // GROUPS))

        def group_total(acc):
            spread = jnp.dot(member[...], acc, precision=lax.Precision.HIGHEST, preferred_element_type=jnp.float32)
            return jnp.sum(spread, axis=1, keepdims=True)

        acc = raw[0].astype(jnp.float32)
        for r in range(1, span):
            acc = acc + raw[r].astype(jnp.float32)
        average = group_total(acc) / count
        acc = jnp.square(raw[0].astype(jnp.float32) - average)
        for r in range(1, span):
            acc = acc + jnp.square(raw[r].astype(jnp.float32) - average)
        inverse = lax.rsqrt(group_total(acc) / count + EPS)
        act[0] = zero
        act[span + 1] = zero
        for r in range(span):
            value = (raw[r].astype(jnp.float32) - average) * inverse
            value = value * gain[...] + shift[...]
            act[r + 1] = (value / (1.0 + jnp.exp(-value))).astype(act.dtype)

    finish(history_copies, 2)
    if kind == "first":
        conv_span(x0, x1, act, taps, bias, None, out, 0, span)
    elif kind == "all":
        finish(source_copies, 0)
        conv_span(x0, x1, act, taps, bias, rawbuf, out, 0, span)
    else:
        finish(source_copies, 0)
        base = core * half if kind == "lead" else (1 - core) * half
        conv_span(x0, x1, act, taps, bias, rawbuf, out, base, half)


def fused_conv(flags, tick, caches, cache_at, recent, frames, frame_at, halves, taps, bias_vec, norm, kind, own=None):
    span, channels, columns = caches.shape[1:]
    outputs = taps.shape[0] // 3
    group_of = jnp.arange(channels) // (channels // GROUPS)
    member = (group_of[:, None] == group_of[None, :]).astype(jnp.float32)
    vmem = pl.BlockSpec(memory_space=pltpu.VMEM)
    anywhere = pl.BlockSpec(memory_space=pl.ANY)
    args = [flags, caches, recent[0], recent[1], frames, halves[0], halves[1]]
    args += [taps, bias_vec.reshape(outputs, 1), member]
    args += [v.reshape(-1, 1).astype(jnp.float32) for v in norm]
    specs = [pl.BlockSpec(memory_space=pltpu.SMEM)] + [anywhere] * 6 + [vmem] * 5
    if own is not None:
        args.append(own)
        specs.append(vmem)
    rows_out = span if kind in ("first", "all") else span // 2
    result = jax.ShapeDtypeStruct((rows_out, outputs, columns), jnp.bfloat16)
    padded = jax.ShapeDtypeStruct((span + 2, channels, columns), jnp.bfloat16)
    shapes = result if kind == "tail" else (result, padded)
    body = functools.partial(
        fused_body, kind=kind, tick=tick, frame_at=frame_at, cache_at=tuple(cache_at)
    )
    return pl.pallas_call(
        body,
        out_shape=shapes,
        in_specs=specs,
        out_specs=vmem if kind == "tail" else (vmem, vmem),
        scratch_shapes=[
            pltpu.VMEM((span + 2, channels, columns), jnp.bfloat16),
            pltpu.VMEM((span + 2, channels, columns), jnp.bfloat16),
            pltpu.VMEM((span, channels, columns), jnp.bfloat16),
            pltpu.SemaphoreType.DMA((4,)),
        ],
    )(*args)


def block_sum(values, span_count):
    peers = lax.axis_size("rows")
    if span_count == peers:
        return values
    lead = (lax.axis_index("rows") % span_count == 0).astype(values.dtype)
    return lax.psum(values * lead, "rows")


def activate(source, gain_vec, shift_vec, cell_count, span_count):
    height, channels, columns = source.shape
    grouped = source.astype(jnp.float32).reshape(height, GROUPS, channels // GROUPS, columns)
    average = block_sum(jnp.sum(grouped, axis=(0, 2, 3)), span_count) / cell_count
    centred = grouped - average[None, :, None, None]
    spread = block_sum(jnp.sum(centred * centred, axis=(0, 2, 3)), span_count) / cell_count
    inverse = lax.rsqrt(spread + EPS)
    normed = (centred * inverse[None, :, None, None]).reshape(height, channels, columns)
    normed = normed * gain_vec[None, :, None] + shift_vec[None, :, None]
    return jax.nn.silu(normed).astype(jnp.bfloat16)


def run_frame(source, first_hist, second_hist, kernels, biases, gains, shifts, cell_count, span_count):
    padded = span_count != lax.axis_size("rows")
    first_in = with_rim(activate(source, gains[0], shifts[0], cell_count, span_count), 0, span_count)
    hidden = causal_conv(first_hist[0], first_hist[1], first_in, kernels[0], biases[0], None, padded)
    second_in = with_rim(activate(hidden, gains[1], shifts[1], cell_count, span_count), 0, span_count)
    result = causal_conv(second_hist[0], second_hist[1], second_in, kernels[1], biases[1], source, padded)
    return (result, (first_hist[1], first_in), (second_hist[1], second_in))


def shards_whole(frames, causal_cache, conv_weight, conv_bias, norm_gain, norm_shift):
    phase_no = lax.axis_index("phase")
    phase_count = lax.axis_size("phase")
    peers = lax.axis_size("rows")
    frame_count, channels, rows_here, columns = frames.shape
    span = rows_here * peers
    half = span // 2
    core = lax.axis_index("rows") % 2
    start = lax.axis_index("rows") * rows_here
    forward = [(s, s + 1) for s in range(phase_count - 1)]
    frames_t = jnp.transpose(frames, (0, 2, 1, 3))
    cache_t = jnp.transpose(causal_cache[0], (0, 1, 3, 2, 4))
    early = lax.all_gather(jnp.stack([frames_t[0], cache_t[0, 0], cache_t[0, 1]]), "rows", axis=1, tiled=True)
    second_cache = lax.all_gather(cache_t[1], "rows", axis=1, tiled=True)
    later = list(frames_t[1:])
    if len(later) == 1:
        later = later * 2
    later = lax.all_gather(jnp.stack(later), "rows", axis=1, tiled=True) if later else early
    frame_of = [(early, 0)] + [(later, f) for f in range(frame_count - 1)]
    cache_of = ((early, (1, 2)), (second_cache, (0, 1)))
    taps = (arrange_taps(conv_weight[0, 0]), arrange_taps(conv_weight[0, 1]))

    def own_rows(x, rim=0):
        return lax.dynamic_slice_in_dim(x, start + rim, rows_here, axis=0)

    got = other = jnp.zeros((half, channels, columns), jnp.bfloat16)
    acts = ([], [])
    blank = jnp.zeros((rows_here, channels, columns), jnp.bfloat16)
    blank_frame = jnp.zeros((span + 2, channels, columns), jnp.bfloat16)
    produced = [blank] * frame_count
    kept = [[blank, blank], [blank, blank]]
    mode = jnp.where(phase_no == 0, 0, 1 + core)
    tick_count = frame_count + phase_count - 1
    frame_nos = jnp.arange(tick_count) - phase_no
    flags = jnp.stack(
        [frame_nos == 0, frame_nos == 1, jnp.full((tick_count,), mode), jnp.full((tick_count,), core)], axis=1
    ).astype(jnp.int32)
    for tick_no in range(tick_count):
        frame_no = tick_no - phase_no
        frame_stack, frame_at = frame_of[min(tick_no, frame_count - 1)]
        recents = []
        for j in range(2):
            a_p = acts[j][-1] if acts[j] else blank_frame
            a_pp = acts[j][-2] if len(acts[j]) > 1 else blank_frame
            recents.append((a_p, a_pp))
        common = (frame_stack, frame_at, (got, other))
        hidden, first_in = fused_conv(
            flags, tick_no, cache_of[0][0], cache_of[0][1], recents[0], *common,
            taps[0], conv_bias[0, 0], (norm_gain[0, 0], norm_shift[0, 0]), "first",
        )
        second = (flags, tick_no, cache_of[1][0], cache_of[1][1], recents[1], *common, taps[1], conv_bias[0, 1])
        if tick_no + 1 == tick_count:
            whole_out, second_in = fused_conv(*second, (norm_gain[0, 1], norm_shift[0, 1]), "all", hidden)
            lead = lax.dynamic_slice_in_dim(whole_out, core * half, half, axis=0)
            tail = lax.dynamic_slice_in_dim(whole_out, (1 - core) * half, half, axis=0)
        else:
            lead, second_in = fused_conv(*second, (norm_gain[0, 1], norm_shift[0, 1]), "lead", hidden)
            tail = fused_conv(*second, (norm_gain[0, 1], norm_shift[0, 1]), "tail", second_in)
        if tick_no + 1 < tick_count:
            got = lax.ppermute(lead, "phase", forward)
            got, tail = lax.optimization_barrier((got, tail))
            other = lax.ppermute(got, "rows", [(i, i ^ 1) for i in range(peers)])
        last = frame_no == frame_count - 1
        for j, a in enumerate((first_in, second_in)):
            stack, (_, k1) = cache_of[j]
            newer = jnp.where(frame_no == 0, own_rows(stack[k1]), own_rows(recents[j][0], 1))
            kept[j] = [jnp.where(last, newer, kept[j][0]), jnp.where(last, own_rows(a, 1), kept[j][1])]
            acts[j].append(a)
        mine = lax.dynamic_slice_in_dim(lead, start - core * half, rows_here, axis=0)
        theirs = lax.dynamic_slice_in_dim(tail, start - (1 - core) * half, rows_here, axis=0)
        result_rows = jnp.where(start // half == core, mine, theirs)
        for f in range(frame_count):
            if 0 <= tick_no - f < phase_count:
                produced[f] = jnp.where(frame_no == f, result_rows, produced[f])
    produced = jnp.transpose(jnp.stack(produced), (0, 2, 1, 3))
    new_cache = jnp.transpose(jnp.stack([jnp.stack(k) for k in kept]), (0, 1, 3, 2, 4))
    return (produced[None], new_cache[None])


def shards(frames, causal_cache, conv_weight, conv_bias, norm_gain, norm_shift):
    peers = lax.axis_size("rows")
    rows_here = frames.shape[2]
    if span_devices(peers, rows_here) == peers and (rows_here * peers) % 2 == 0:
        return shards_whole(frames, causal_cache, conv_weight, conv_bias, norm_gain, norm_shift)
    return shards_split(frames, causal_cache, conv_weight, conv_bias, norm_gain, norm_shift)


def shards_split(frames, causal_cache, conv_weight, conv_bias, norm_gain, norm_shift):
    phase_no = lax.axis_index("phase")
    phase_count = lax.axis_size("phase")
    peers = lax.axis_size("rows")
    frame_count = frames.shape[0]
    channels = frames.shape[1]
    rows_here = frames.shape[2]
    columns = frames.shape[3]
    span_count = span_devices(peers, rows_here)
    span = rows_here * span_count
    cell_count = float(channels // GROUPS * rows_here * peers * columns)
    padded = span_count != peers
    frames_t = jnp.transpose(frames, (0, 2, 1, 3))
    cache_t = jnp.transpose(causal_cache[0], (0, 1, 3, 2, 4))
    early = gather_span(jnp.stack([frames_t[0], cache_t[0, 0], cache_t[0, 1]]), 1, span_count)
    late = gather_span(jnp.stack([cache_t[1, 0], cache_t[1, 1]] + list(frames_t[1:])), 1, span_count)
    frames_span = [early[0]] + [late[2 + f] for f in range(frame_count - 1)]
    first_hist = tuple(with_rim(early[1 + k], 0, span_count) for k in range(2))
    second_hist = tuple(with_rim(late[k], 0, span_count) for k in range(2))
    local_taps = (arrange_taps(conv_weight[0, 0]), arrange_taps(conv_weight[0, 1]))
    incoming = jnp.zeros_like(frames_span[0])
    produced = [jnp.zeros_like(frames_span[0]) for _ in range(frame_count)]
    tick_count = frame_count + phase_count - 1
    for tick_no in range(tick_count):
        frame_no = tick_no - phase_no
        active_now = jnp.logical_and(frame_no >= 0, frame_no < frame_count)
        source = jnp.where(phase_no == 0, frames_span[min(tick_no, frame_count - 1)], incoming)
        result, first_next, second_next = run_frame(
            source, first_hist, second_hist, local_taps, conv_bias[0], norm_gain[0], norm_shift[0],
            cell_count, span_count,
        )
        first_hist = tuple(jnp.where(active_now, a, b) for a, b in zip(first_next, first_hist))
        second_hist = tuple(jnp.where(active_now, a, b) for a, b in zip(second_next, second_hist))
        for f in range(frame_count):
            if 0 <= tick_no - f < phase_count:
                produced[f] = jnp.where(frame_no == f, result, produced[f])
        if tick_no + 1 < tick_count:
            incoming = pass_on(result, span_count)
    start = (lax.axis_index("rows") % span_count) * rows_here
    rim = 1 if padded else 0
    produced = jnp.stack([lax.dynamic_slice_in_dim(p, start, rows_here, axis=0) for p in produced])
    new_cache = jnp.stack(
        [
            jnp.stack([lax.dynamic_slice_in_dim(h, start + rim, rows_here, axis=0) for h in hist])
            for hist in (first_hist, second_hist)
        ]
    )
    produced = jnp.transpose(produced, (0, 2, 1, 3))
    new_cache = jnp.transpose(new_cache, (0, 1, 3, 2, 4))
    return (produced[None], new_cache[None])


def solution(mesh):
    in_specs = (
        P(None, None, "rows", None),
        P("phase", None, None, None, "rows", None),
        P("phase", None, None, None, None, None, None),
        P("phase", None, None),
        P("phase", None, None),
        P("phase", None, None),
    )
    out_specs = (P("phase", None, None, "rows", None), P("phase", None, None, None, "rows", None))
    return jax.shard_map(shards, mesh=mesh, in_specs=in_specs, out_specs=out_specs, check_vma=False)
```

```python
import jax
import jax.numpy as jnp
from jax import lax
from jax.sharding import PartitionSpec as P
from jax.experimental import pallas as pl
from jax.experimental.pallas import tpu as pltpu
import functools

GROUPS = 32
EPS = 1e-06
MAX_SPAN = 16


def span_devices(peers, rows_here):
    count = 1
    while count * 2 <= peers and peers % (count * 2) == 0 and count * 2 * rows_here <= MAX_SPAN:
        count *= 2
    return count


def gather_span(array, dim, span_count):
    if span_count == 1:
        return array
    peers = lax.axis_size("rows")
    if span_count == peers:
        return lax.all_gather(array, "rows", axis=dim, tiled=True)
    place = lax.axis_index("rows") % span_count
    pieces = [array]
    for shift in range(1, span_count):
        pairs = [
            (b * span_count + p, b * span_count + (p + shift) % span_count)
            for b in range(peers // span_count)
            for p in range(span_count)
        ]
        pieces.append(lax.ppermute(array, "rows", pairs))
    stacked = jnp.stack(pieces)
    order = (place - jnp.arange(span_count)) % span_count
    picked = jnp.take(stacked, order, axis=0)
    picked = jnp.moveaxis(picked, 0, dim)
    shape = list(array.shape)
    shape[dim] = shape[dim] * span_count
    return picked.reshape(shape)


def with_rim(array, dim, span_count):
    peers = lax.axis_size("rows")
    length = array.shape[dim]
    if span_count == peers:
        return array
    up = [(i, i + span_count) for i in range(peers - span_count)]
    down = [(j, i) for i, j in up]
    last = lax.slice_in_dim(array, length - 1, length, axis=dim)
    leading = lax.slice_in_dim(array, 0, 1, axis=dim)
    before = lax.ppermute(last, "rows", up)
    after = lax.ppermute(leading, "rows", down)
    return jnp.concatenate([before, array, after], axis=dim)


def pass_on(result, span_count):
    phase_count = lax.axis_size("phase")
    forward = [(s, s + 1) for s in range(phase_count - 1)]
    length = result.shape[0]
    if span_count % 2 or length % 2:
        return lax.ppermute(result, "phase", forward)
    peers = lax.axis_size("rows")
    half = length // 2
    core = lax.axis_index("rows") % 2
    mine = lax.dynamic_slice_in_dim(result, core * half, half, axis=0)
    got = lax.ppermute(mine, "phase", forward)
    other = lax.ppermute(got, "rows", [(i, i ^ 1) for i in range(peers)])
    return jnp.where(core == 0, jnp.concatenate([got, other]), jnp.concatenate([other, got]))


def arrange_taps(weight):
    outputs = weight.shape[3]
    channels = weight.shape[4]
    return jnp.transpose(weight, (2, 3, 0, 1, 4)).reshape(3 * outputs, 9 * channels)


def conv_rows(x0, x1, x2, taps, bias, res, out, rows_out, padded):
    outputs = out.shape[1]
    channels = x0.shape[1]
    columns = x0.shape[2]
    pair = 4 if rows_out % 4 == 0 else (2 if rows_out % 2 == 0 else 1)
    lanes = pair * columns
    lane = lax.broadcasted_iota(jnp.int32, (outputs, lanes), 1) % columns
    frames = (x0, x1, x2)

    def column(r):
        if padded or 0 < r < rows_out - 1:
            base = r if padded else r - 1
            parts = [x[pl.ds(base, 3)] for x in frames]
            return jnp.concatenate(parts, axis=0).reshape(9 * channels, columns)
        zero = jnp.zeros((1, channels, columns), x0.dtype)
        parts = []
        for x in frames:
            for dy in range(3):
                q = r + dy - 1
                parts.append(zero if q < 0 or q >= rows_out else x[pl.ds(q, 1)])
        return jnp.concatenate(parts, axis=0).reshape(9 * channels, columns)

    for r in range(0, rows_out, pair):
        cols = [column(r + k) for k in range(pair)]
        rhs = cols[0] if pair == 1 else jnp.concatenate(cols, axis=1)
        acc = jnp.dot(taps[...], rhs, preferred_element_type=jnp.float32)
        left = pltpu.roll(acc[:outputs], 1, 1)
        right = pltpu.roll(acc[2 * outputs :], lanes - 1, 1)
        total = acc[outputs : 2 * outputs] + jnp.where(lane == 0, 0.0, left)
        total = total + jnp.where(lane == columns - 1, 0.0, right) + bias[...]
        for k in range(pair):
            piece = total[:, k * columns : (k + 1) * columns]
            if res is not None:
                piece = piece + res[r + k].astype(jnp.float32)
            out[r + k] = piece.astype(out.dtype)


def conv_body(x0, x1, x2, taps, bias, *rest, rows_out, with_res, padded):
    res = rest[0] if with_res else None
    conv_rows(x0, x1, x2, taps, bias, res, rest[-1], rows_out, padded)


def causal_conv(x0, x1, x2, taps, bias_vec, res, padded):
    rows_out = x0.shape[0] - 2 if padded else x0.shape[0]
    outputs = taps.shape[0] // 3
    args = [x0, x1, x2, taps, bias_vec.reshape(outputs, 1)]
    if res is not None:
        args.append(res)
    body = functools.partial(conv_body, rows_out=rows_out, with_res=res is not None, padded=padded)
    shape = jax.ShapeDtypeStruct((rows_out, outputs, x0.shape[2]), jnp.bfloat16)
    return pl.pallas_call(body, out_shape=shape)(*args)


def conv_span(x0, x1, x2, taps, bias, res, out, base, count):
    outputs = out.shape[1]
    channels = x0.shape[1]
    columns = x0.shape[2]
    pair = next(p for p in (16, 8, 4, 2, 1) if count % p == 0)
    lanes = pair * columns
    lane = lax.broadcasted_iota(jnp.int32, (outputs, lanes), 1) % columns

    def step(i, carry):
        r = base + i * pair
        cols = []
        for k in range(pair):
            parts = [x[pl.ds(r + k, 3)] for x in (x0, x1, x2)]
            cols.append(jnp.concatenate(parts, axis=0).reshape(9 * channels, columns))
        rhs = cols[0] if pair == 1 else jnp.concatenate(cols, axis=1)
        acc = jnp.dot(taps[...], rhs, preferred_element_type=jnp.float32)
        left = pltpu.roll(acc[:outputs], 1, 1)
        right = pltpu.roll(acc[2 * outputs :], lanes - 1, 1)
        total = acc[outputs : 2 * outputs] + jnp.where(lane == 0, 0.0, left)
        total = total + jnp.where(lane == columns - 1, 0.0, right) + bias[...]
        for k in range(pair):
            piece = total[:, k * columns : (k + 1) * columns]
            if res is not None:
                piece = piece + res[r + k].astype(jnp.float32)
            out[i * pair + k] = piece.astype(out.dtype)
        return carry

    lax.fori_loop(0, count // pair, step, 0)


def fused_body(flags, caches, a_p, a_pp, frames, src_b, src_c, taps, bias, member, gain, shift, *rest,
               kind, tick, frame_at, cache_at):
    rest = list(rest)
    own = rest.pop(0) if kind != "first" else None
    if kind == "tail":
        out, x0, x1, rawbuf, sems = rest
        act = own
    else:
        out, act, x0, x1, rawbuf, sems = rest
    span, channels, columns = rawbuf.shape
    half = span // 2
    first, second, mode, core = flags[tick, 0], flags[tick, 1], flags[tick, 2], flags[tick, 3]
    c0, c1 = caches.at[cache_at[0]], caches.at[cache_at[1]]
    whole = frames.at[frame_at]
    top, bottom = rawbuf.at[pl.ds(0, half)], rawbuf.at[pl.ds(half, half)]
    inner0, inner1 = x0.at[pl.ds(1, span)], x1.at[pl.ds(1, span)]

    def inner(x):
        return x.at[pl.ds(1, span)]

    def begin(pairs, base):
        for i, (a, b) in enumerate(pairs):
            pltpu.make_async_copy(a, b, sems.at[base + i]).start()

    def finish(pairs, base):
        for i, (a, b) in enumerate(pairs):
            pltpu.make_async_copy(a, b, sems.at[base + i]).wait()

    @pl.when(mode == 0)
    def _():
        begin([(whole.at[pl.ds(0, half)], top), (whole.at[pl.ds(half, half)], bottom)], 0)

    @pl.when(mode == 1)
    def _():
        begin([(src_b, top), (src_c, bottom)], 0)

    @pl.when(mode == 2)
    def _():
        begin([(src_c, top), (src_b, bottom)], 0)

    @pl.when(first == 1)
    def _():
        begin([(c0, inner0), (c1, inner1)], 2)

    @pl.when(jnp.logical_and(first == 0, second == 1))
    def _():
        begin([(c1, inner0), (inner(a_p), inner1)], 2)

    @pl.when(jnp.logical_and(first == 0, second == 0))
    def _():
        begin([(inner(a_pp), inner0), (inner(a_p), inner1)], 2)

    zero = jnp.zeros((channels, columns), x0.dtype)
    for x in (x0, x1):
        x[0] = zero
        x[span + 1] = zero
    source_copies = [(src_b, top), (src_c, bottom)]
    history_copies = [(inner(a_pp), inner0), (inner(a_p), inner1)]

    if kind != "tail":
        if kind == "first":
            finish(source_copies, 0)
            raw = rawbuf
        else:
            raw = own
        count = float(span * columns * (channels // GROUPS))

        def group_total(acc):
            spread = jnp.dot(member[...], acc, precision=lax.Precision.HIGHEST, preferred_element_type=jnp.float32)
            return jnp.sum(spread, axis=1, keepdims=True)

        acc = raw[0].astype(jnp.float32)
        for r in range(1, span):
            acc = acc + raw[r].astype(jnp.float32)
        average = group_total(acc) / count
        acc = jnp.square(raw[0].astype(jnp.float32) - average)
        for r in range(1, span):
            acc = acc + jnp.square(raw[r].astype(jnp.float32) - average)
        inverse = lax.rsqrt(group_total(acc) / count + EPS)
        act[0] = zero
        act[span + 1] = zero
        for r in range(span):
            value = (raw[r].astype(jnp.float32) - average) * inverse
            value = value * gain[...] + shift[...]
            act[r + 1] = (value / (1.0 + jnp.exp(-value))).astype(act.dtype)

    finish(history_copies, 2)
    if kind == "first":
        conv_span(x0, x1, act, taps, bias, None, out, 0, span)
    elif kind == "all":
        finish(source_copies, 0)
        conv_span(x0, x1, act, taps, bias, rawbuf, out, 0, span)
    else:
        finish(source_copies, 0)
        base = core * half if kind == "lead" else (1 - core) * half
        conv_span(x0, x1, act, taps, bias, rawbuf, out, base, half)


def fused_conv(flags, tick, caches, cache_at, recent, frames, frame_at, halves, taps, bias_vec, norm, kind, own=None):
    span, channels, columns = caches.shape[1:]
    outputs = taps.shape[0] // 3
    group_of = jnp.arange(channels) // (channels // GROUPS)
    member = (group_of[:, None] == group_of[None, :]).astype(jnp.float32)
    vmem = pl.BlockSpec(memory_space=pltpu.VMEM)
    anywhere = pl.BlockSpec(memory_space=pl.ANY)
    args = [flags, caches, recent[0], recent[1], frames, halves[0], halves[1]]
    args += [taps, bias_vec.reshape(outputs, 1), member]
    args += [v.reshape(-1, 1).astype(jnp.float32) for v in norm]
    specs = [pl.BlockSpec(memory_space=pltpu.SMEM)] + [anywhere] * 4 + [vmem] * 7
    if own is not None:
        args.append(own)
        specs.append(vmem)
    rows_out = span if kind in ("first", "all") else span // 2
    result = jax.ShapeDtypeStruct((rows_out, outputs, columns), jnp.bfloat16)
    padded = jax.ShapeDtypeStruct((span + 2, channels, columns), jnp.bfloat16)
    shapes = result if kind == "tail" else (result, padded)
    body = functools.partial(
        fused_body, kind=kind, tick=tick, frame_at=frame_at, cache_at=tuple(cache_at)
    )
    return pl.pallas_call(
        body,
        out_shape=shapes,
        in_specs=specs,
        out_specs=vmem if kind == "tail" else (vmem, vmem),
        scratch_shapes=[
            pltpu.VMEM((span + 2, channels, columns), jnp.bfloat16),
            pltpu.VMEM((span + 2, channels, columns), jnp.bfloat16),
            pltpu.VMEM((span, channels, columns), jnp.bfloat16),
            pltpu.SemaphoreType.DMA((4,)),
        ],
    )(*args)


def block_sum(values, span_count):
    peers = lax.axis_size("rows")
    if span_count == peers:
        return values
    lead = (lax.axis_index("rows") % span_count == 0).astype(values.dtype)
    return lax.psum(values * lead, "rows")


def activate(source, gain_vec, shift_vec, cell_count, span_count):
    height, channels, columns = source.shape
    grouped = source.astype(jnp.float32).reshape(height, GROUPS, channels // GROUPS, columns)
    average = block_sum(jnp.sum(grouped, axis=(0, 2, 3)), span_count) / cell_count
    centred = grouped - average[None, :, None, None]
    spread = block_sum(jnp.sum(centred * centred, axis=(0, 2, 3)), span_count) / cell_count
    inverse = lax.rsqrt(spread + EPS)
    normed = (centred * inverse[None, :, None, None]).reshape(height, channels, columns)
    normed = normed * gain_vec[None, :, None] + shift_vec[None, :, None]
    return jax.nn.silu(normed).astype(jnp.bfloat16)


def run_frame(source, first_hist, second_hist, kernels, biases, gains, shifts, cell_count, span_count):
    padded = span_count != lax.axis_size("rows")
    first_in = with_rim(activate(source, gains[0], shifts[0], cell_count, span_count), 0, span_count)
    hidden = causal_conv(first_hist[0], first_hist[1], first_in, kernels[0], biases[0], None, padded)
    second_in = with_rim(activate(hidden, gains[1], shifts[1], cell_count, span_count), 0, span_count)
    result = causal_conv(second_hist[0], second_hist[1], second_in, kernels[1], biases[1], source, padded)
    return (result, (first_hist[1], first_in), (second_hist[1], second_in))


def shards_whole(frames, causal_cache, conv_weight, conv_bias, norm_gain, norm_shift):
    phase_no = lax.axis_index("phase")
    phase_count = lax.axis_size("phase")
    peers = lax.axis_size("rows")
    frame_count, channels, rows_here, columns = frames.shape
    span = rows_here * peers
    half = span // 2
    core = lax.axis_index("rows") % 2
    start = lax.axis_index("rows") * rows_here
    forward = [(s, s + 1) for s in range(phase_count - 1)]
    frames_t = jnp.transpose(frames, (0, 2, 1, 3))
    cache_t = jnp.transpose(causal_cache[0], (0, 1, 3, 2, 4))
    early = lax.all_gather(jnp.stack([frames_t[0], cache_t[0, 0], cache_t[0, 1]]), "rows", axis=1, tiled=True)
    second_cache = lax.all_gather(cache_t[1], "rows", axis=1, tiled=True)
    later = list(frames_t[1:])
    if len(later) == 1:
        later = later * 2
    later = lax.all_gather(jnp.stack(later), "rows", axis=1, tiled=True) if later else early
    frame_of = [(early, 0)] + [(later, f) for f in range(frame_count - 1)]
    cache_of = ((early, (1, 2)), (second_cache, (0, 1)))
    taps = (arrange_taps(conv_weight[0, 0]), arrange_taps(conv_weight[0, 1]))

    def own_rows(x, rim=0):
        return lax.dynamic_slice_in_dim(x, start + rim, rows_here, axis=0)

    got = other = jnp.zeros((half, channels, columns), jnp.bfloat16)
    acts = ([], [])
    blank = jnp.zeros((rows_here, channels, columns), jnp.bfloat16)
    blank_frame = jnp.zeros((span + 2, channels, columns), jnp.bfloat16)
    produced = [blank] * frame_count
    kept = [[blank, blank], [blank, blank]]
    mode = jnp.where(phase_no == 0, 0, 1 + core)
    tick_count = frame_count + phase_count - 1
    frame_nos = jnp.arange(tick_count) - phase_no
    flags = jnp.stack(
        [frame_nos == 0, frame_nos == 1, jnp.full((tick_count,), mode), jnp.full((tick_count,), core)], axis=1
    ).astype(jnp.int32)
    for tick_no in range(tick_count):
        frame_no = tick_no - phase_no
        frame_stack, frame_at = frame_of[min(tick_no, frame_count - 1)]
        recents = []
        for j in range(2):
            a_p = acts[j][-1] if acts[j] else blank_frame
            a_pp = acts[j][-2] if len(acts[j]) > 1 else blank_frame
            recents.append((a_p, a_pp))
        common = (frame_stack, frame_at, (got, other))
        hidden, first_in = fused_conv(
            flags, tick_no, cache_of[0][0], cache_of[0][1], recents[0], *common,
            taps[0], conv_bias[0, 0], (norm_gain[0, 0], norm_shift[0, 0]), "first",
        )
        second = (flags, tick_no, cache_of[1][0], cache_of[1][1], recents[1], *common, taps[1], conv_bias[0, 1])
        if tick_no + 1 == tick_count:
            whole_out, second_in = fused_conv(*second, (norm_gain[0, 1], norm_shift[0, 1]), "all", hidden)
            lead = lax.dynamic_slice_in_dim(whole_out, core * half, half, axis=0)
            tail = lax.dynamic_slice_in_dim(whole_out, (1 - core) * half, half, axis=0)
        else:
            lead, second_in = fused_conv(*second, (norm_gain[0, 1], norm_shift[0, 1]), "lead", hidden)
            tail = fused_conv(*second, (norm_gain[0, 1], norm_shift[0, 1]), "tail", second_in)
        if tick_no + 1 < tick_count:
            got = lax.ppermute(lead, "phase", forward)
            got, tail = lax.optimization_barrier((got, tail))
            other = lax.ppermute(got, "rows", [(i, i ^ 1) for i in range(peers)])
        last = frame_no == frame_count - 1
        for j, a in enumerate((first_in, second_in)):
            stack, (_, k1) = cache_of[j]
            newer = jnp.where(frame_no == 0, own_rows(stack[k1]), own_rows(recents[j][0], 1))
            kept[j] = [jnp.where(last, newer, kept[j][0]), jnp.where(last, own_rows(a, 1), kept[j][1])]
            acts[j].append(a)
        mine = lax.dynamic_slice_in_dim(lead, start - core * half, rows_here, axis=0)
        theirs = lax.dynamic_slice_in_dim(tail, start - (1 - core) * half, rows_here, axis=0)
        result_rows = jnp.where(start // half == core, mine, theirs)
        for f in range(frame_count):
            if 0 <= tick_no - f < phase_count:
                produced[f] = jnp.where(frame_no == f, result_rows, produced[f])
    produced = jnp.transpose(jnp.stack(produced), (0, 2, 1, 3))
    new_cache = jnp.transpose(jnp.stack([jnp.stack(k) for k in kept]), (0, 1, 3, 2, 4))
    return (produced[None], new_cache[None])


def shards(frames, causal_cache, conv_weight, conv_bias, norm_gain, norm_shift):
    peers = lax.axis_size("rows")
    rows_here = frames.shape[2]
    if span_devices(peers, rows_here) == peers and (rows_here * peers) % 2 == 0:
        return shards_whole(frames, causal_cache, conv_weight, conv_bias, norm_gain, norm_shift)
    return shards_split(frames, causal_cache, conv_weight, conv_bias, norm_gain, norm_shift)


def shards_split(frames, causal_cache, conv_weight, conv_bias, norm_gain, norm_shift):
    phase_no = lax.axis_index("phase")
    phase_count = lax.axis_size("phase")
    peers = lax.axis_size("rows")
    frame_count = frames.shape[0]
    channels = frames.shape[1]
    rows_here = frames.shape[2]
    columns = frames.shape[3]
    span_count = span_devices(peers, rows_here)
    span = rows_here * span_count
    cell_count = float(channels // GROUPS * rows_here * peers * columns)
    padded = span_count != peers
    frames_t = jnp.transpose(frames, (0, 2, 1, 3))
    cache_t = jnp.transpose(causal_cache[0], (0, 1, 3, 2, 4))
    early = gather_span(jnp.stack([frames_t[0], cache_t[0, 0], cache_t[0, 1]]), 1, span_count)
    late = gather_span(jnp.stack([cache_t[1, 0], cache_t[1, 1]] + list(frames_t[1:])), 1, span_count)
    frames_span = [early[0]] + [late[2 + f] for f in range(frame_count - 1)]
    first_hist = tuple(with_rim(early[1 + k], 0, span_count) for k in range(2))
    second_hist = tuple(with_rim(late[k], 0, span_count) for k in range(2))
    local_taps = (arrange_taps(conv_weight[0, 0]), arrange_taps(conv_weight[0, 1]))
    incoming = jnp.zeros_like(frames_span[0])
    produced = [jnp.zeros_like(frames_span[0]) for _ in range(frame_count)]
    tick_count = frame_count + phase_count - 1
    for tick_no in range(tick_count):
        frame_no = tick_no - phase_no
        active_now = jnp.logical_and(frame_no >= 0, frame_no < frame_count)
        source = jnp.where(phase_no == 0, frames_span[min(tick_no, frame_count - 1)], incoming)
        result, first_next, second_next = run_frame(
            source, first_hist, second_hist, local_taps, conv_bias[0], norm_gain[0], norm_shift[0],
            cell_count, span_count,
        )
        first_hist = tuple(jnp.where(active_now, a, b) for a, b in zip(first_next, first_hist))
        second_hist = tuple(jnp.where(active_now, a, b) for a, b in zip(second_next, second_hist))
        for f in range(frame_count):
            if 0 <= tick_no - f < phase_count:
                produced[f] = jnp.where(frame_no == f, result, produced[f])
        if tick_no + 1 < tick_count:
            incoming = pass_on(result, span_count)
    start = (lax.axis_index("rows") % span_count) * rows_here
    rim = 1 if padded else 0
    produced = jnp.stack([lax.dynamic_slice_in_dim(p, start, rows_here, axis=0) for p in produced])
    new_cache = jnp.stack(
        [
            jnp.stack([lax.dynamic_slice_in_dim(h, start + rim, rows_here, axis=0) for h in hist])
            for hist in (first_hist, second_hist)
        ]
    )
    produced = jnp.transpose(produced, (0, 2, 1, 3))
    new_cache = jnp.transpose(new_cache, (0, 1, 3, 2, 4))
    return (produced[None], new_cache[None])


def solution(mesh):
    in_specs = (
        P(None, None, "rows", None),
        P("phase", None, None, None, "rows", None),
        P("phase", None, None, None, None, None, None),
        P("phase", None, None),
        P("phase", None, None),
        P("phase", None, None),
    )
    out_specs = (P("phase", None, None, "rows", None), P("phase", None, None, None, "rows", None))
    return jax.shard_map(shards, mesh=mesh, in_specs=in_specs, out_specs=out_specs, check_vma=False)
```

```python
import jax
import jax.numpy as jnp
from jax import lax
from jax.sharding import PartitionSpec as P
from jax.experimental import pallas as pl
from jax.experimental.pallas import tpu as pltpu
import functools

GROUPS = 32
EPS = 1e-06
MAX_SPAN = 16


def span_devices(peers, rows_here):
    count = 1
    while count * 2 <= peers and peers % (count * 2) == 0 and count * 2 * rows_here <= MAX_SPAN:
        count *= 2
    return count


def gather_span(array, dim, span_count):
    if span_count == 1:
        return array
    peers = lax.axis_size("rows")
    if span_count == peers:
        return lax.all_gather(array, "rows", axis=dim, tiled=True)
    place = lax.axis_index("rows") % span_count
    pieces = [array]
    for shift in range(1, span_count):
        pairs = [
            (b * span_count + p, b * span_count + (p + shift) % span_count)
            for b in range(peers // span_count)
            for p in range(span_count)
        ]
        pieces.append(lax.ppermute(array, "rows", pairs))
    stacked = jnp.stack(pieces)
    order = (place - jnp.arange(span_count)) % span_count
    picked = jnp.take(stacked, order, axis=0)
    picked = jnp.moveaxis(picked, 0, dim)
    shape = list(array.shape)
    shape[dim] = shape[dim] * span_count
    return picked.reshape(shape)


def with_rim(array, dim, span_count):
    peers = lax.axis_size("rows")
    length = array.shape[dim]
    if span_count == peers:
        return array
    up = [(i, i + span_count) for i in range(peers - span_count)]
    down = [(j, i) for i, j in up]
    last = lax.slice_in_dim(array, length - 1, length, axis=dim)
    leading = lax.slice_in_dim(array, 0, 1, axis=dim)
    before = lax.ppermute(last, "rows", up)
    after = lax.ppermute(leading, "rows", down)
    return jnp.concatenate([before, array, after], axis=dim)


def pass_on(result, span_count):
    phase_count = lax.axis_size("phase")
    forward = [(s, s + 1) for s in range(phase_count - 1)]
    length = result.shape[0]
    if span_count % 2 or length % 2:
        return lax.ppermute(result, "phase", forward)
    peers = lax.axis_size("rows")
    half = length // 2
    core = lax.axis_index("rows") % 2
    mine = lax.dynamic_slice_in_dim(result, core * half, half, axis=0)
    got = lax.ppermute(mine, "phase", forward)
    other = lax.ppermute(got, "rows", [(i, i ^ 1) for i in range(peers)])
    return jnp.where(core == 0, jnp.concatenate([got, other]), jnp.concatenate([other, got]))


def arrange_taps(weight):
    outputs = weight.shape[3]
    channels = weight.shape[4]
    return jnp.transpose(weight, (2, 3, 0, 1, 4)).reshape(3 * outputs, 9 * channels)


def conv_rows(x0, x1, x2, taps, bias, res, out, rows_out, padded):
    outputs = out.shape[1]
    channels = x0.shape[1]
    columns = x0.shape[2]
    pair = 4 if rows_out % 4 == 0 else (2 if rows_out % 2 == 0 else 1)
    lanes = pair * columns
    lane = lax.broadcasted_iota(jnp.int32, (outputs, lanes), 1) % columns
    frames = (x0, x1, x2)

    def column(r):
        if padded or 0 < r < rows_out - 1:
            base = r if padded else r - 1
            parts = [x[pl.ds(base, 3)] for x in frames]
            return jnp.concatenate(parts, axis=0).reshape(9 * channels, columns)
        zero = jnp.zeros((1, channels, columns), x0.dtype)
        parts = []
        for x in frames:
            for dy in range(3):
                q = r + dy - 1
                parts.append(zero if q < 0 or q >= rows_out else x[pl.ds(q, 1)])
        return jnp.concatenate(parts, axis=0).reshape(9 * channels, columns)

    for r in range(0, rows_out, pair):
        cols = [column(r + k) for k in range(pair)]
        rhs = cols[0] if pair == 1 else jnp.concatenate(cols, axis=1)
        acc = jnp.dot(taps[...], rhs, preferred_element_type=jnp.float32)
        left = pltpu.roll(acc[:outputs], 1, 1)
        right = pltpu.roll(acc[2 * outputs :], lanes - 1, 1)
        total = acc[outputs : 2 * outputs] + jnp.where(lane == 0, 0.0, left)
        total = total + jnp.where(lane == columns - 1, 0.0, right) + bias[...]
        for k in range(pair):
            piece = total[:, k * columns : (k + 1) * columns]
            if res is not None:
                piece = piece + res[r + k].astype(jnp.float32)
            out[r + k] = piece.astype(out.dtype)


def conv_body(x0, x1, x2, taps, bias, *rest, rows_out, with_res, padded):
    res = rest[0] if with_res else None
    conv_rows(x0, x1, x2, taps, bias, res, rest[-1], rows_out, padded)


def causal_conv(x0, x1, x2, taps, bias_vec, res, padded):
    rows_out = x0.shape[0] - 2 if padded else x0.shape[0]
    outputs = taps.shape[0] // 3
    args = [x0, x1, x2, taps, bias_vec.reshape(outputs, 1)]
    if res is not None:
        args.append(res)
    body = functools.partial(conv_body, rows_out=rows_out, with_res=res is not None, padded=padded)
    shape = jax.ShapeDtypeStruct((rows_out, outputs, x0.shape[2]), jnp.bfloat16)
    return pl.pallas_call(body, out_shape=shape)(*args)


def conv_span(x0, x1, x2, taps, bias, res, out, base, count):
    outputs = out.shape[1]
    channels = x0.shape[1]
    columns = x0.shape[2]
    pair = next(p for p in (16, 8, 4, 2, 1) if count % p == 0)
    lanes = pair * columns
    lane = lax.broadcasted_iota(jnp.int32, (outputs, lanes), 1) % columns

    def step(i, carry):
        r = base + i * pair
        cols = []
        for k in range(pair):
            parts = [x[pl.ds(r + k, 3)] for x in (x0, x1, x2)]
            cols.append(jnp.concatenate(parts, axis=0).reshape(9 * channels, columns))
        rhs = cols[0] if pair == 1 else jnp.concatenate(cols, axis=1)
        acc = jnp.dot(taps[...], rhs, preferred_element_type=jnp.float32)
        left = pltpu.roll(acc[:outputs], 1, 1)
        right = pltpu.roll(acc[2 * outputs :], lanes - 1, 1)
        total = acc[outputs : 2 * outputs] + jnp.where(lane == 0, 0.0, left)
        total = total + jnp.where(lane == columns - 1, 0.0, right) + bias[...]
        for k in range(pair):
            piece = total[:, k * columns : (k + 1) * columns]
            if res is not None:
                piece = piece + res[r + k].astype(jnp.float32)
            out[i * pair + k] = piece.astype(out.dtype)
        return carry

    lax.fori_loop(0, count // pair, step, 0)


def fused_body(flags, caches, a_p, a_pp, frames, src_b, src_c, taps, bias, member, gain, shift, *rest,
               kind, tick, frame_at, cache_at):
    rest = list(rest)
    own = rest.pop(0) if kind != "first" else None
    if kind == "tail":
        out, x0, x1, rawbuf, tapbuf, sems = rest
        act = own
    else:
        out, act, x0, x1, rawbuf, tapbuf, sems = rest
    span, channels, columns = rawbuf.shape
    half = span // 2
    first, second, mode, core = flags[tick, 0], flags[tick, 1], flags[tick, 2], flags[tick, 3]
    c0, c1 = caches.at[cache_at[0]], caches.at[cache_at[1]]
    whole = frames.at[frame_at]
    top, bottom = rawbuf.at[pl.ds(0, half)], rawbuf.at[pl.ds(half, half)]
    inner0, inner1 = x0.at[pl.ds(1, span)], x1.at[pl.ds(1, span)]

    def inner(x):
        return x.at[pl.ds(1, span)]

    def begin(pairs, base):
        for i, (a, b) in enumerate(pairs):
            pltpu.make_async_copy(a, b, sems.at[base + i]).start()

    def finish(pairs, base):
        for i, (a, b) in enumerate(pairs):
            pltpu.make_async_copy(a, b, sems.at[base + i]).wait()

    pltpu.make_async_copy(taps, tapbuf, sems.at[4]).start()

    @pl.when(mode == 0)
    def _():
        begin([(whole.at[pl.ds(0, half)], top), (whole.at[pl.ds(half, half)], bottom)], 0)

    @pl.when(mode == 1)
    def _():
        begin([(src_b, top), (src_c, bottom)], 0)

    @pl.when(mode == 2)
    def _():
        begin([(src_c, top), (src_b, bottom)], 0)

    @pl.when(first == 1)
    def _():
        begin([(c0, inner0), (c1, inner1)], 2)

    @pl.when(jnp.logical_and(first == 0, second == 1))
    def _():
        begin([(c1, inner0), (inner(a_p), inner1)], 2)

    @pl.when(jnp.logical_and(first == 0, second == 0))
    def _():
        begin([(inner(a_pp), inner0), (inner(a_p), inner1)], 2)

    zero = jnp.zeros((channels, columns), x0.dtype)
    for x in (x0, x1):
        x[0] = zero
        x[span + 1] = zero
    source_copies = [(src_b, top), (src_c, bottom)]
    history_copies = [(inner(a_pp), inner0), (inner(a_p), inner1)]

    if kind != "tail":
        if kind == "first":
            finish(source_copies, 0)
            raw = rawbuf
        else:
            raw = own
        count = float(span * columns * (channels // GROUPS))

        def group_total(acc):
            spread = jnp.dot(member[...], acc, precision=lax.Precision.HIGHEST, preferred_element_type=jnp.float32)
            return jnp.sum(spread, axis=1, keepdims=True)

        acc = raw[0].astype(jnp.float32)
        for r in range(1, span):
            acc = acc + raw[r].astype(jnp.float32)
        average = group_total(acc) / count
        acc = jnp.square(raw[0].astype(jnp.float32) - average)
        for r in range(1, span):
            acc = acc + jnp.square(raw[r].astype(jnp.float32) - average)
        inverse = lax.rsqrt(group_total(acc) / count + EPS)
        act[0] = zero
        act[span + 1] = zero
        for r in range(span):
            value = (raw[r].astype(jnp.float32) - average) * inverse
            value = value * gain[...] + shift[...]
            act[r + 1] = (value / (1.0 + jnp.exp(-value))).astype(act.dtype)

    finish(history_copies, 2)
    pltpu.make_async_copy(taps, tapbuf, sems.at[4]).wait()
    taps = tapbuf
    if kind == "first":
        conv_span(x0, x1, act, taps, bias, None, out, 0, span)
    elif kind == "all":
        finish(source_copies, 0)
        conv_span(x0, x1, act, taps, bias, rawbuf, out, 0, span)
    else:
        finish(source_copies, 0)
        base = core * half if kind == "lead" else (1 - core) * half
        conv_span(x0, x1, act, taps, bias, rawbuf, out, base, half)


def fused_conv(flags, tick, caches, cache_at, recent, frames, frame_at, halves, taps, bias_vec, norm, kind, own=None):
    span, channels, columns = caches.shape[1:]
    outputs = taps.shape[0] // 3
    group_of = jnp.arange(channels) // (channels // GROUPS)
    member = (group_of[:, None] == group_of[None, :]).astype(jnp.float32)
    vmem = pl.BlockSpec(memory_space=pltpu.VMEM)
    anywhere = pl.BlockSpec(memory_space=pl.ANY)
    args = [flags, caches, recent[0], recent[1], frames, halves[0], halves[1]]
    args += [taps, bias_vec.reshape(outputs, 1), member]
    args += [v.reshape(-1, 1).astype(jnp.float32) for v in norm]
    specs = [pl.BlockSpec(memory_space=pltpu.SMEM)] + [anywhere] * 7 + [vmem] * 4
    if own is not None:
        args.append(own)
        specs.append(vmem)
    rows_out = span if kind in ("first", "all") else span // 2
    result = jax.ShapeDtypeStruct((rows_out, outputs, columns), jnp.bfloat16)
    padded = jax.ShapeDtypeStruct((span + 2, channels, columns), jnp.bfloat16)
    shapes = result if kind == "tail" else (result, padded)
    body = functools.partial(
        fused_body, kind=kind, tick=tick, frame_at=frame_at, cache_at=tuple(cache_at)
    )
    return pl.pallas_call(
        body,
        out_shape=shapes,
        in_specs=specs,
        out_specs=vmem if kind == "tail" else (vmem, vmem),
        scratch_shapes=[
            pltpu.VMEM((span + 2, channels, columns), jnp.bfloat16),
            pltpu.VMEM((span + 2, channels, columns), jnp.bfloat16),
            pltpu.VMEM((span, channels, columns), jnp.bfloat16),
            pltpu.VMEM(taps.shape, taps.dtype),
            pltpu.SemaphoreType.DMA((5,)),
        ],
    )(*args)


def block_sum(values, span_count):
    peers = lax.axis_size("rows")
    if span_count == peers:
        return values
    lead = (lax.axis_index("rows") % span_count == 0).astype(values.dtype)
    return lax.psum(values * lead, "rows")


def activate(source, gain_vec, shift_vec, cell_count, span_count):
    height, channels, columns = source.shape
    grouped = source.astype(jnp.float32).reshape(height, GROUPS, channels // GROUPS, columns)
    average = block_sum(jnp.sum(grouped, axis=(0, 2, 3)), span_count) / cell_count
    centred = grouped - average[None, :, None, None]
    spread = block_sum(jnp.sum(centred * centred, axis=(0, 2, 3)), span_count) / cell_count
    inverse = lax.rsqrt(spread + EPS)
    normed = (centred * inverse[None, :, None, None]).reshape(height, channels, columns)
    normed = normed * gain_vec[None, :, None] + shift_vec[None, :, None]
    return jax.nn.silu(normed).astype(jnp.bfloat16)


def run_frame(source, first_hist, second_hist, kernels, biases, gains, shifts, cell_count, span_count):
    padded = span_count != lax.axis_size("rows")
    first_in = with_rim(activate(source, gains[0], shifts[0], cell_count, span_count), 0, span_count)
    hidden = causal_conv(first_hist[0], first_hist[1], first_in, kernels[0], biases[0], None, padded)
    second_in = with_rim(activate(hidden, gains[1], shifts[1], cell_count, span_count), 0, span_count)
    result = causal_conv(second_hist[0], second_hist[1], second_in, kernels[1], biases[1], source, padded)
    return (result, (first_hist[1], first_in), (second_hist[1], second_in))


def shards_whole(frames, causal_cache, conv_weight, conv_bias, norm_gain, norm_shift):
    phase_no = lax.axis_index("phase")
    phase_count = lax.axis_size("phase")
    peers = lax.axis_size("rows")
    frame_count, channels, rows_here, columns = frames.shape
    span = rows_here * peers
    half = span // 2
    core = lax.axis_index("rows") % 2
    start = lax.axis_index("rows") * rows_here
    forward = [(s, s + 1) for s in range(phase_count - 1)]
    frames_t = jnp.transpose(frames, (0, 2, 1, 3))
    cache_t = jnp.transpose(causal_cache[0], (0, 1, 3, 2, 4))
    early = lax.all_gather(jnp.stack([frames_t[0], cache_t[0, 0], cache_t[0, 1]]), "rows", axis=1, tiled=True)
    second_cache = lax.all_gather(cache_t[1], "rows", axis=1, tiled=True)
    later = list(frames_t[1:])
    if len(later) == 1:
        later = later * 2
    later = lax.all_gather(jnp.stack(later), "rows", axis=1, tiled=True) if later else early
    frame_of = [(early, 0)] + [(later, f) for f in range(frame_count - 1)]
    cache_of = ((early, (1, 2)), (second_cache, (0, 1)))
    taps = (arrange_taps(conv_weight[0, 0]), arrange_taps(conv_weight[0, 1]))

    def own_rows(x, rim=0):
        return lax.dynamic_slice_in_dim(x, start + rim, rows_here, axis=0)

    got = other = jnp.zeros((half, channels, columns), jnp.bfloat16)
    acts = ([], [])
    blank = jnp.zeros((rows_here, channels, columns), jnp.bfloat16)
    blank_frame = jnp.zeros((span + 2, channels, columns), jnp.bfloat16)
    produced = [blank] * frame_count
    kept = [[blank, blank], [blank, blank]]
    mode = jnp.where(phase_no == 0, 0, 1 + core)
    tick_count = frame_count + phase_count - 1
    frame_nos = jnp.arange(tick_count) - phase_no
    flags = jnp.stack(
        [frame_nos == 0, frame_nos == 1, jnp.full((tick_count,), mode), jnp.full((tick_count,), core)], axis=1
    ).astype(jnp.int32)
    for tick_no in range(tick_count):
        frame_no = tick_no - phase_no
        frame_stack, frame_at = frame_of[min(tick_no, frame_count - 1)]
        recents = []
        for j in range(2):
            a_p = acts[j][-1] if acts[j] else blank_frame
            a_pp = acts[j][-2] if len(acts[j]) > 1 else blank_frame
            recents.append((a_p, a_pp))
        common = (frame_stack, frame_at, (got, other))
        hidden, first_in = fused_conv(
            flags, tick_no, cache_of[0][0], cache_of[0][1], recents[0], *common,
            taps[0], conv_bias[0, 0], (norm_gain[0, 0], norm_shift[0, 0]), "first",
        )
        second = (flags, tick_no, cache_of[1][0], cache_of[1][1], recents[1], *common, taps[1], conv_bias[0, 1])
        if tick_no + 1 == tick_count:
            whole_out, second_in = fused_conv(*second, (norm_gain[0, 1], norm_shift[0, 1]), "all", hidden)
            lead = lax.dynamic_slice_in_dim(whole_out, core * half, half, axis=0)
            tail = lax.dynamic_slice_in_dim(whole_out, (1 - core) * half, half, axis=0)
        else:
            lead, second_in = fused_conv(*second, (norm_gain[0, 1], norm_shift[0, 1]), "lead", hidden)
            tail = fused_conv(*second, (norm_gain[0, 1], norm_shift[0, 1]), "tail", second_in)
        if tick_no + 1 < tick_count:
            got = lax.ppermute(lead, "phase", forward)
            got, tail = lax.optimization_barrier((got, tail))
            other = lax.ppermute(got, "rows", [(i, i ^ 1) for i in range(peers)])
        last = frame_no == frame_count - 1
        for j, a in enumerate((first_in, second_in)):
            stack, (_, k1) = cache_of[j]
            newer = jnp.where(frame_no == 0, own_rows(stack[k1]), own_rows(recents[j][0], 1))
            kept[j] = [jnp.where(last, newer, kept[j][0]), jnp.where(last, own_rows(a, 1), kept[j][1])]
            acts[j].append(a)
        mine = lax.dynamic_slice_in_dim(lead, start - core * half, rows_here, axis=0)
        theirs = lax.dynamic_slice_in_dim(tail, start - (1 - core) * half, rows_here, axis=0)
        result_rows = jnp.where(start // half == core, mine, theirs)
        for f in range(frame_count):
            if 0 <= tick_no - f < phase_count:
                produced[f] = jnp.where(frame_no == f, result_rows, produced[f])
    produced = jnp.transpose(jnp.stack(produced), (0, 2, 1, 3))
    new_cache = jnp.transpose(jnp.stack([jnp.stack(k) for k in kept]), (0, 1, 3, 2, 4))
    return (produced[None], new_cache[None])


def shards(frames, causal_cache, conv_weight, conv_bias, norm_gain, norm_shift):
    peers = lax.axis_size("rows")
    rows_here = frames.shape[2]
    if span_devices(peers, rows_here) == peers and (rows_here * peers) % 2 == 0:
        return shards_whole(frames, causal_cache, conv_weight, conv_bias, norm_gain, norm_shift)
    return shards_split(frames, causal_cache, conv_weight, conv_bias, norm_gain, norm_shift)


def shards_split(frames, causal_cache, conv_weight, conv_bias, norm_gain, norm_shift):
    phase_no = lax.axis_index("phase")
    phase_count = lax.axis_size("phase")
    peers = lax.axis_size("rows")
    frame_count = frames.shape[0]
    channels = frames.shape[1]
    rows_here = frames.shape[2]
    columns = frames.shape[3]
    span_count = span_devices(peers, rows_here)
    span = rows_here * span_count
    cell_count = float(channels // GROUPS * rows_here * peers * columns)
    padded = span_count != peers
    frames_t = jnp.transpose(frames, (0, 2, 1, 3))
    cache_t = jnp.transpose(causal_cache[0], (0, 1, 3, 2, 4))
    early = gather_span(jnp.stack([frames_t[0], cache_t[0, 0], cache_t[0, 1]]), 1, span_count)
    late = gather_span(jnp.stack([cache_t[1, 0], cache_t[1, 1]] + list(frames_t[1:])), 1, span_count)
    frames_span = [early[0]] + [late[2 + f] for f in range(frame_count - 1)]
    first_hist = tuple(with_rim(early[1 + k], 0, span_count) for k in range(2))
    second_hist = tuple(with_rim(late[k], 0, span_count) for k in range(2))
    local_taps = (arrange_taps(conv_weight[0, 0]), arrange_taps(conv_weight[0, 1]))
    incoming = jnp.zeros_like(frames_span[0])
    produced = [jnp.zeros_like(frames_span[0]) for _ in range(frame_count)]
    tick_count = frame_count + phase_count - 1
    for tick_no in range(tick_count):
        frame_no = tick_no - phase_no
        active_now = jnp.logical_and(frame_no >= 0, frame_no < frame_count)
        source = jnp.where(phase_no == 0, frames_span[min(tick_no, frame_count - 1)], incoming)
        result, first_next, second_next = run_frame(
            source, first_hist, second_hist, local_taps, conv_bias[0], norm_gain[0], norm_shift[0],
            cell_count, span_count,
        )
        first_hist = tuple(jnp.where(active_now, a, b) for a, b in zip(first_next, first_hist))
        second_hist = tuple(jnp.where(active_now, a, b) for a, b in zip(second_next, second_hist))
        for f in range(frame_count):
            if 0 <= tick_no - f < phase_count:
                produced[f] = jnp.where(frame_no == f, result, produced[f])
        if tick_no + 1 < tick_count:
            incoming = pass_on(result, span_count)
    start = (lax.axis_index("rows") % span_count) * rows_here
    rim = 1 if padded else 0
    produced = jnp.stack([lax.dynamic_slice_in_dim(p, start, rows_here, axis=0) for p in produced])
    new_cache = jnp.stack(
        [
            jnp.stack([lax.dynamic_slice_in_dim(h, start + rim, rows_here, axis=0) for h in hist])
            for hist in (first_hist, second_hist)
        ]
    )
    produced = jnp.transpose(produced, (0, 2, 1, 3))
    new_cache = jnp.transpose(new_cache, (0, 1, 3, 2, 4))
    return (produced[None], new_cache[None])


def solution(mesh):
    in_specs = (
        P(None, None, "rows", None),
        P("phase", None, None, None, "rows", None),
        P("phase", None, None, None, None, None, None),
        P("phase", None, None),
        P("phase", None, None),
        P("phase", None, None),
    )
    out_specs = (P("phase", None, None, "rows", None), P("phase", None, None, None, "rows", None))
    return jax.shard_map(shards, mesh=mesh, in_specs=in_specs, out_specs=out_specs, check_vma=False)
```

```python
import jax
import jax.numpy as jnp
from jax import lax
from jax.sharding import PartitionSpec as P
from jax.experimental import pallas as pl
from jax.experimental.pallas import tpu as pltpu
import functools

GROUPS = 32
EPS = 1e-06
MAX_SPAN = 16


def span_devices(peers, rows_here):
    count = 1
    while count * 2 <= peers and peers % (count * 2) == 0 and count * 2 * rows_here <= MAX_SPAN:
        count *= 2
    return count


def gather_span(array, dim, span_count):
    if span_count == 1:
        return array
    peers = lax.axis_size("rows")
    if span_count == peers:
        return lax.all_gather(array, "rows", axis=dim, tiled=True)
    place = lax.axis_index("rows") % span_count
    pieces = [array]
    for shift in range(1, span_count):
        pairs = [
            (b * span_count + p, b * span_count + (p + shift) % span_count)
            for b in range(peers // span_count)
            for p in range(span_count)
        ]
        pieces.append(lax.ppermute(array, "rows", pairs))
    stacked = jnp.stack(pieces)
    order = (place - jnp.arange(span_count)) % span_count
    picked = jnp.take(stacked, order, axis=0)
    picked = jnp.moveaxis(picked, 0, dim)
    shape = list(array.shape)
    shape[dim] = shape[dim] * span_count
    return picked.reshape(shape)


def with_rim(array, dim, span_count):
    peers = lax.axis_size("rows")
    length = array.shape[dim]
    if span_count == peers:
        return array
    up = [(i, i + span_count) for i in range(peers - span_count)]
    down = [(j, i) for i, j in up]
    last = lax.slice_in_dim(array, length - 1, length, axis=dim)
    leading = lax.slice_in_dim(array, 0, 1, axis=dim)
    before = lax.ppermute(last, "rows", up)
    after = lax.ppermute(leading, "rows", down)
    return jnp.concatenate([before, array, after], axis=dim)


def pass_on(result, span_count):
    phase_count = lax.axis_size("phase")
    forward = [(s, s + 1) for s in range(phase_count - 1)]
    length = result.shape[0]
    if span_count % 2 or length % 2:
        return lax.ppermute(result, "phase", forward)
    peers = lax.axis_size("rows")
    half = length // 2
    core = lax.axis_index("rows") % 2
    mine = lax.dynamic_slice_in_dim(result, core * half, half, axis=0)
    got = lax.ppermute(mine, "phase", forward)
    other = lax.ppermute(got, "rows", [(i, i ^ 1) for i in range(peers)])
    return jnp.where(core == 0, jnp.concatenate([got, other]), jnp.concatenate([other, got]))


def arrange_taps(weight):
    outputs = weight.shape[3]
    channels = weight.shape[4]
    return jnp.transpose(weight, (2, 3, 0, 1, 4)).reshape(3 * outputs, 9 * channels)


def conv_rows(x0, x1, x2, taps, bias, res, out, rows_out, padded):
    outputs = out.shape[1]
    channels = x0.shape[1]
    columns = x0.shape[2]
    pair = 4 if rows_out % 4 == 0 else (2 if rows_out % 2 == 0 else 1)
    lanes = pair * columns
    lane = lax.broadcasted_iota(jnp.int32, (outputs, lanes), 1) % columns
    frames = (x0, x1, x2)

    def column(r):
        if padded or 0 < r < rows_out - 1:
            base = r if padded else r - 1
            parts = [x[pl.ds(base, 3)] for x in frames]
            return jnp.concatenate(parts, axis=0).reshape(9 * channels, columns)
        zero = jnp.zeros((1, channels, columns), x0.dtype)
        parts = []
        for x in frames:
            for dy in range(3):
                q = r + dy - 1
                parts.append(zero if q < 0 or q >= rows_out else x[pl.ds(q, 1)])
        return jnp.concatenate(parts, axis=0).reshape(9 * channels, columns)

    for r in range(0, rows_out, pair):
        cols = [column(r + k) for k in range(pair)]
        rhs = cols[0] if pair == 1 else jnp.concatenate(cols, axis=1)
        acc = jnp.dot(taps[...], rhs, preferred_element_type=jnp.float32)
        left = pltpu.roll(acc[:outputs], 1, 1)
        right = pltpu.roll(acc[2 * outputs :], lanes - 1, 1)
        total = acc[outputs : 2 * outputs] + jnp.where(lane == 0, 0.0, left)
        total = total + jnp.where(lane == columns - 1, 0.0, right) + bias[...]
        for k in range(pair):
            piece = total[:, k * columns : (k + 1) * columns]
            if res is not None:
                piece = piece + res[r + k].astype(jnp.float32)
            out[r + k] = piece.astype(out.dtype)


def conv_body(x0, x1, x2, taps, bias, *rest, rows_out, with_res, padded):
    res = rest[0] if with_res else None
    conv_rows(x0, x1, x2, taps, bias, res, rest[-1], rows_out, padded)


def causal_conv(x0, x1, x2, taps, bias_vec, res, padded):
    rows_out = x0.shape[0] - 2 if padded else x0.shape[0]
    outputs = taps.shape[0] // 3
    args = [x0, x1, x2, taps, bias_vec.reshape(outputs, 1)]
    if res is not None:
        args.append(res)
    body = functools.partial(conv_body, rows_out=rows_out, with_res=res is not None, padded=padded)
    shape = jax.ShapeDtypeStruct((rows_out, outputs, x0.shape[2]), jnp.bfloat16)
    return pl.pallas_call(body, out_shape=shape)(*args)


def conv_span(x0, x1, x2, taps, bias, res, out, base, count):
    outputs = out.shape[1]
    channels = x0.shape[1]
    columns = x0.shape[2]
    pair = next(p for p in (16, 8, 4, 2, 1) if count % p == 0)
    lanes = pair * columns
    lane = lax.broadcasted_iota(jnp.int32, (outputs, lanes), 1) % columns

    def step(i, carry):
        r = base + i * pair
        cols = []
        for k in range(pair):
            parts = [x[pl.ds(r + k, 3)] for x in (x0, x1, x2)]
            cols.append(jnp.concatenate(parts, axis=0).reshape(9 * channels, columns))
        rhs = cols[0] if pair == 1 else jnp.concatenate(cols, axis=1)
        acc = jnp.dot(taps[...], rhs, preferred_element_type=jnp.float32)
        left = pltpu.roll(acc[:outputs], 1, 1)
        right = pltpu.roll(acc[2 * outputs :], lanes - 1, 1)
        total = acc[outputs : 2 * outputs] + jnp.where(lane == 0, 0.0, left)
        total = total + jnp.where(lane == columns - 1, 0.0, right) + bias[...]
        for k in range(pair):
            piece = total[:, k * columns : (k + 1) * columns]
            if res is not None:
                piece = piece + res[r + k].astype(jnp.float32)
            out[i * pair + k] = piece.astype(out.dtype)
        return carry

    lax.fori_loop(0, count // pair, step, 0)


def fused_body(flags, caches, a_p, a_pp, frames, src_b, src_c, taps, bias, member, gain, shift, *rest,
               kind, tick, frame_at, cache_at):
    rest = list(rest)
    own = rest.pop(0) if kind != "first" else None
    if kind == "tail":
        out, x0, x1, rawbuf, tapbuf, sems = rest
        act = own
    else:
        out, act, x0, x1, rawbuf, tapbuf, sems = rest
    span, channels, columns = rawbuf.shape
    half = span // 2
    first, second, mode, core = flags[tick, 0], flags[tick, 1], flags[tick, 2], flags[tick, 3]
    c0, c1 = caches.at[cache_at[0]], caches.at[cache_at[1]]
    whole = frames.at[frame_at]
    top, bottom = rawbuf.at[pl.ds(0, half)], rawbuf.at[pl.ds(half, half)]
    inner0, inner1 = x0.at[pl.ds(1, span)], x1.at[pl.ds(1, span)]

    def inner(x):
        return x.at[pl.ds(1, span)]

    def begin(pairs, base):
        for i, (a, b) in enumerate(pairs):
            pltpu.make_async_copy(a, b, sems.at[base + i]).start()

    def finish(pairs, base):
        for i, (a, b) in enumerate(pairs):
            pltpu.make_async_copy(a, b, sems.at[base + i]).wait()

    pltpu.make_async_copy(taps, tapbuf, sems.at[4]).start()

    if kind in ("lead", "tail"):
        part = core * half if kind == "lead" else (1 - core) * half
        mine = rawbuf.at[pl.ds(part, half)]
        source_copies = [(src_b, mine)]

        @pl.when(mode == 0)
        def _():
            begin([(whole.at[pl.ds(part, half)], mine)], 0)

        @pl.when(mode != 0)
        def _():
            begin([(src_b if kind == "lead" else src_c, mine)], 0)

    else:
        source_copies = [(src_b, top), (src_c, bottom)]

        @pl.when(mode == 0)
        def _():
            begin([(whole.at[pl.ds(0, half)], top), (whole.at[pl.ds(half, half)], bottom)], 0)

        @pl.when(mode == 1)
        def _():
            begin([(src_b, top), (src_c, bottom)], 0)

        @pl.when(mode == 2)
        def _():
            begin([(src_c, top), (src_b, bottom)], 0)

    @pl.when(first == 1)
    def _():
        begin([(c0, inner0), (c1, inner1)], 2)

    @pl.when(jnp.logical_and(first == 0, second == 1))
    def _():
        begin([(c1, inner0), (inner(a_p), inner1)], 2)

    @pl.when(jnp.logical_and(first == 0, second == 0))
    def _():
        begin([(inner(a_pp), inner0), (inner(a_p), inner1)], 2)

    zero = jnp.zeros((channels, columns), x0.dtype)
    for x in (x0, x1):
        x[0] = zero
        x[span + 1] = zero
    history_copies = [(inner(a_pp), inner0), (inner(a_p), inner1)]

    if kind != "tail":
        if kind == "first":
            finish(source_copies, 0)
            raw = rawbuf
        else:
            raw = own
        count = float(span * columns * (channels // GROUPS))

        def group_total(acc):
            spread = jnp.dot(member[...], acc, precision=lax.Precision.HIGHEST, preferred_element_type=jnp.float32)
            return jnp.sum(spread, axis=1, keepdims=True)

        acc = raw[0].astype(jnp.float32)
        for r in range(1, span):
            acc = acc + raw[r].astype(jnp.float32)
        average = group_total(acc) / count
        acc = jnp.square(raw[0].astype(jnp.float32) - average)
        for r in range(1, span):
            acc = acc + jnp.square(raw[r].astype(jnp.float32) - average)
        inverse = lax.rsqrt(group_total(acc) / count + EPS)
        act[0] = zero
        act[span + 1] = zero
        for r in range(span):
            value = (raw[r].astype(jnp.float32) - average) * inverse
            value = value * gain[...] + shift[...]
            act[r + 1] = (value / (1.0 + jnp.exp(-value))).astype(act.dtype)

    finish(history_copies, 2)
    pltpu.make_async_copy(taps, tapbuf, sems.at[4]).wait()
    taps = tapbuf
    if kind == "first":
        conv_span(x0, x1, act, taps, bias, None, out, 0, span)
    elif kind == "all":
        finish(source_copies, 0)
        conv_span(x0, x1, act, taps, bias, rawbuf, out, 0, span)
    else:
        finish(source_copies, 0)
        base = core * half if kind == "lead" else (1 - core) * half
        conv_span(x0, x1, act, taps, bias, rawbuf, out, base, half)


def fused_conv(flags, tick, caches, cache_at, recent, frames, frame_at, halves, taps, bias_vec, norm, kind, own=None):
    span, channels, columns = caches.shape[1:]
    outputs = taps.shape[0] // 3
    group_of = jnp.arange(channels) // (channels // GROUPS)
    member = (group_of[:, None] == group_of[None, :]).astype(jnp.float32)
    vmem = pl.BlockSpec(memory_space=pltpu.VMEM)
    anywhere = pl.BlockSpec(memory_space=pl.ANY)
    args = [flags, caches, recent[0], recent[1], frames, halves[0], halves[1]]
    args += [taps, bias_vec.reshape(outputs, 1), member]
    args += [v.reshape(-1, 1).astype(jnp.float32) for v in norm]
    specs = [pl.BlockSpec(memory_space=pltpu.SMEM)] + [anywhere] * 7 + [vmem] * 4
    if own is not None:
        args.append(own)
        specs.append(vmem)
    rows_out = span if kind in ("first", "all") else span // 2
    result = jax.ShapeDtypeStruct((rows_out, outputs, columns), jnp.bfloat16)
    padded = jax.ShapeDtypeStruct((span + 2, channels, columns), jnp.bfloat16)
    shapes = result if kind == "tail" else (result, padded)
    body = functools.partial(
        fused_body, kind=kind, tick=tick, frame_at=frame_at, cache_at=tuple(cache_at)
    )
    return pl.pallas_call(
        body,
        out_shape=shapes,
        in_specs=specs,
        out_specs=vmem if kind == "tail" else (vmem, vmem),
        scratch_shapes=[
            pltpu.VMEM((span + 2, channels, columns), jnp.bfloat16),
            pltpu.VMEM((span + 2, channels, columns), jnp.bfloat16),
            pltpu.VMEM((span, channels, columns), jnp.bfloat16),
            pltpu.VMEM(taps.shape, taps.dtype),
            pltpu.SemaphoreType.DMA((5,)),
        ],
    )(*args)


def block_sum(values, span_count):
    peers = lax.axis_size("rows")
    if span_count == peers:
        return values
    lead = (lax.axis_index("rows") % span_count == 0).astype(values.dtype)
    return lax.psum(values * lead, "rows")


def activate(source, gain_vec, shift_vec, cell_count, span_count):
    height, channels, columns = source.shape
    grouped = source.astype(jnp.float32).reshape(height, GROUPS, channels // GROUPS, columns)
    average = block_sum(jnp.sum(grouped, axis=(0, 2, 3)), span_count) / cell_count
    centred = grouped - average[None, :, None, None]
    spread = block_sum(jnp.sum(centred * centred, axis=(0, 2, 3)), span_count) / cell_count
    inverse = lax.rsqrt(spread + EPS)
    normed = (centred * inverse[None, :, None, None]).reshape(height, channels, columns)
    normed = normed * gain_vec[None, :, None] + shift_vec[None, :, None]
    return jax.nn.silu(normed).astype(jnp.bfloat16)


def run_frame(source, first_hist, second_hist, kernels, biases, gains, shifts, cell_count, span_count):
    padded = span_count != lax.axis_size("rows")
    first_in = with_rim(activate(source, gains[0], shifts[0], cell_count, span_count), 0, span_count)
    hidden = causal_conv(first_hist[0], first_hist[1], first_in, kernels[0], biases[0], None, padded)
    second_in = with_rim(activate(hidden, gains[1], shifts[1], cell_count, span_count), 0, span_count)
    result = causal_conv(second_hist[0], second_hist[1], second_in, kernels[1], biases[1], source, padded)
    return (result, (first_hist[1], first_in), (second_hist[1], second_in))


def shards_whole(frames, causal_cache, conv_weight, conv_bias, norm_gain, norm_shift):
    phase_no = lax.axis_index("phase")
    phase_count = lax.axis_size("phase")
    peers = lax.axis_size("rows")
    frame_count, channels, rows_here, columns = frames.shape
    span = rows_here * peers
    half = span // 2
    core = lax.axis_index("rows") % 2
    start = lax.axis_index("rows") * rows_here
    forward = [(s, s + 1) for s in range(phase_count - 1)]
    frames_t = jnp.transpose(frames, (0, 2, 1, 3))
    cache_t = jnp.transpose(causal_cache[0], (0, 1, 3, 2, 4))
    early = lax.all_gather(jnp.stack([frames_t[0], cache_t[0, 0], cache_t[0, 1]]), "rows", axis=1, tiled=True)
    second_cache = lax.all_gather(cache_t[1], "rows", axis=1, tiled=True)
    later = list(frames_t[1:])
    if len(later) == 1:
        later = later * 2
    later = lax.all_gather(jnp.stack(later), "rows", axis=1, tiled=True) if later else early
    frame_of = [(early, 0)] + [(later, f) for f in range(frame_count - 1)]
    cache_of = ((early, (1, 2)), (second_cache, (0, 1)))
    taps = (arrange_taps(conv_weight[0, 0]), arrange_taps(conv_weight[0, 1]))

    def own_rows(x, rim=0):
        return lax.dynamic_slice_in_dim(x, start + rim, rows_here, axis=0)

    got = other = jnp.zeros((half, channels, columns), jnp.bfloat16)
    acts = ([], [])
    blank = jnp.zeros((rows_here, channels, columns), jnp.bfloat16)
    blank_frame = jnp.zeros((span + 2, channels, columns), jnp.bfloat16)
    produced = [blank] * frame_count
    kept = [[blank, blank], [blank, blank]]
    mode = jnp.where(phase_no == 0, 0, 1 + core)
    tick_count = frame_count + phase_count - 1
    frame_nos = jnp.arange(tick_count) - phase_no
    flags = jnp.stack(
        [frame_nos == 0, frame_nos == 1, jnp.full((tick_count,), mode), jnp.full((tick_count,), core)], axis=1
    ).astype(jnp.int32)
    for tick_no in range(tick_count):
        frame_no = tick_no - phase_no
        frame_stack, frame_at = frame_of[min(tick_no, frame_count - 1)]
        recents = []
        for j in range(2):
            a_p = acts[j][-1] if acts[j] else blank_frame
            a_pp = acts[j][-2] if len(acts[j]) > 1 else blank_frame
            recents.append((a_p, a_pp))
        common = (frame_stack, frame_at, (got, other))
        hidden, first_in = fused_conv(
            flags, tick_no, cache_of[0][0], cache_of[0][1], recents[0], *common,
            taps[0], conv_bias[0, 0], (norm_gain[0, 0], norm_shift[0, 0]), "first",
        )
        second = (flags, tick_no, cache_of[1][0], cache_of[1][1], recents[1], *common, taps[1], conv_bias[0, 1])
        if tick_no + 1 == tick_count:
            whole_out, second_in = fused_conv(*second, (norm_gain[0, 1], norm_shift[0, 1]), "all", hidden)
            lead = lax.dynamic_slice_in_dim(whole_out, core * half, half, axis=0)
            tail = lax.dynamic_slice_in_dim(whole_out, (1 - core) * half, half, axis=0)
        else:
            lead, second_in = fused_conv(*second, (norm_gain[0, 1], norm_shift[0, 1]), "lead", hidden)
            tail = fused_conv(*second, (norm_gain[0, 1], norm_shift[0, 1]), "tail", second_in)
        if tick_no + 1 < tick_count:
            got = lax.ppermute(lead, "phase", forward)
            got, tail = lax.optimization_barrier((got, tail))
            other = lax.ppermute(got, "rows", [(i, i ^ 1) for i in range(peers)])
        last = frame_no == frame_count - 1
        for j, a in enumerate((first_in, second_in)):
            stack, (_, k1) = cache_of[j]
            newer = jnp.where(frame_no == 0, own_rows(stack[k1]), own_rows(recents[j][0], 1))
            kept[j] = [jnp.where(last, newer, kept[j][0]), jnp.where(last, own_rows(a, 1), kept[j][1])]
            acts[j].append(a)
        mine = lax.dynamic_slice_in_dim(lead, start - core * half, rows_here, axis=0)
        theirs = lax.dynamic_slice_in_dim(tail, start - (1 - core) * half, rows_here, axis=0)
        result_rows = jnp.where(start // half == core, mine, theirs)
        for f in range(frame_count):
            if 0 <= tick_no - f < phase_count:
                produced[f] = jnp.where(frame_no == f, result_rows, produced[f])
    produced = jnp.transpose(jnp.stack(produced), (0, 2, 1, 3))
    new_cache = jnp.transpose(jnp.stack([jnp.stack(k) for k in kept]), (0, 1, 3, 2, 4))
    return (produced[None], new_cache[None])


def shards(frames, causal_cache, conv_weight, conv_bias, norm_gain, norm_shift):
    peers = lax.axis_size("rows")
    rows_here = frames.shape[2]
    if span_devices(peers, rows_here) == peers and (rows_here * peers) % 2 == 0:
        return shards_whole(frames, causal_cache, conv_weight, conv_bias, norm_gain, norm_shift)
    return shards_split(frames, causal_cache, conv_weight, conv_bias, norm_gain, norm_shift)


def shards_split(frames, causal_cache, conv_weight, conv_bias, norm_gain, norm_shift):
    phase_no = lax.axis_index("phase")
    phase_count = lax.axis_size("phase")
    peers = lax.axis_size("rows")
    frame_count = frames.shape[0]
    channels = frames.shape[1]
    rows_here = frames.shape[2]
    columns = frames.shape[3]
    span_count = span_devices(peers, rows_here)
    span = rows_here * span_count
    cell_count = float(channels // GROUPS * rows_here * peers * columns)
    padded = span_count != peers
    frames_t = jnp.transpose(frames, (0, 2, 1, 3))
    cache_t = jnp.transpose(causal_cache[0], (0, 1, 3, 2, 4))
    early = gather_span(jnp.stack([frames_t[0], cache_t[0, 0], cache_t[0, 1]]), 1, span_count)
    late = gather_span(jnp.stack([cache_t[1, 0], cache_t[1, 1]] + list(frames_t[1:])), 1, span_count)
    frames_span = [early[0]] + [late[2 + f] for f in range(frame_count - 1)]
    first_hist = tuple(with_rim(early[1 + k], 0, span_count) for k in range(2))
    second_hist = tuple(with_rim(late[k], 0, span_count) for k in range(2))
    local_taps = (arrange_taps(conv_weight[0, 0]), arrange_taps(conv_weight[0, 1]))
    incoming = jnp.zeros_like(frames_span[0])
    produced = [jnp.zeros_like(frames_span[0]) for _ in range(frame_count)]
    tick_count = frame_count + phase_count - 1
    for tick_no in range(tick_count):
        frame_no = tick_no - phase_no
        active_now = jnp.logical_and(frame_no >= 0, frame_no < frame_count)
        source = jnp.where(phase_no == 0, frames_span[min(tick_no, frame_count - 1)], incoming)
        result, first_next, second_next = run_frame(
            source, first_hist, second_hist, local_taps, conv_bias[0], norm_gain[0], norm_shift[0],
            cell_count, span_count,
        )
        first_hist = tuple(jnp.where(active_now, a, b) for a, b in zip(first_next, first_hist))
        second_hist = tuple(jnp.where(active_now, a, b) for a, b in zip(second_next, second_hist))
        for f in range(frame_count):
            if 0 <= tick_no - f < phase_count:
                produced[f] = jnp.where(frame_no == f, result, produced[f])
        if tick_no + 1 < tick_count:
            incoming = pass_on(result, span_count)
    start = (lax.axis_index("rows") % span_count) * rows_here
    rim = 1 if padded else 0
    produced = jnp.stack([lax.dynamic_slice_in_dim(p, start, rows_here, axis=0) for p in produced])
    new_cache = jnp.stack(
        [
            jnp.stack([lax.dynamic_slice_in_dim(h, start + rim, rows_here, axis=0) for h in hist])
            for hist in (first_hist, second_hist)
        ]
    )
    produced = jnp.transpose(produced, (0, 2, 1, 3))
    new_cache = jnp.transpose(new_cache, (0, 1, 3, 2, 4))
    return (produced[None], new_cache[None])


def solution(mesh):
    in_specs = (
        P(None, None, "rows", None),
        P("phase", None, None, None, "rows", None),
        P("phase", None, None, None, None, None, None),
        P("phase", None, None),
        P("phase", None, None),
        P("phase", None, None),
    )
    out_specs = (P("phase", None, None, "rows", None), P("phase", None, None, None, "rows", None))
    return jax.shard_map(shards, mesh=mesh, in_specs=in_specs, out_specs=out_specs, check_vma=False)
```

```python
import jax
import jax.numpy as jnp
from jax import lax
from jax.sharding import PartitionSpec as P
from jax.experimental import pallas as pl
from jax.experimental.pallas import tpu as pltpu
import functools

GROUPS = 32
EPS = 1e-06
MAX_SPAN = 16


def span_devices(peers, rows_here):
    count = 1
    while count * 2 <= peers and peers % (count * 2) == 0 and count * 2 * rows_here <= MAX_SPAN:
        count *= 2
    return count


def gather_span(array, dim, span_count):
    if span_count == 1:
        return array
    peers = lax.axis_size("rows")
    if span_count == peers:
        return lax.all_gather(array, "rows", axis=dim, tiled=True)
    place = lax.axis_index("rows") % span_count
    pieces = [array]
    for shift in range(1, span_count):
        pairs = [
            (b * span_count + p, b * span_count + (p + shift) % span_count)
            for b in range(peers // span_count)
            for p in range(span_count)
        ]
        pieces.append(lax.ppermute(array, "rows", pairs))
    stacked = jnp.stack(pieces)
    order = (place - jnp.arange(span_count)) % span_count
    picked = jnp.take(stacked, order, axis=0)
    picked = jnp.moveaxis(picked, 0, dim)
    shape = list(array.shape)
    shape[dim] = shape[dim] * span_count
    return picked.reshape(shape)


def with_rim(array, dim, span_count):
    peers = lax.axis_size("rows")
    length = array.shape[dim]
    if span_count == peers:
        return array
    up = [(i, i + span_count) for i in range(peers - span_count)]
    down = [(j, i) for i, j in up]
    last = lax.slice_in_dim(array, length - 1, length, axis=dim)
    leading = lax.slice_in_dim(array, 0, 1, axis=dim)
    before = lax.ppermute(last, "rows", up)
    after = lax.ppermute(leading, "rows", down)
    return jnp.concatenate([before, array, after], axis=dim)


def pass_on(result, span_count):
    phase_count = lax.axis_size("phase")
    forward = [(s, s + 1) for s in range(phase_count - 1)]
    length = result.shape[0]
    if span_count % 2 or length % 2:
        return lax.ppermute(result, "phase", forward)
    peers = lax.axis_size("rows")
    half = length // 2
    core = lax.axis_index("rows") % 2
    mine = lax.dynamic_slice_in_dim(result, core * half, half, axis=0)
    got = lax.ppermute(mine, "phase", forward)
    other = lax.ppermute(got, "rows", [(i, i ^ 1) for i in range(peers)])
    return jnp.where(core == 0, jnp.concatenate([got, other]), jnp.concatenate([other, got]))


def arrange_taps(weight):
    outputs = weight.shape[3]
    channels = weight.shape[4]
    return jnp.transpose(weight, (2, 3, 0, 1, 4)).reshape(3 * outputs, 9 * channels)


def conv_rows(x0, x1, x2, taps, bias, res, out, rows_out, padded):
    outputs = out.shape[1]
    channels = x0.shape[1]
    columns = x0.shape[2]
    pair = 4 if rows_out % 4 == 0 else (2 if rows_out % 2 == 0 else 1)
    lanes = pair * columns
    lane = lax.broadcasted_iota(jnp.int32, (outputs, lanes), 1) % columns
    frames = (x0, x1, x2)

    def column(r):
        if padded or 0 < r < rows_out - 1:
            base = r if padded else r - 1
            parts = [x[pl.ds(base, 3)] for x in frames]
            return jnp.concatenate(parts, axis=0).reshape(9 * channels, columns)
        zero = jnp.zeros((1, channels, columns), x0.dtype)
        parts = []
        for x in frames:
            for dy in range(3):
                q = r + dy - 1
                parts.append(zero if q < 0 or q >= rows_out else x[pl.ds(q, 1)])
        return jnp.concatenate(parts, axis=0).reshape(9 * channels, columns)

    for r in range(0, rows_out, pair):
        cols = [column(r + k) for k in range(pair)]
        rhs = cols[0] if pair == 1 else jnp.concatenate(cols, axis=1)
        acc = jnp.dot(taps[...], rhs, preferred_element_type=jnp.float32)
        left = pltpu.roll(acc[:outputs], 1, 1)
        right = pltpu.roll(acc[2 * outputs :], lanes - 1, 1)
        total = acc[outputs : 2 * outputs] + jnp.where(lane == 0, 0.0, left)
        total = total + jnp.where(lane == columns - 1, 0.0, right) + bias[...]
        for k in range(pair):
            piece = total[:, k * columns : (k + 1) * columns]
            if res is not None:
                piece = piece + res[r + k].astype(jnp.float32)
            out[r + k] = piece.astype(out.dtype)


def conv_body(x0, x1, x2, taps, bias, *rest, rows_out, with_res, padded):
    res = rest[0] if with_res else None
    conv_rows(x0, x1, x2, taps, bias, res, rest[-1], rows_out, padded)


def causal_conv(x0, x1, x2, taps, bias_vec, res, padded):
    rows_out = x0.shape[0] - 2 if padded else x0.shape[0]
    outputs = taps.shape[0] // 3
    args = [x0, x1, x2, taps, bias_vec.reshape(outputs, 1)]
    if res is not None:
        args.append(res)
    body = functools.partial(conv_body, rows_out=rows_out, with_res=res is not None, padded=padded)
    shape = jax.ShapeDtypeStruct((rows_out, outputs, x0.shape[2]), jnp.bfloat16)
    return pl.pallas_call(body, out_shape=shape)(*args)


def conv_span(x0, x1, x2, taps, bias, res, out, base, count):
    outputs = out.shape[1]
    channels = x0.shape[1]
    columns = x0.shape[2]
    pair = next(p for p in (16, 8, 4, 2, 1) if count % p == 0)
    lanes = pair * columns
    lane = lax.broadcasted_iota(jnp.int32, (outputs, lanes), 1) % columns

    def step(i, carry):
        r = base + i * pair
        cols = []
        for k in range(pair):
            parts = [x[pl.ds(r + k, 3)] for x in (x0, x1, x2)]
            cols.append(jnp.concatenate(parts, axis=0).reshape(9 * channels, columns))
        rhs = cols[0] if pair == 1 else jnp.concatenate(cols, axis=1)
        acc = jnp.dot(taps[...], rhs, preferred_element_type=jnp.float32)
        left = pltpu.roll(acc[:outputs], 1, 1)
        right = pltpu.roll(acc[2 * outputs :], lanes - 1, 1)
        total = acc[outputs : 2 * outputs] + jnp.where(lane == 0, 0.0, left)
        total = total + jnp.where(lane == columns - 1, 0.0, right) + bias[...]
        for k in range(pair):
            piece = total[:, k * columns : (k + 1) * columns]
            if res is not None:
                piece = piece + res[r + k].astype(jnp.float32)
            out[i * pair + k] = piece.astype(out.dtype)
        return carry

    lax.fori_loop(0, count // pair, step, 0)


def fused_body(flags, caches, a_p, a_pp, frames, src_b, src_c, taps, bias, member, gain, shift, *rest,
               kind, tick, frame_at, cache_at):
    rest = list(rest)
    own = rest.pop(0) if kind != "first" else None
    if kind == "tail":
        out, x0, x1, rawbuf, tapbuf, sems = rest
        act = own
    else:
        out, act, x0, x1, rawbuf, tapbuf, sems = rest
    span, channels, columns = rawbuf.shape
    half = span // 2
    first, second, mode, core = flags[tick, 0], flags[tick, 1], flags[tick, 2], flags[tick, 3]
    c0, c1 = caches.at[cache_at[0]], caches.at[cache_at[1]]
    whole = frames.at[frame_at]
    top, bottom = rawbuf.at[pl.ds(0, half)], rawbuf.at[pl.ds(half, half)]
    inner0, inner1 = x0.at[pl.ds(1, span)], x1.at[pl.ds(1, span)]

    def inner(x):
        return x.at[pl.ds(1, span)]

    def begin(pairs, base):
        for i, (a, b) in enumerate(pairs):
            pltpu.make_async_copy(a, b, sems.at[base + i]).start()

    def finish(pairs, base):
        for i, (a, b) in enumerate(pairs):
            pltpu.make_async_copy(a, b, sems.at[base + i]).wait()

    @pl.when(mode == 0)
    def _():
        begin([(whole.at[pl.ds(0, half)], top), (whole.at[pl.ds(half, half)], bottom)], 0)

    @pl.when(mode == 1)
    def _():
        begin([(src_b, top), (src_c, bottom)], 0)

    @pl.when(mode == 2)
    def _():
        begin([(src_c, top), (src_b, bottom)], 0)

    pltpu.make_async_copy(taps, tapbuf, sems.at[4]).start()

    @pl.when(first == 1)
    def _():
        begin([(c0, inner0), (c1, inner1)], 2)

    @pl.when(jnp.logical_and(first == 0, second == 1))
    def _():
        begin([(c1, inner0), (inner(a_p), inner1)], 2)

    @pl.when(jnp.logical_and(first == 0, second == 0))
    def _():
        begin([(inner(a_pp), inner0), (inner(a_p), inner1)], 2)

    zero = jnp.zeros((channels, columns), x0.dtype)
    for x in (x0, x1):
        x[0] = zero
        x[span + 1] = zero
    source_copies = [(src_b, top), (src_c, bottom)]
    history_copies = [(inner(a_pp), inner0), (inner(a_p), inner1)]

    if kind != "tail":
        if kind == "first":
            finish(source_copies, 0)
            raw = rawbuf
        else:
            raw = own
        count = float(span * columns * (channels // GROUPS))

        def group_total(acc):
            spread = jnp.dot(member[...], acc, precision=lax.Precision.HIGHEST, preferred_element_type=jnp.float32)
            return jnp.sum(spread, axis=1, keepdims=True)

        acc = raw[0].astype(jnp.float32)
        for r in range(1, span):
            acc = acc + raw[r].astype(jnp.float32)
        average = group_total(acc) / count
        acc = jnp.square(raw[0].astype(jnp.float32) - average)
        for r in range(1, span):
            acc = acc + jnp.square(raw[r].astype(jnp.float32) - average)
        inverse = lax.rsqrt(group_total(acc) / count + EPS)
        act[0] = zero
        act[span + 1] = zero
        for r in range(span):
            value = (raw[r].astype(jnp.float32) - average) * inverse
            value = value * gain[...] + shift[...]
            act[r + 1] = (value / (1.0 + jnp.exp(-value))).astype(act.dtype)

    finish(history_copies, 2)
    pltpu.make_async_copy(taps, tapbuf, sems.at[4]).wait()
    taps = tapbuf
    if kind == "first":
        conv_span(x0, x1, act, taps, bias, None, out, 0, span)
    elif kind == "all":
        finish(source_copies, 0)
        conv_span(x0, x1, act, taps, bias, rawbuf, out, 0, span)
    else:
        finish(source_copies, 0)
        base = core * half if kind == "lead" else (1 - core) * half
        conv_span(x0, x1, act, taps, bias, rawbuf, out, base, half)


def fused_conv(flags, tick, caches, cache_at, recent, frames, frame_at, halves, taps, bias_vec, norm, kind, own=None):
    span, channels, columns = caches.shape[1:]
    outputs = taps.shape[0] // 3
    group_of = jnp.arange(channels) // (channels // GROUPS)
    member = (group_of[:, None] == group_of[None, :]).astype(jnp.float32)
    vmem = pl.BlockSpec(memory_space=pltpu.VMEM)
    anywhere = pl.BlockSpec(memory_space=pl.ANY)
    args = [flags, caches, recent[0], recent[1], frames, halves[0], halves[1]]
    args += [taps, bias_vec.reshape(outputs, 1), member]
    args += [v.reshape(-1, 1).astype(jnp.float32) for v in norm]
    specs = [pl.BlockSpec(memory_space=pltpu.SMEM)] + [anywhere] * 7 + [vmem] * 4
    if own is not None:
        args.append(own)
        specs.append(vmem)
    rows_out = span if kind in ("first", "all") else span // 2
    result = jax.ShapeDtypeStruct((rows_out, outputs, columns), jnp.bfloat16)
    padded = jax.ShapeDtypeStruct((span + 2, channels, columns), jnp.bfloat16)
    shapes = result if kind == "tail" else (result, padded)
    body = functools.partial(
        fused_body, kind=kind, tick=tick, frame_at=frame_at, cache_at=tuple(cache_at)
    )
    return pl.pallas_call(
        body,
        out_shape=shapes,
        in_specs=specs,
        out_specs=vmem if kind == "tail" else (vmem, vmem),
        scratch_shapes=[
            pltpu.VMEM((span + 2, channels, columns), jnp.bfloat16),
            pltpu.VMEM((span + 2, channels, columns), jnp.bfloat16),
            pltpu.VMEM((span, channels, columns), jnp.bfloat16),
            pltpu.VMEM(taps.shape, taps.dtype),
            pltpu.SemaphoreType.DMA((5,)),
        ],
    )(*args)


def block_sum(values, span_count):
    peers = lax.axis_size("rows")
    if span_count == peers:
        return values
    lead = (lax.axis_index("rows") % span_count == 0).astype(values.dtype)
    return lax.psum(values * lead, "rows")


def activate(source, gain_vec, shift_vec, cell_count, span_count):
    height, channels, columns = source.shape
    grouped = source.astype(jnp.float32).reshape(height, GROUPS, channels // GROUPS, columns)
    average = block_sum(jnp.sum(grouped, axis=(0, 2, 3)), span_count) / cell_count
    centred = grouped - average[None, :, None, None]
    spread = block_sum(jnp.sum(centred * centred, axis=(0, 2, 3)), span_count) / cell_count
    inverse = lax.rsqrt(spread + EPS)
    normed = (centred * inverse[None, :, None, None]).reshape(height, channels, columns)
    normed = normed * gain_vec[None, :, None] + shift_vec[None, :, None]
    return jax.nn.silu(normed).astype(jnp.bfloat16)


def run_frame(source, first_hist, second_hist, kernels, biases, gains, shifts, cell_count, span_count):
    padded = span_count != lax.axis_size("rows")
    first_in = with_rim(activate(source, gains[0], shifts[0], cell_count, span_count), 0, span_count)
    hidden = causal_conv(first_hist[0], first_hist[1], first_in, kernels[0], biases[0], None, padded)
    second_in = with_rim(activate(hidden, gains[1], shifts[1], cell_count, span_count), 0, span_count)
    result = causal_conv(second_hist[0], second_hist[1], second_in, kernels[1], biases[1], source, padded)
    return (result, (first_hist[1], first_in), (second_hist[1], second_in))


def shards_whole(frames, causal_cache, conv_weight, conv_bias, norm_gain, norm_shift):
    phase_no = lax.axis_index("phase")
    phase_count = lax.axis_size("phase")
    peers = lax.axis_size("rows")
    frame_count, channels, rows_here, columns = frames.shape
    span = rows_here * peers
    half = span // 2
    core = lax.axis_index("rows") % 2
    start = lax.axis_index("rows") * rows_here
    forward = [(s, s + 1) for s in range(phase_count - 1)]
    frames_t = jnp.transpose(frames, (0, 2, 1, 3))
    cache_t = jnp.transpose(causal_cache[0], (0, 1, 3, 2, 4))
    early = lax.all_gather(jnp.stack([frames_t[0], cache_t[0, 0], cache_t[0, 1]]), "rows", axis=1, tiled=True)
    second_cache = lax.all_gather(cache_t[1], "rows", axis=1, tiled=True)
    later = list(frames_t[1:])
    if len(later) == 1:
        later = later * 2
    later = lax.all_gather(jnp.stack(later), "rows", axis=1, tiled=True) if later else early
    frame_of = [(early, 0)] + [(later, f) for f in range(frame_count - 1)]
    cache_of = ((early, (1, 2)), (second_cache, (0, 1)))
    taps = (arrange_taps(conv_weight[0, 0]), arrange_taps(conv_weight[0, 1]))

    def own_rows(x, rim=0):
        return lax.dynamic_slice_in_dim(x, start + rim, rows_here, axis=0)

    got = other = jnp.zeros((half, channels, columns), jnp.bfloat16)
    acts = ([], [])
    blank = jnp.zeros((rows_here, channels, columns), jnp.bfloat16)
    blank_frame = jnp.zeros((span + 2, channels, columns), jnp.bfloat16)
    produced = [blank] * frame_count
    kept = [[blank, blank], [blank, blank]]
    mode = jnp.where(phase_no == 0, 0, 1 + core)
    tick_count = frame_count + phase_count - 1
    frame_nos = jnp.arange(tick_count) - phase_no
    flags = jnp.stack(
        [frame_nos == 0, frame_nos == 1, jnp.full((tick_count,), mode), jnp.full((tick_count,), core)], axis=1
    ).astype(jnp.int32)
    for tick_no in range(tick_count):
        frame_no = tick_no - phase_no
        frame_stack, frame_at = frame_of[min(tick_no, frame_count - 1)]
        recents = []
        for j in range(2):
            a_p = acts[j][-1] if acts[j] else blank_frame
            a_pp = acts[j][-2] if len(acts[j]) > 1 else blank_frame
            recents.append((a_p, a_pp))
        common = (frame_stack, frame_at, (got, other))
        hidden, first_in = fused_conv(
            flags, tick_no, cache_of[0][0], cache_of[0][1], recents[0], *common,
            taps[0], conv_bias[0, 0], (norm_gain[0, 0], norm_shift[0, 0]), "first",
        )
        second = (flags, tick_no, cache_of[1][0], cache_of[1][1], recents[1], *common, taps[1], conv_bias[0, 1])
        if tick_no + 1 == tick_count:
            whole_out, second_in = fused_conv(*second, (norm_gain[0, 1], norm_shift[0, 1]), "all", hidden)
            lead = lax.dynamic_slice_in_dim(whole_out, core * half, half, axis=0)
            tail = lax.dynamic_slice_in_dim(whole_out, (1 - core) * half, half, axis=0)
        else:
            lead, second_in = fused_conv(*second, (norm_gain[0, 1], norm_shift[0, 1]), "lead", hidden)
            tail = fused_conv(*second, (norm_gain[0, 1], norm_shift[0, 1]), "tail", second_in)
        if tick_no + 1 < tick_count:
            got = lax.ppermute(lead, "phase", forward)
            got, tail = lax.optimization_barrier((got, tail))
            other = lax.ppermute(got, "rows", [(i, i ^ 1) for i in range(peers)])
        last = frame_no == frame_count - 1
        for j, a in enumerate((first_in, second_in)):
            stack, (_, k1) = cache_of[j]
            newer = jnp.where(frame_no == 0, own_rows(stack[k1]), own_rows(recents[j][0], 1))
            kept[j] = [jnp.where(last, newer, kept[j][0]), jnp.where(last, own_rows(a, 1), kept[j][1])]
            acts[j].append(a)
        mine = lax.dynamic_slice_in_dim(lead, start - core * half, rows_here, axis=0)
        theirs = lax.dynamic_slice_in_dim(tail, start - (1 - core) * half, rows_here, axis=0)
        result_rows = jnp.where(start // half == core, mine, theirs)
        for f in range(frame_count):
            if 0 <= tick_no - f < phase_count:
                produced[f] = jnp.where(frame_no == f, result_rows, produced[f])
    produced = jnp.transpose(jnp.stack(produced), (0, 2, 1, 3))
    new_cache = jnp.transpose(jnp.stack([jnp.stack(k) for k in kept]), (0, 1, 3, 2, 4))
    return (produced[None], new_cache[None])


def shards(frames, causal_cache, conv_weight, conv_bias, norm_gain, norm_shift):
    peers = lax.axis_size("rows")
    rows_here = frames.shape[2]
    if span_devices(peers, rows_here) == peers and (rows_here * peers) % 2 == 0:
        return shards_whole(frames, causal_cache, conv_weight, conv_bias, norm_gain, norm_shift)
    return shards_split(frames, causal_cache, conv_weight, conv_bias, norm_gain, norm_shift)


def shards_split(frames, causal_cache, conv_weight, conv_bias, norm_gain, norm_shift):
    phase_no = lax.axis_index("phase")
    phase_count = lax.axis_size("phase")
    peers = lax.axis_size("rows")
    frame_count = frames.shape[0]
    channels = frames.shape[1]
    rows_here = frames.shape[2]
    columns = frames.shape[3]
    span_count = span_devices(peers, rows_here)
    span = rows_here * span_count
    cell_count = float(channels // GROUPS * rows_here * peers * columns)
    padded = span_count != peers
    frames_t = jnp.transpose(frames, (0, 2, 1, 3))
    cache_t = jnp.transpose(causal_cache[0], (0, 1, 3, 2, 4))
    early = gather_span(jnp.stack([frames_t[0], cache_t[0, 0], cache_t[0, 1]]), 1, span_count)
    late = gather_span(jnp.stack([cache_t[1, 0], cache_t[1, 1]] + list(frames_t[1:])), 1, span_count)
    frames_span = [early[0]] + [late[2 + f] for f in range(frame_count - 1)]
    first_hist = tuple(with_rim(early[1 + k], 0, span_count) for k in range(2))
    second_hist = tuple(with_rim(late[k], 0, span_count) for k in range(2))
    local_taps = (arrange_taps(conv_weight[0, 0]), arrange_taps(conv_weight[0, 1]))
    incoming = jnp.zeros_like(frames_span[0])
    produced = [jnp.zeros_like(frames_span[0]) for _ in range(frame_count)]
    tick_count = frame_count + phase_count - 1
    for tick_no in range(tick_count):
        frame_no = tick_no - phase_no
        active_now = jnp.logical_and(frame_no >= 0, frame_no < frame_count)
        source = jnp.where(phase_no == 0, frames_span[min(tick_no, frame_count - 1)], incoming)
        result, first_next, second_next = run_frame(
            source, first_hist, second_hist, local_taps, conv_bias[0], norm_gain[0], norm_shift[0],
            cell_count, span_count,
        )
        first_hist = tuple(jnp.where(active_now, a, b) for a, b in zip(first_next, first_hist))
        second_hist = tuple(jnp.where(active_now, a, b) for a, b in zip(second_next, second_hist))
        for f in range(frame_count):
            if 0 <= tick_no - f < phase_count:
                produced[f] = jnp.where(frame_no == f, result, produced[f])
        if tick_no + 1 < tick_count:
            incoming = pass_on(result, span_count)
    start = (lax.axis_index("rows") % span_count) * rows_here
    rim = 1 if padded else 0
    produced = jnp.stack([lax.dynamic_slice_in_dim(p, start, rows_here, axis=0) for p in produced])
    new_cache = jnp.stack(
        [
            jnp.stack([lax.dynamic_slice_in_dim(h, start + rim, rows_here, axis=0) for h in hist])
            for hist in (first_hist, second_hist)
        ]
    )
    produced = jnp.transpose(produced, (0, 2, 1, 3))
    new_cache = jnp.transpose(new_cache, (0, 1, 3, 2, 4))
    return (produced[None], new_cache[None])


def solution(mesh):
    in_specs = (
        P(None, None, "rows", None),
        P("phase", None, None, None, "rows", None),
        P("phase", None, None, None, None, None, None),
        P("phase", None, None),
        P("phase", None, None),
        P("phase", None, None),
    )
    out_specs = (P("phase", None, None, "rows", None), P("phase", None, None, None, "rows", None))
    return jax.shard_map(shards, mesh=mesh, in_specs=in_specs, out_specs=out_specs, check_vma=False)
```
